256 devices in a mesh: tm: 32 (over z, x), sensor: 8 (over y, core).
Axes of the slice: x: 4, y: 4, z: 8, core: 2. Of those that a mesh axis runs over, the one named last changes fastest.
Arguments:
- observations: bfloat16 [8192, 32768], P('tm', 'sensor'), may hold values from -6 to 6
- obs_list: int32 [8192, 128], P('tm', 'sensor'), may hold values from -1 to 255, as said below
- gain_rows: bfloat16 [32768, 1024], P('sensor'), may hold values from -0.0048828125 to 0.0048828125
- decay: float32 [8192, 1024], P('tm'), may hold values from 0 to 1
- smooth_gain: float32 [8192, 1024], P('tm'), may hold values from 0 to 1
- model_rate: float32 [1024], replicated, may hold values from 0.5 to 1
- first_state: float32 [1024], replicated, may hold values from -6 to 6
Outputs:
- filtered: float32 [8192, 1024], P('tm', 'sensor')
- smoothed: float32 [8192, 1024], P('tm', 'sensor')
The draws below stay inside these ranges and needn't reach their ends.
Inputs may be any that keep to these rules, and one draw needn't show every extreme that they name: `obs_list`: in row t the 16 slots of sensor index j name distinct blocks from j * 32 to (j + 1) * 32 - 1; -1 marks an empty slot; slots of lower sensor indices are emptier.
All inputs are finite; a program needn't handle non-finite values.
Results may differ from the reference program's by a relative error of at most 0.0003.
Values sent between devices are 32-bit elements; how exact they have to be, the bound alone decides.
No kernel may reach another device: no remote copies, remote signals or barrier semaphores. Data moves between devices by JAX's collectives and lax.ppermute only.
A program may use at most 64 MiB of HBM per device.

```python
import math
import jax
import jax.numpy as jnp
from jax import lax

MODE_COUNT = 1024
NB_DEV = 32
SLOT_DEV = 16
HOUR_STEPS = 8192
NBLK = 256
N_SENSOR = 8


def factor_law(key, salt, fast_share):
    key = jax.random.fold_in(key, salt)
    random_keys = jax.random.split(key, 6)
    picked = jax.random.uniform(random_keys[0], (MODE_COUNT,)) < fast_share
    slow_rate = jax.random.uniform(random_keys[1], (MODE_COUNT,), minval=0.05, maxval=0.5) * math.log(10.0) / HOUR_STEPS
    fast_rate = jax.random.uniform(random_keys[2], (MODE_COUNT,), minval=1.0 / 50.0, maxval=1.0 / 30.0)
    decay_rate = jnp.where(picked, fast_rate, slow_rate)
    coarse_noise = jax.random.uniform(random_keys[3], (HOUR_STEPS, MODE_COUNT), minval=0.5, maxval=1.6)
    surge_events = jax.random.randint(random_keys[4], (HOUR_STEPS, MODE_COUNT), 0, HOUR_STEPS) < 2
    surge_multiplier = jax.random.uniform(random_keys[5], (HOUR_STEPS, MODE_COUNT), minval=0.5, maxval=0.8)
    entry_value = jnp.exp(-decay_rate[None, :] * coarse_noise) * jnp.where(surge_events, surge_multiplier, 1.0)
    return entry_value.astype(jnp.float32)


def draw_decay(key, part):
    return factor_law(key, 11, 0.35)


def draw_smooth_gain(key, part):
    return factor_law(key, 23, 0.35)


def draw_obs_list(key, part):
    random_keys = jax.random.split(jax.random.fold_in(key, 37), 2)
    sensor_ids = jnp.arange(N_SENSOR, dtype=jnp.int32)
    highest = jnp.minimum(SLOT_DEV, 1 + SLOT_DEV * (sensor_ids + 1) // N_SENSOR)
    counts = jax.random.randint(random_keys[0], (HOUR_STEPS, N_SENSOR), 0, SLOT_DEV + 1)
    counts = jnp.minimum(counts, highest[None, :])
    counts = counts.at[0, N_SENSOR - 1].set(SLOT_DEV)
    scores = jax.random.randint(random_keys[1], (HOUR_STEPS, N_SENSOR, NB_DEV), 0, 2 ** 20) * NB_DEV + jnp.arange(NB_DEV, dtype=jnp.int32)[None, None, :]
    order = jnp.argsort(scores, axis=2, stable=True).astype(jnp.int32)[:, :, :SLOT_DEV]
    global_ids = order + sensor_ids[None, :, None] * NB_DEV
    slot_index = jnp.arange(SLOT_DEV, dtype=jnp.int32)
    global_ids = jnp.where(slot_index[None, None, :] < counts[:, :, None], global_ids, -1)
    return global_ids.reshape(HOUR_STEPS, N_SENSOR * SLOT_DEV).astype(jnp.int32)


def block_levels(rng, extent, shards, smallest, largest):
    factor_of, own = 1.0, jax.random.fold_in(rng, 6)
    for position, shards_of in shards:
        steps = jnp.exp(jax.random.uniform(jax.random.fold_in(own, position), (shards_of,), jnp.float32, smallest / len(shards), largest / len(shards)))
        factor_of = factor_of * jnp.repeat(steps, extent[position] // shards_of).reshape([-1 if axis == position else 1 for axis in range(len(extent))])
    return factor_of


def scatter_about(own_key, extent, scale, reach, cuts=(), kind=jnp.bfloat16):
    array = scale * jax.random.normal(own_key, extent, jnp.float32)
    if cuts:
        array = array * block_levels(own_key, extent, cuts, -0.22, 0.18)
    return jnp.clip(array, -reach, reach).astype(kind)


def setup_inputs(seed: int = 0) -> dict:
    seeds = jax.random.split(jax.random.key(seed), 8)
    observations = scatter_about(seeds[0], (HOUR_STEPS, NBLK * 128), 1.0, 6.0, ((0, 32), (1, 8)))
    obs_list = draw_obs_list(jax.random.fold_in(seeds[7], 71), 0)
    gain_rows = scatter_about(seeds[2], (NBLK * 128, MODE_COUNT), (100 * SLOT_DEV * N_SENSOR * 128) ** -0.5, 0.0048828125, ((0, 8),))
    decay = draw_decay(jax.random.fold_in(seeds[7], 71), 0)
    smooth_gain = draw_smooth_gain(jax.random.fold_in(seeds[7], 71), 0)
    model_rate = jnp.clip(jax.random.uniform(seeds[5], (MODE_COUNT,), jnp.float32, 0.5, 1.0), 0.5, 1.0)
    first_state = scatter_about(seeds[6], (MODE_COUNT,), 1.0, 6.0, (), jnp.float32)
    return {"observations": observations, "obs_list": obs_list, "gain_rows": gain_rows, "decay": decay, "smooth_gain": smooth_gain, "model_rate": model_rate, "first_state": first_state}


def link(earlier, later):
    return (later[0] * earlier[0], later[0] * earlier[1] + later[1])


def reference(observations, obs_list, gain_rows, decay, smooth_gain, model_rate, first_state):
    blocks = jnp.arange(NBLK, dtype=jnp.int32)

    def add_slot(listed, slot_ids):
        return listed + (slot_ids[:, None] == blocks[None, :]).astype(jnp.float32), None

    listed, _ = lax.scan(add_slot, jnp.zeros((HOUR_STEPS, NBLK), jnp.float32), obs_list.T)
    weighted = (observations.reshape(HOUR_STEPS, NBLK, 128) * listed[:, :, None]).reshape(HOUR_STEPS, NBLK * 128).astype(jnp.bfloat16)
    inflow = jnp.dot(weighted, gain_rows, preferred_element_type=jnp.float32)

    def forward(state, pair):
        state = pair[0] * state + pair[1]
        return state, state

    _, filtered = lax.scan(forward, first_state.astype(jnp.float32), (decay, inflow))
    hours = jnp.arange(HOUR_STEPS, dtype=jnp.int32)
    step_gain = jnp.where((hours == HOUR_STEPS - 1)[:, None], jnp.float32(0.0), smooth_gain)
    offset = filtered - (step_gain * model_rate[None, :]) * filtered

    def backward(state, pair):
        state = pair[0] * state + pair[1]
        return state, state

    _, smoothed = lax.scan(backward, jnp.zeros((MODE_COUNT,), jnp.float32), (step_gain, offset), reverse=True)
    return filtered, smoothed
```

```python
import jax
import jax.numpy as jnp
from jax import lax
from jax.sharding import PartitionSpec as P


def link(earlier, later):
    return (later[0] * earlier[0], later[0] * earlier[1] + later[1])


def sensor_reduce_scatter(partial, width):
    count = lax.axis_size("sensor")
    chips = count // 2
    j = lax.axis_index("sensor")
    chip = j // 2
    core = j % 2
    rows = partial.shape[0]
    split = partial.reshape(rows, chips, 2, width)
    send = lax.dynamic_index_in_dim(split, 1 - core, 2, False)
    keep = lax.dynamic_index_in_dim(split, core, 2, False)
    chip_sum = keep + lax.ppermute(send, "sensor", [(i, i ^ 1) for i in range(count)])
    total = lax.dynamic_index_in_dim(chip_sum, chip, 1, False)
    for shift in range(1, chips):
        piece = lax.dynamic_index_in_dim(chip_sum, (chip + shift) % chips, 1, False)
        perm = [(i, (((i // 2) + shift) % chips) * 2 + i % 2) for i in range(count)]
        total = total + lax.ppermute(piece, "sensor", perm)
    return total


def gather_tm(x):
    count = lax.axis_size("tm")
    place = lax.axis_index("tm")
    held = x[None]
    step = 1
    while step < count:
        other = lax.ppermute(held, "tm", [(i, i ^ step) for i in range(count)])
        low = (place & step) == 0
        held = jnp.where(
            low, jnp.concatenate([held, other], 0), jnp.concatenate([other, held], 0)
        )
        step *= 2
    return held


def per_device(observations, obs_list, gain_rows, decay, smooth_gain, model_rate, first_state):
    sensor_count = lax.axis_size("sensor")
    sensor_index = lax.axis_index("sensor")
    time_index = lax.axis_index("tm")
    time_count = lax.axis_size("tm")
    rows_here = observations.shape[0]
    block_count = observations.shape[1] // 128
    own_blocks = sensor_index * block_count + jnp.arange(block_count, dtype=jnp.int32)
    listed = jnp.any(obs_list[:, :, None] == own_blocks[None, None, :], axis=1).astype(jnp.float32)
    weighted = (
        (observations.reshape(rows_here, block_count, 128) * listed[:, :, None])
        .reshape(rows_here, block_count * 128)
        .astype(jnp.bfloat16)
    )
    partial_sum = jnp.dot(weighted, gain_rows, preferred_element_type=jnp.float32)
    width = gain_rows.shape[1] // sensor_count
    inflow = sensor_reduce_scatter(partial_sum, width)
    start_col = sensor_index * width
    factors = lax.dynamic_slice_in_dim(decay, start_col, width, 1)
    gains = lax.dynamic_slice_in_dim(smooth_gain, start_col, width, 1)
    rates = lax.dynamic_slice_in_dim(model_rate, start_col, width, 0)
    initial = lax.dynamic_slice_in_dim(first_state, start_col, width, 0)
    hour_ids = time_index * rows_here + jnp.arange(rows_here, dtype=jnp.int32)
    total_hours = rows_here * time_count
    step_gain = jnp.where((hour_ids == total_hours - 1)[:, None], jnp.float32(0.0), gains)
    scale = step_gain * rates[None, :]

    prod_fwd, local_fwd = lax.associative_scan(link, (factors, inflow), axis=0)
    off_local = local_fwd - scale * local_fwd
    off_prod = prod_fwd - scale * prod_fwd
    prod_back, back = lax.associative_scan(
        link,
        (jnp.concatenate([step_gain, step_gain], 1), jnp.concatenate([off_local, off_prod], 1)),
        axis=0,
        reverse=True,
    )
    prod_back = prod_back[:, :width]
    back_local = back[:, :width]
    back_prod = back[:, width:]

    summary = jnp.stack(
        [prod_fwd[-1], local_fwd[-1], prod_back[0], back_local[0], back_prod[0]], 0
    )
    every = gather_tm(summary)
    entering = [initial]
    for k in range(time_count - 1):
        entering.append(every[k, 0] * entering[-1] + every[k, 1])
    after = [jnp.zeros_like(initial)]
    for k in range(time_count - 1, 0, -1):
        after.append(every[k, 3] + every[k, 4] * entering[k] + every[k, 2] * after[-1])
    after = after[::-1]
    entering_here = lax.dynamic_index_in_dim(jnp.stack(entering, 0), time_index, 0, False)
    after_here = lax.dynamic_index_in_dim(jnp.stack(after, 0), time_index, 0, False)

    filtered = local_fwd + prod_fwd * entering_here[None, :]
    smoothed = back_local + back_prod * entering_here[None, :] + prod_back * after_here[None, :]
    return (filtered, smoothed)


def solution(mesh):
    in_specs = (
        P("tm", "sensor"),
        P("tm", "sensor"),
        P("sensor", None),
        P("tm", None),
        P("tm", None),
        P(),
        P(),
    )
    out_specs = (P("tm", "sensor"), P("tm", "sensor"))
    return jax.shard_map(
        per_device, mesh=mesh, in_specs=in_specs, out_specs=out_specs, check_vma=False
    )
```

```python
import jax
import jax.numpy as jnp
from jax import lax
from jax.sharding import PartitionSpec as P


def link(earlier, later):
    return (later[0] * earlier[0], later[0] * earlier[1] + later[1])


def sensor_reduce_scatter(partial, width):
    count = lax.axis_size("sensor")
    chips = count // 2
    j = lax.axis_index("sensor")
    chip = j // 2
    core = j % 2

    def piece(index):
        return lax.dynamic_slice_in_dim(partial, index * width, width, 1)

    send = jnp.stack([piece(2 * c + 1 - core) for c in range(chips)], 0)
    keep = jnp.stack([piece(2 * c + core) for c in range(chips)], 0)
    chip_sum = keep + lax.ppermute(send, "sensor", [(i, i ^ 1) for i in range(count)])
    total = lax.dynamic_index_in_dim(chip_sum, chip, 0, False)
    for shift in range(1, chips):
        part = lax.dynamic_index_in_dim(chip_sum, (chip + shift) % chips, 0, False)
        perm = [(i, (((i // 2) + shift) % chips) * 2 + i % 2) for i in range(count)]
        total = total + lax.ppermute(part, "sensor", perm)
    return total


def gather_tm(x):
    count = lax.axis_size("tm")
    place = lax.axis_index("tm")
    held = x[None]
    step = 1
    while step < count:
        other = lax.ppermute(held, "tm", [(i, i ^ step) for i in range(count)])
        low = (place & step) == 0
        held = jnp.where(
            low, jnp.concatenate([held, other], 0), jnp.concatenate([other, held], 0)
        )
        step *= 2
    return held


def per_device(observations, obs_list, gain_rows, decay, smooth_gain, model_rate, first_state):
    sensor_count = lax.axis_size("sensor")
    sensor_index = lax.axis_index("sensor")
    time_index = lax.axis_index("tm")
    time_count = lax.axis_size("tm")
    rows_here = observations.shape[0]
    block_count = observations.shape[1] // 128
    own_blocks = sensor_index * block_count + jnp.arange(block_count, dtype=jnp.int32)
    listed = jnp.any(obs_list[:, :, None] == own_blocks[None, None, :], axis=1).astype(jnp.float32)
    weighted = (
        (observations.reshape(rows_here, block_count, 128) * listed[:, :, None])
        .reshape(rows_here, block_count * 128)
        .astype(jnp.bfloat16)
    )
    partial_sum = jnp.dot(weighted, gain_rows, preferred_element_type=jnp.float32)
    width = gain_rows.shape[1] // sensor_count
    inflow = sensor_reduce_scatter(partial_sum, width)
    start_col = sensor_index * width
    factors = lax.dynamic_slice_in_dim(decay, start_col, width, 1)
    gains = lax.dynamic_slice_in_dim(smooth_gain, start_col, width, 1)
    rates = lax.dynamic_slice_in_dim(model_rate, start_col, width, 0)
    initial = lax.dynamic_slice_in_dim(first_state, start_col, width, 0)
    hour_ids = time_index * rows_here + jnp.arange(rows_here, dtype=jnp.int32)
    total_hours = rows_here * time_count
    step_gain = jnp.where((hour_ids == total_hours - 1)[:, None], jnp.float32(0.0), gains)
    scale = step_gain * rates[None, :]

    prod_fwd, local_fwd = lax.associative_scan(link, (factors, inflow), axis=0)
    off_local = local_fwd - scale * local_fwd
    off_prod = prod_fwd - scale * prod_fwd
    prod_back, back = lax.associative_scan(
        link,
        (jnp.concatenate([step_gain, step_gain], 1), jnp.concatenate([off_local, off_prod], 1)),
        axis=0,
        reverse=True,
    )
    prod_back = prod_back[:, :width]
    back_local = back[:, :width]
    back_prod = back[:, width:]

    summary = jnp.stack(
        [prod_fwd[-1], local_fwd[-1], prod_back[0], back_local[0], back_prod[0]], 0
    )
    every = gather_tm(summary)
    entering = [initial]
    for k in range(time_count - 1):
        entering.append(every[k, 0] * entering[-1] + every[k, 1])
    after = [jnp.zeros_like(initial)]
    for k in range(time_count - 1, 0, -1):
        after.append(every[k, 3] + every[k, 4] * entering[k] + every[k, 2] * after[-1])
    after = after[::-1]
    entering_here = lax.dynamic_index_in_dim(jnp.stack(entering, 0), time_index, 0, False)
    after_here = lax.dynamic_index_in_dim(jnp.stack(after, 0), time_index, 0, False)

    filtered = local_fwd + prod_fwd * entering_here[None, :]
    smoothed = back_local + back_prod * entering_here[None, :] + prod_back * after_here[None, :]
    return (filtered, smoothed)


def solution(mesh):
    in_specs = (
        P("tm", "sensor"),
        P("tm", "sensor"),
        P("sensor", None),
        P("tm", None),
        P("tm", None),
        P(),
        P(),
    )
    out_specs = (P("tm", "sensor"), P("tm", "sensor"))
    return jax.shard_map(
        per_device, mesh=mesh, in_specs=in_specs, out_specs=out_specs, check_vma=False
    )
```

```python
import jax
import jax.numpy as jnp
from jax import lax
from jax.experimental import pallas as pl
from jax.experimental.pallas import tpu as pltpu
from jax.sharding import PartitionSpec as P


SUB = 8


def _chunk_scan(a, x, rows, reverse):
    sub = lax.broadcasted_iota(jnp.int32, a.shape, 0) % SUB
    for k in (1, 2, 4):
        shift = rows - k if reverse else k
        prev_a = pltpu.roll(a, shift, 0)
        prev_x = [pltpu.roll(v, shift, 0) for v in x]
        inside = sub < SUB - k if reverse else sub >= k
        x = [jnp.where(inside, a * p + v, v) for p, v in zip(prev_x, x)]
        a = jnp.where(inside, a * prev_a, a)
    return a, x


def _carry(a, x, out_a, out_x, rows, reverse):
    chunks = rows // SUB
    order = range(chunks - 1, -1, -1) if reverse else range(chunks)
    edge = 0 if reverse else SUB - 1
    carry_a = None
    for i in order:
        ca = a[i * SUB:(i + 1) * SUB]
        cx = [v[i * SUB:(i + 1) * SUB] for v in x]
        if carry_a is not None:
            cx = [c * px + v for c, px, v in zip([ca] * len(cx), carry_x, cx)]
            ca = ca * carry_a
        if out_a is not None:
            out_a[i * SUB:(i + 1) * SUB, :] = ca
        for o, v in zip(out_x, cx):
            o[i * SUB:(i + 1) * SUB, :] = v
        carry_a = jnp.broadcast_to(ca[edge:edge + 1], ca.shape)
        carry_x = [jnp.broadcast_to(v[edge:edge + 1], v.shape) for v in cx]


def scan_kernel(a_ref, u_ref, g_ref, s_ref, pf_ref, lf_ref, pb_ref, bl_ref, bp_ref):
    rows = a_ref.shape[0]
    a, (u,) = _chunk_scan(a_ref[...], [u_ref[...]], rows, False)
    _carry(a, [u], pf_ref, [lf_ref], rows, False)
    scale = s_ref[...]
    lf = lf_ref[...]
    pf = pf_ref[...]
    g, (ol, op) = _chunk_scan(g_ref[...], [lf - scale * lf, pf - scale * pf], rows, True)
    _carry(g, [ol, op], pb_ref, [bl_ref, bp_ref], rows, True)


def local_scans(factors, inflow, step_gain, scale):
    shape = jax.ShapeDtypeStruct(factors.shape, jnp.float32)
    rows, cols = factors.shape
    return pl.pallas_call(
        scan_kernel,
        out_shape=[shape] * 5,
        cost_estimate=pl.CostEstimate(flops=40 * rows * cols, bytes_accessed=36 * rows * cols, transcendentals=0),
    )(factors, inflow, step_gain, scale)


def sensor_reduce_scatter(partial, width):
    count = lax.axis_size("sensor")
    chips = count // 2
    j = lax.axis_index("sensor")
    chip = j // 2
    core = j % 2

    def piece(index):
        return lax.dynamic_slice_in_dim(partial, index * width, width, 1)

    send = jnp.stack([piece(2 * c + 1 - core) for c in range(chips)], 0)
    keep = jnp.stack([piece(2 * c + core) for c in range(chips)], 0)
    chip_sum = keep + lax.ppermute(send, "sensor", [(i, i ^ 1) for i in range(count)])
    total = lax.dynamic_index_in_dim(chip_sum, chip, 0, False)
    for shift in range(1, chips):
        part = lax.dynamic_index_in_dim(chip_sum, (chip + shift) % chips, 0, False)
        perm = [(i, (((i // 2) + shift) % chips) * 2 + i % 2) for i in range(count)]
        total = total + lax.ppermute(part, "sensor", perm)
    return total


def gather_tm(x):
    count = lax.axis_size("tm")
    place = lax.axis_index("tm")
    held = x[None]
    step = 1
    while step < count:
        other = lax.ppermute(held, "tm", [(i, i ^ step) for i in range(count)])
        low = (place & step) == 0
        held = jnp.where(
            low, jnp.concatenate([held, other], 0), jnp.concatenate([other, held], 0)
        )
        step *= 2
    return held


def per_device(observations, obs_list, gain_rows, decay, smooth_gain, model_rate, first_state):
    sensor_count = lax.axis_size("sensor")
    sensor_index = lax.axis_index("sensor")
    time_index = lax.axis_index("tm")
    time_count = lax.axis_size("tm")
    rows_here = observations.shape[0]
    block_count = observations.shape[1] // 128
    own_blocks = sensor_index * block_count + jnp.arange(block_count, dtype=jnp.int32)
    listed = jnp.any(obs_list[:, :, None] == own_blocks[None, None, :], axis=1).astype(jnp.float32)
    weighted = (
        (observations.reshape(rows_here, block_count, 128) * listed[:, :, None])
        .reshape(rows_here, block_count * 128)
        .astype(jnp.bfloat16)
    )
    partial_sum = jnp.dot(weighted, gain_rows, preferred_element_type=jnp.float32)
    width = gain_rows.shape[1] // sensor_count
    inflow = sensor_reduce_scatter(partial_sum, width)
    start_col = sensor_index * width
    factors = lax.dynamic_slice_in_dim(decay, start_col, width, 1)
    gains = lax.dynamic_slice_in_dim(smooth_gain, start_col, width, 1)
    rates = lax.dynamic_slice_in_dim(model_rate, start_col, width, 0)
    initial = lax.dynamic_slice_in_dim(first_state, start_col, width, 0)
    hour_ids = time_index * rows_here + jnp.arange(rows_here, dtype=jnp.int32)
    total_hours = rows_here * time_count
    step_gain = jnp.where((hour_ids == total_hours - 1)[:, None], jnp.float32(0.0), gains)
    scale = step_gain * rates[None, :]

    prod_fwd, local_fwd, prod_back, back_local, back_prod = local_scans(
        factors, inflow, step_gain, scale
    )

    summary = jnp.stack(
        [prod_fwd[-1], local_fwd[-1], prod_back[0], back_local[0], back_prod[0]], 0
    )
    every = gather_tm(summary)
    entering = [initial]
    for k in range(time_count - 1):
        entering.append(every[k, 0] * entering[-1] + every[k, 1])
    after = [jnp.zeros_like(initial)]
    for k in range(time_count - 1, 0, -1):
        after.append(every[k, 3] + every[k, 4] * entering[k] + every[k, 2] * after[-1])
    after = after[::-1]
    entering_here = lax.dynamic_index_in_dim(jnp.stack(entering, 0), time_index, 0, False)
    after_here = lax.dynamic_index_in_dim(jnp.stack(after, 0), time_index, 0, False)

    filtered = local_fwd + prod_fwd * entering_here[None, :]
    smoothed = back_local + back_prod * entering_here[None, :] + prod_back * after_here[None, :]
    return (filtered, smoothed)


def solution(mesh):
    in_specs = (
        P("tm", "sensor"),
        P("tm", "sensor"),
        P("sensor", None),
        P("tm", None),
        P("tm", None),
        P(),
        P(),
    )
    out_specs = (P("tm", "sensor"), P("tm", "sensor"))
    return jax.shard_map(
        per_device, mesh=mesh, in_specs=in_specs, out_specs=out_specs, check_vma=False
    )
```

```python
import jax
import jax.numpy as jnp
from jax import lax
from jax.experimental import pallas as pl
from jax.experimental.pallas import tpu as pltpu
from jax.sharding import PartitionSpec as P


SUB = 8


def _chunk_scan(a, x, rows, reverse):
    sub = lax.broadcasted_iota(jnp.int32, a.shape, 0) % SUB
    for k in (1, 2, 4):
        shift = rows - k if reverse else k
        prev_a = pltpu.roll(a, shift, 0)
        prev_x = [pltpu.roll(v, shift, 0) for v in x]
        inside = sub < SUB - k if reverse else sub >= k
        x = [jnp.where(inside, a * p + v, v) for p, v in zip(prev_x, x)]
        a = jnp.where(inside, a * prev_a, a)
    return a, x


def _carry(a, x, out_a, out_x, rows, reverse):
    chunks = rows // SUB
    order = range(chunks - 1, -1, -1) if reverse else range(chunks)
    edge = 0 if reverse else SUB - 1
    carry_a = None
    for i in order:
        ca = a[i * SUB:(i + 1) * SUB]
        cx = [v[i * SUB:(i + 1) * SUB] for v in x]
        if carry_a is not None:
            cx = [c * px + v for c, px, v in zip([ca] * len(cx), carry_x, cx)]
            ca = ca * carry_a
        if out_a is not None:
            out_a[i * SUB:(i + 1) * SUB, :] = ca
        for o, v in zip(out_x, cx):
            o[i * SUB:(i + 1) * SUB, :] = v
        carry_a = jnp.broadcast_to(ca[edge:edge + 1], ca.shape)
        carry_x = [jnp.broadcast_to(v[edge:edge + 1], v.shape) for v in cx]


def scan_kernel(a_ref, u_ref, g_ref, s_ref, pf_ref, lf_ref, pb_ref, bl_ref, bp_ref, sum_ref):
    rows = a_ref.shape[0]
    a, (u,) = _chunk_scan(a_ref[...], [u_ref[...]], rows, False)
    _carry(a, [u], pf_ref, [lf_ref], rows, False)
    scale = s_ref[...]
    lf = lf_ref[...]
    pf = pf_ref[...]
    g, (ol, op) = _chunk_scan(g_ref[...], [lf - scale * lf, pf - scale * pf], rows, True)
    _carry(g, [ol, op], pb_ref, [bl_ref, bp_ref], rows, True)
    sum_ref[...] = jnp.zeros_like(sum_ref)
    sum_ref[0:1, :] = pf_ref[rows - 1:rows, :]
    sum_ref[1:2, :] = lf_ref[rows - 1:rows, :]
    sum_ref[2:3, :] = pb_ref[0:1, :]
    sum_ref[3:4, :] = bl_ref[0:1, :]
    sum_ref[4:5, :] = bp_ref[0:1, :]


def local_scans(factors, inflow, step_gain, scale):
    shape = jax.ShapeDtypeStruct(factors.shape, jnp.float32)
    rows, cols = factors.shape
    return pl.pallas_call(
        scan_kernel,
        out_shape=[shape] * 5 + [jax.ShapeDtypeStruct((SUB, cols), jnp.float32)],
        cost_estimate=pl.CostEstimate(flops=40 * rows * cols, bytes_accessed=36 * rows * cols, transcendentals=0),
    )(factors, inflow, step_gain, scale)


def combine_kernel(every_ref, init_ref, pf_ref, lf_ref, pb_ref, bl_ref, bp_ref, f_ref, s_ref):
    count = every_ref.shape[0]
    place = lax.axis_index("tm")
    entering = [init_ref[...]]
    for k in range(count - 1):
        tile = every_ref[k]
        entering.append(tile[0:1] * entering[-1] + tile[1:2])
    after = jnp.zeros_like(entering[0])
    e_here = jnp.where(place == count - 1, entering[count - 1], 0.0)
    y_here = jnp.zeros_like(after)
    for k in range(count - 1, 0, -1):
        tile = every_ref[k]
        after = tile[3:4] + tile[4:5] * entering[k] + tile[2:3] * after
        e_here = jnp.where(place == k - 1, entering[k - 1], e_here)
        y_here = jnp.where(place == k - 1, after, y_here)
    f_ref[...] = lf_ref[...] + pf_ref[...] * e_here
    s_ref[...] = bl_ref[...] + bp_ref[...] * e_here + pb_ref[...] * y_here


def combine(every, initial, pf, lf, pb, bl, bp):
    rows, cols = pf.shape
    shape = jax.ShapeDtypeStruct(pf.shape, jnp.float32)
    return pl.pallas_call(
        combine_kernel,
        out_shape=[shape, shape],
        cost_estimate=pl.CostEstimate(flops=5 * rows * cols, bytes_accessed=28 * rows * cols, transcendentals=0),
    )(every, initial, pf, lf, pb, bl, bp)


def sensor_reduce_scatter(partial, width):
    count = lax.axis_size("sensor")
    chips = count // 2
    j = lax.axis_index("sensor")
    chip = j // 2
    core = j % 2

    def piece(index):
        return lax.dynamic_slice_in_dim(partial, index * width, width, 1)

    send = jnp.stack([piece(2 * c + 1 - core) for c in range(chips)], 0)
    keep = jnp.stack([piece(2 * c + core) for c in range(chips)], 0)
    chip_sum = keep + lax.ppermute(send, "sensor", [(i, i ^ 1) for i in range(count)])
    total = lax.dynamic_index_in_dim(chip_sum, chip, 0, False)
    for shift in range(1, chips):
        part = lax.dynamic_index_in_dim(chip_sum, (chip + shift) % chips, 0, False)
        perm = [(i, (((i // 2) + shift) % chips) * 2 + i % 2) for i in range(count)]
        total = total + lax.ppermute(part, "sensor", perm)
    return total


def gather_tm(x):
    count = lax.axis_size("tm")
    place = lax.axis_index("tm")
    held = x[None]
    step = 1
    while step < count:
        other = lax.ppermute(held, "tm", [(i, i ^ step) for i in range(count)])
        low = (place & step) == 0
        held = jnp.where(
            low, jnp.concatenate([held, other], 0), jnp.concatenate([other, held], 0)
        )
        step *= 2
    return held


def per_device(observations, obs_list, gain_rows, decay, smooth_gain, model_rate, first_state):
    sensor_count = lax.axis_size("sensor")
    sensor_index = lax.axis_index("sensor")
    time_index = lax.axis_index("tm")
    time_count = lax.axis_size("tm")
    rows_here = observations.shape[0]
    block_count = observations.shape[1] // 128
    own_blocks = sensor_index * block_count + jnp.arange(block_count, dtype=jnp.int32)
    listed = jnp.any(obs_list[:, :, None] == own_blocks[None, None, :], axis=1).astype(jnp.float32)
    weighted = (
        (observations.reshape(rows_here, block_count, 128) * listed[:, :, None])
        .reshape(rows_here, block_count * 128)
        .astype(jnp.bfloat16)
    )
    partial_sum = jnp.dot(weighted, gain_rows, preferred_element_type=jnp.float32)
    width = gain_rows.shape[1] // sensor_count
    inflow = sensor_reduce_scatter(partial_sum, width)
    start_col = sensor_index * width
    factors = lax.dynamic_slice_in_dim(decay, start_col, width, 1)
    gains = lax.dynamic_slice_in_dim(smooth_gain, start_col, width, 1)
    rates = lax.dynamic_slice_in_dim(model_rate, start_col, width, 0)
    initial = lax.dynamic_slice_in_dim(first_state, start_col, width, 0)
    hour_ids = time_index * rows_here + jnp.arange(rows_here, dtype=jnp.int32)
    total_hours = rows_here * time_count
    step_gain = jnp.where((hour_ids == total_hours - 1)[:, None], jnp.float32(0.0), gains)
    scale = step_gain * rates[None, :]

    prod_fwd, local_fwd, prod_back, back_local, back_prod, summary = local_scans(
        factors, inflow, step_gain, scale
    )
    every = gather_tm(summary)
    filtered, smoothed = combine(
        every, initial[None, :], prod_fwd, local_fwd, prod_back, back_local, back_prod
    )
    return (filtered, smoothed)


def solution(mesh):
    in_specs = (
        P("tm", "sensor"),
        P("tm", "sensor"),
        P("sensor", None),
        P("tm", None),
        P("tm", None),
        P(),
        P(),
    )
    out_specs = (P("tm", "sensor"), P("tm", "sensor"))
    return jax.shard_map(
        per_device, mesh=mesh, in_specs=in_specs, out_specs=out_specs, check_vma=False
    )
```

```python
import jax
import jax.numpy as jnp
from jax import lax
from jax.experimental import pallas as pl
from jax.experimental.pallas import tpu as pltpu
from jax.sharding import PartitionSpec as P


SUB = 8


def _chunk_scan(a, x, rows, reverse):
    sub = lax.broadcasted_iota(jnp.int32, a.shape, 0) % SUB
    for k in (1, 2, 4):
        shift = rows - k if reverse else k
        prev_a = pltpu.roll(a, shift, 0)
        prev_x = [pltpu.roll(v, shift, 0) for v in x]
        inside = sub < SUB - k if reverse else sub >= k
        x = [jnp.where(inside, a * p + v, v) for p, v in zip(prev_x, x)]
        a = jnp.where(inside, a * prev_a, a)
    return a, x


def _carry(a, x, out_a, out_x, rows, reverse):
    chunks = rows // SUB
    order = range(chunks - 1, -1, -1) if reverse else range(chunks)
    edge = 0 if reverse else SUB - 1
    carry_a = None
    for i in order:
        ca = a[i * SUB:(i + 1) * SUB]
        cx = [v[i * SUB:(i + 1) * SUB] for v in x]
        if carry_a is not None:
            cx = [c * px + v for c, px, v in zip([ca] * len(cx), carry_x, cx)]
            ca = ca * carry_a
        if out_a is not None:
            out_a[i * SUB:(i + 1) * SUB, :] = ca
        for o, v in zip(out_x, cx):
            o[i * SUB:(i + 1) * SUB, :] = v
        carry_a = jnp.broadcast_to(ca[edge:edge + 1], ca.shape)
        carry_x = [jnp.broadcast_to(v[edge:edge + 1], v.shape) for v in cx]


def scan_kernel(a_ref, u_ref, g_ref, s_ref, pf_ref, lf_ref, pb_ref, bl_ref, bp_ref, sum_ref):
    rows = a_ref.shape[0]
    a, (u,) = _chunk_scan(a_ref[...], [u_ref[...]], rows, False)
    _carry(a, [u], pf_ref, [lf_ref], rows, False)
    scale = s_ref[...]
    lf = lf_ref[...]
    pf = pf_ref[...]
    g, (ol, op) = _chunk_scan(g_ref[...], [lf - scale * lf, pf - scale * pf], rows, True)
    _carry(g, [ol, op], pb_ref, [bl_ref, bp_ref], rows, True)
    sum_ref[...] = jnp.zeros_like(sum_ref)
    sum_ref[0:1, :] = pf_ref[rows - 1:rows, :]
    sum_ref[1:2, :] = lf_ref[rows - 1:rows, :]
    sum_ref[2:3, :] = pb_ref[0:1, :]
    sum_ref[3:4, :] = bl_ref[0:1, :]
    sum_ref[4:5, :] = bp_ref[0:1, :]


def local_scans(factors, inflow, step_gain, scale):
    shape = jax.ShapeDtypeStruct(factors.shape, jnp.float32)
    rows, cols = factors.shape
    return pl.pallas_call(
        scan_kernel,
        out_shape=[shape] * 5 + [jax.ShapeDtypeStruct((SUB, cols), jnp.float32)],
        cost_estimate=pl.CostEstimate(flops=40 * rows * cols, bytes_accessed=36 * rows * cols, transcendentals=0),
    )(factors, inflow, step_gain, scale)


def combine_kernel(every_ref, init_ref, pf_ref, lf_ref, pb_ref, bl_ref, bp_ref, f_ref, s_ref):
    count = every_ref.shape[0]
    place = lax.axis_index("tm")
    entering = [init_ref[...]]
    for k in range(count - 1):
        tile = every_ref[k]
        entering.append(tile[0:1] * entering[-1] + tile[1:2])
    after = jnp.zeros_like(entering[0])
    e_here = jnp.where(place == count - 1, entering[count - 1], 0.0)
    y_here = jnp.zeros_like(after)
    for k in range(count - 1, 0, -1):
        tile = every_ref[k]
        after = tile[3:4] + tile[4:5] * entering[k] + tile[2:3] * after
        e_here = jnp.where(place == k - 1, entering[k - 1], e_here)
        y_here = jnp.where(place == k - 1, after, y_here)
    f_ref[...] = lf_ref[...] + pf_ref[...] * e_here
    s_ref[...] = bl_ref[...] + bp_ref[...] * e_here + pb_ref[...] * y_here


def combine(every, initial, pf, lf, pb, bl, bp):
    rows, cols = pf.shape
    shape = jax.ShapeDtypeStruct(pf.shape, jnp.float32)
    return pl.pallas_call(
        combine_kernel,
        out_shape=[shape, shape],
        cost_estimate=pl.CostEstimate(flops=5 * rows * cols, bytes_accessed=28 * rows * cols, transcendentals=0),
    )(every, initial, pf, lf, pb, bl, bp)


def matmul_kernel(core_ref, obs_ref, listed_ref, gain_ref, keep_ref, send_ref, lhs_ref):
    @pl.when(pl.program_id(0) == 0)
    def _():
        for b in range(listed_ref.shape[1]):
            cols = pl.ds(128 * b, 128)
            block = obs_ref[:, cols]
            lhs_ref[:, cols] = jnp.where(listed_ref[:, b:b + 1] > 0, block, jnp.zeros_like(block))

    prod = jnp.dot(lhs_ref[...], gain_ref[...], preferred_element_type=jnp.float32)
    half = prod.shape[1] // 2
    even = core_ref[0] == 0
    keep_ref[0] = jnp.where(even, prod[:, :half], prod[:, half:])
    send_ref[0] = jnp.where(even, prod[:, half:], prod[:, :half])


def listed_matmul(core, observations, listed, gain_rows):
    rows, depth = observations.shape
    modes = gain_rows.shape[1]
    tile = 256
    tiles = modes // tile
    piece = jax.ShapeDtypeStruct((tiles, rows, tile // 2), jnp.float32)
    return pl.pallas_call(
        matmul_kernel,
        grid=(tiles,),
        in_specs=[
            pl.BlockSpec(memory_space=pltpu.SMEM),
            pl.BlockSpec((rows, depth), lambda j: (0, 0)),
            pl.BlockSpec((rows, listed.shape[1]), lambda j: (0, 0)),
            pl.BlockSpec((depth, tile), lambda j: (0, j)),
        ],
        out_specs=[
            pl.BlockSpec((1, rows, tile // 2), lambda j: (j, 0, 0)),
            pl.BlockSpec((1, rows, tile // 2), lambda j: (j, 0, 0)),
        ],
        out_shape=[piece, piece],
        scratch_shapes=[pltpu.VMEM((rows, depth), jnp.bfloat16)],
        compiler_params=pltpu.CompilerParams(dimension_semantics=("arbitrary",)),
        cost_estimate=pl.CostEstimate(
            flops=2 * rows * depth * modes,
            bytes_accessed=2 * rows * depth + 2 * depth * modes + 4 * rows * modes,
            transcendentals=0,
        ),
    )(core, observations, listed, gain_rows)


def sensor_reduce_scatter(keep, send):
    count = lax.axis_size("sensor")
    chips = count // 2
    j = lax.axis_index("sensor")
    chip = j // 2
    chip_sum = keep + lax.ppermute(send, "sensor", [(i, i ^ 1) for i in range(count)])
    total = lax.dynamic_index_in_dim(chip_sum, chip, 0, False)
    for shift in range(1, chips):
        part = lax.dynamic_index_in_dim(chip_sum, (chip + shift) % chips, 0, False)
        perm = [(i, (((i // 2) + shift) % chips) * 2 + i % 2) for i in range(count)]
        total = total + lax.ppermute(part, "sensor", perm)
    return total


def gather_tm(x):
    count = lax.axis_size("tm")
    place = lax.axis_index("tm")
    held = x[None]
    step = 1
    while step < count:
        other = lax.ppermute(held, "tm", [(i, i ^ step) for i in range(count)])
        low = (place & step) == 0
        held = jnp.where(
            low, jnp.concatenate([held, other], 0), jnp.concatenate([other, held], 0)
        )
        step *= 2
    return held


def per_device(observations, obs_list, gain_rows, decay, smooth_gain, model_rate, first_state):
    sensor_count = lax.axis_size("sensor")
    sensor_index = lax.axis_index("sensor")
    time_index = lax.axis_index("tm")
    time_count = lax.axis_size("tm")
    rows_here = observations.shape[0]
    block_count = observations.shape[1] // 128
    own_blocks = sensor_index * block_count + jnp.arange(block_count, dtype=jnp.int32)
    listed = jnp.any(obs_list[:, :, None] == own_blocks[None, None, :], axis=1).astype(jnp.float32)
    core = (sensor_index % 2).astype(jnp.int32)[None]
    keep, send = listed_matmul(core, observations, listed, gain_rows)
    width = gain_rows.shape[1] // sensor_count
    inflow = sensor_reduce_scatter(keep, send)
    start_col = sensor_index * width
    factors = lax.dynamic_slice_in_dim(decay, start_col, width, 1)
    gains = lax.dynamic_slice_in_dim(smooth_gain, start_col, width, 1)
    rates = lax.dynamic_slice_in_dim(model_rate, start_col, width, 0)
    initial = lax.dynamic_slice_in_dim(first_state, start_col, width, 0)
    hour_ids = time_index * rows_here + jnp.arange(rows_here, dtype=jnp.int32)
    total_hours = rows_here * time_count
    step_gain = jnp.where((hour_ids == total_hours - 1)[:, None], jnp.float32(0.0), gains)
    scale = step_gain * rates[None, :]

    prod_fwd, local_fwd, prod_back, back_local, back_prod, summary = local_scans(
        factors, inflow, step_gain, scale
    )
    every = gather_tm(summary)
    filtered, smoothed = combine(
        every, initial[None, :], prod_fwd, local_fwd, prod_back, back_local, back_prod
    )
    return (filtered, smoothed)


def solution(mesh):
    in_specs = (
        P("tm", "sensor"),
        P("tm", "sensor"),
        P("sensor", None),
        P("tm", None),
        P("tm", None),
        P(),
        P(),
    )
    out_specs = (P("tm", "sensor"), P("tm", "sensor"))
    return jax.shard_map(
        per_device, mesh=mesh, in_specs=in_specs, out_specs=out_specs, check_vma=False
    )
```

```python
import jax
import jax.numpy as jnp
from jax import lax
from jax.experimental import pallas as pl
from jax.experimental.pallas import tpu as pltpu
from jax.sharding import PartitionSpec as P


SUB = 8


def _chunk_scan(a, x, rows, reverse):
    sub = lax.broadcasted_iota(jnp.int32, a.shape, 0) % SUB
    for k in (1, 2, 4):
        shift = rows - k if reverse else k
        prev_a = pltpu.roll(a, shift, 0)
        prev_x = [pltpu.roll(v, shift, 0) for v in x]
        inside = sub < SUB - k if reverse else sub >= k
        x = [jnp.where(inside, a * p + v, v) for p, v in zip(prev_x, x)]
        a = jnp.where(inside, a * prev_a, a)
    return a, x


def _carry(a, x, out_a, out_x, rows, reverse):
    chunks = rows // SUB
    order = range(chunks - 1, -1, -1) if reverse else range(chunks)
    edge = 0 if reverse else SUB - 1
    carry_a = None
    for i in order:
        ca = a[i * SUB:(i + 1) * SUB]
        cx = [v[i * SUB:(i + 1) * SUB] for v in x]
        if carry_a is not None:
            cx = [c * px + v for c, px, v in zip([ca] * len(cx), carry_x, cx)]
            ca = ca * carry_a
        if out_a is not None:
            out_a[i * SUB:(i + 1) * SUB, :] = ca
        for o, v in zip(out_x, cx):
            o[i * SUB:(i + 1) * SUB, :] = v
        carry_a = jnp.broadcast_to(ca[edge:edge + 1], ca.shape)
        carry_x = [jnp.broadcast_to(v[edge:edge + 1], v.shape) for v in cx]


def scan_kernel(a_ref, u_ref, g_ref, s_ref, pf_ref, lf_ref, pb_ref, bl_ref, bp_ref, sum_ref):
    rows = a_ref.shape[0]
    a, (u,) = _chunk_scan(a_ref[...], [u_ref[...]], rows, False)
    _carry(a, [u], pf_ref, [lf_ref], rows, False)
    scale = s_ref[...]
    lf = lf_ref[...]
    pf = pf_ref[...]
    g, (ol, op) = _chunk_scan(g_ref[...], [lf - scale * lf, pf - scale * pf], rows, True)
    _carry(g, [ol, op], pb_ref, [bl_ref, bp_ref], rows, True)
    sum_ref[...] = jnp.zeros_like(sum_ref)
    sum_ref[0:1, :] = pf_ref[rows - 1:rows, :]
    sum_ref[1:2, :] = lf_ref[rows - 1:rows, :]
    sum_ref[2:3, :] = pb_ref[0:1, :]
    sum_ref[3:4, :] = bl_ref[0:1, :]
    sum_ref[4:5, :] = bp_ref[0:1, :]


def local_scans(factors, inflow, step_gain, scale):
    shape = jax.ShapeDtypeStruct(factors.shape, jnp.float32)
    rows, cols = factors.shape
    return pl.pallas_call(
        scan_kernel,
        out_shape=[shape] * 5 + [jax.ShapeDtypeStruct((SUB, cols), jnp.float32)],
        cost_estimate=pl.CostEstimate(flops=40 * rows * cols, bytes_accessed=36 * rows * cols, transcendentals=0),
    )(factors, inflow, step_gain, scale)


def combine_kernel(every_ref, init_ref, pf_ref, lf_ref, pb_ref, bl_ref, bp_ref, f_ref, s_ref):
    count = every_ref.shape[0]
    place = lax.axis_index("tm")
    entering = [init_ref[...]]
    for k in range(count - 1):
        tile = every_ref[k]
        entering.append(tile[0:1] * entering[-1] + tile[1:2])
    after = jnp.zeros_like(entering[0])
    e_here = jnp.where(place == count - 1, entering[count - 1], 0.0)
    y_here = jnp.zeros_like(after)
    for k in range(count - 1, 0, -1):
        tile = every_ref[k]
        after = tile[3:4] + tile[4:5] * entering[k] + tile[2:3] * after
        e_here = jnp.where(place == k - 1, entering[k - 1], e_here)
        y_here = jnp.where(place == k - 1, after, y_here)
    f_ref[...] = lf_ref[...] + pf_ref[...] * e_here
    s_ref[...] = bl_ref[...] + bp_ref[...] * e_here + pb_ref[...] * y_here


def combine(every, initial, pf, lf, pb, bl, bp):
    rows, cols = pf.shape
    shape = jax.ShapeDtypeStruct(pf.shape, jnp.float32)
    return pl.pallas_call(
        combine_kernel,
        out_shape=[shape, shape],
        cost_estimate=pl.CostEstimate(flops=5 * rows * cols, bytes_accessed=28 * rows * cols, transcendentals=0),
    )(every, initial, pf, lf, pb, bl, bp)


def matmul_kernel(core_ref, obs_ref, listed_ref, gain_ref, keep_ref, send_ref, lhs_ref):
    @pl.when(pl.program_id(0) == 0)
    def _():
        for b in range(listed_ref.shape[1]):
            cols = pl.ds(128 * b, 128)
            block = obs_ref[:, cols]
            lhs_ref[:, cols] = jnp.where(listed_ref[:, b:b + 1] > 0, block, jnp.zeros_like(block))

    prod = jnp.dot(lhs_ref[...], gain_ref[...], preferred_element_type=jnp.float32)
    half = prod.shape[1] // 2
    even = core_ref[0] == 0
    keep_ref[0] = jnp.where(even, prod[:, :half], prod[:, half:])
    send_ref[0] = jnp.where(even, prod[:, half:], prod[:, :half])


def listed_matmul(core, observations, listed, gain_rows):
    rows, depth = observations.shape
    modes = gain_rows.shape[1]
    tile = 256
    tiles = modes // tile
    piece = jax.ShapeDtypeStruct((tiles, rows, tile // 2), jnp.float32)
    return pl.pallas_call(
        matmul_kernel,
        grid=(tiles,),
        in_specs=[
            pl.BlockSpec(memory_space=pltpu.SMEM),
            pl.BlockSpec((rows, depth), lambda j: (0, 0)),
            pl.BlockSpec((rows, listed.shape[1]), lambda j: (0, 0)),
            pl.BlockSpec((depth, tile), lambda j: (0, j)),
        ],
        out_specs=[
            pl.BlockSpec((1, rows, tile // 2), lambda j: (j, 0, 0)),
            pl.BlockSpec((1, rows, tile // 2), lambda j: (j, 0, 0)),
        ],
        out_shape=[piece, piece],
        scratch_shapes=[pltpu.VMEM((rows, depth), jnp.bfloat16)],
        compiler_params=pltpu.CompilerParams(dimension_semantics=("arbitrary",)),
        cost_estimate=pl.CostEstimate(
            flops=2 * rows * depth * modes,
            bytes_accessed=2 * rows * depth + 2 * depth * modes + 4 * rows * modes,
            transcendentals=0,
        ),
    )(core, observations, listed, gain_rows)


def sensor_reduce_scatter(keep, send):
    count = lax.axis_size("sensor")
    chips = count // 2
    j = lax.axis_index("sensor")
    chip = j // 2
    chip_sum = keep + lax.ppermute(send, "sensor", [(i, i ^ 1) for i in range(count)])
    total = lax.dynamic_index_in_dim(chip_sum, chip, 0, False)
    for shift in range(1, chips):
        part = lax.dynamic_index_in_dim(chip_sum, (chip + shift) % chips, 0, False)
        perm = [(i, (((i // 2) + shift) % chips) * 2 + i % 2) for i in range(count)]
        total = total + lax.ppermute(part, "sensor", perm)
    return total


def gather_tm(x):
    count = lax.axis_size("tm")
    copies = jnp.broadcast_to(x[None], (count,) + x.shape)
    return lax.all_to_all(copies, "tm", 0, 0, tiled=True)


def per_device(observations, obs_list, gain_rows, decay, smooth_gain, model_rate, first_state):
    sensor_count = lax.axis_size("sensor")
    sensor_index = lax.axis_index("sensor")
    time_index = lax.axis_index("tm")
    time_count = lax.axis_size("tm")
    rows_here = observations.shape[0]
    block_count = observations.shape[1] // 128
    own_blocks = sensor_index * block_count + jnp.arange(block_count, dtype=jnp.int32)
    listed = jnp.any(obs_list[:, :, None] == own_blocks[None, None, :], axis=1).astype(jnp.float32)
    core = (sensor_index % 2).astype(jnp.int32)[None]
    keep, send = listed_matmul(core, observations, listed, gain_rows)
    width = gain_rows.shape[1] // sensor_count
    inflow = sensor_reduce_scatter(keep, send)
    start_col = sensor_index * width
    factors = lax.dynamic_slice_in_dim(decay, start_col, width, 1)
    gains = lax.dynamic_slice_in_dim(smooth_gain, start_col, width, 1)
    rates = lax.dynamic_slice_in_dim(model_rate, start_col, width, 0)
    initial = lax.dynamic_slice_in_dim(first_state, start_col, width, 0)
    hour_ids = time_index * rows_here + jnp.arange(rows_here, dtype=jnp.int32)
    total_hours = rows_here * time_count
    step_gain = jnp.where((hour_ids == total_hours - 1)[:, None], jnp.float32(0.0), gains)
    scale = step_gain * rates[None, :]

    prod_fwd, local_fwd, prod_back, back_local, back_prod, summary = local_scans(
        factors, inflow, step_gain, scale
    )
    every = gather_tm(summary)
    filtered, smoothed = combine(
        every, initial[None, :], prod_fwd, local_fwd, prod_back, back_local, back_prod
    )
    return (filtered, smoothed)


def solution(mesh):
    in_specs = (
        P("tm", "sensor"),
        P("tm", "sensor"),
        P("sensor", None),
        P("tm", None),
        P("tm", None),
        P(),
        P(),
    )
    out_specs = (P("tm", "sensor"), P("tm", "sensor"))
    return jax.shard_map(
        per_device, mesh=mesh, in_specs=in_specs, out_specs=out_specs, check_vma=False
    )
```

```python
import jax
import jax.numpy as jnp
from jax import lax
from jax.experimental import pallas as pl
from jax.experimental.pallas import tpu as pltpu
from jax.sharding import PartitionSpec as P


SUB = 8


def _chunk_scan(a, x, rows, reverse):
    sub = lax.broadcasted_iota(jnp.int32, a.shape, 0) % SUB
    for k in (1, 2, 4):
        shift = rows - k if reverse else k
        prev_a = pltpu.roll(a, shift, 0)
        prev_x = [pltpu.roll(v, shift, 0) for v in x]
        inside = sub < SUB - k if reverse else sub >= k
        x = [jnp.where(inside, a * p + v, v) for p, v in zip(prev_x, x)]
        a = jnp.where(inside, a * prev_a, a)
    return a, x


def _carry(a, x, out_a, out_x, rows, reverse):
    chunks = rows // SUB
    order = range(chunks - 1, -1, -1) if reverse else range(chunks)
    edge = 0 if reverse else SUB - 1
    carry_a = None
    for i in order:
        ca = a[i * SUB:(i + 1) * SUB]
        cx = [v[i * SUB:(i + 1) * SUB] for v in x]
        if carry_a is not None:
            cx = [c * px + v for c, px, v in zip([ca] * len(cx), carry_x, cx)]
            ca = ca * carry_a
        if out_a is not None:
            out_a[i * SUB:(i + 1) * SUB, :] = ca
        for o, v in zip(out_x, cx):
            o[i * SUB:(i + 1) * SUB, :] = v
        carry_a = jnp.broadcast_to(ca[edge:edge + 1], ca.shape)
        carry_x = [jnp.broadcast_to(v[edge:edge + 1], v.shape) for v in cx]


def scan_kernel(a_ref, own_ref, r1_ref, r2_ref, r3_ref, g_ref, s_ref, pf_ref, lf_ref, pb_ref, bl_ref,
                bp_ref, sum_ref):
    rows = a_ref.shape[0]
    inflow = ((own_ref[...] + r1_ref[...]) + r2_ref[...]) + r3_ref[...]
    a, (u,) = _chunk_scan(a_ref[...], [inflow], rows, False)
    _carry(a, [u], pf_ref, [lf_ref], rows, False)
    scale = s_ref[...]
    lf = lf_ref[...]
    pf = pf_ref[...]
    g, (ol, op) = _chunk_scan(g_ref[...], [lf - scale * lf, pf - scale * pf], rows, True)
    _carry(g, [ol, op], pb_ref, [bl_ref, bp_ref], rows, True)
    sub = lax.broadcasted_iota(jnp.int32, (SUB, pf_ref.shape[1]), 0)
    tile = jnp.zeros((SUB, pf_ref.shape[1]), jnp.float32)
    for row, value in enumerate(
        [pf_ref[rows - 1:rows, :], lf_ref[rows - 1:rows, :], pb_ref[0:1, :], bl_ref[0:1, :], bp_ref[0:1, :]]
    ):
        tile = jnp.where(sub == row, jnp.broadcast_to(value, tile.shape), tile)
    for k in range(sum_ref.shape[0]):
        sum_ref[k] = tile


def local_scans(factors, parts, step_gain, scale, blocks):
    shape = jax.ShapeDtypeStruct(factors.shape, jnp.float32)
    rows, cols = factors.shape
    return pl.pallas_call(
        scan_kernel,
        out_shape=[shape] * 5 + [jax.ShapeDtypeStruct((blocks, SUB, cols), jnp.float32)],
        cost_estimate=pl.CostEstimate(flops=40 * rows * cols, bytes_accessed=48 * rows * cols, transcendentals=0),
    )(factors, *parts, step_gain, scale)


def combine_kernel(every_ref, init_ref, pf_ref, lf_ref, pb_ref, bl_ref, bp_ref, f_ref, s_ref):
    count = every_ref.shape[0]
    place = lax.axis_index("tm")
    entering = [init_ref[...]]
    for k in range(count - 1):
        tile = every_ref[k]
        entering.append(tile[0:1] * entering[-1] + tile[1:2])
    after = jnp.zeros_like(entering[0])
    e_here = jnp.where(place == count - 1, entering[count - 1], 0.0)
    y_here = jnp.zeros_like(after)
    for k in range(count - 1, 0, -1):
        tile = every_ref[k]
        after = tile[3:4] + tile[4:5] * entering[k] + tile[2:3] * after
        e_here = jnp.where(place == k - 1, entering[k - 1], e_here)
        y_here = jnp.where(place == k - 1, after, y_here)
    f_ref[...] = lf_ref[...] + pf_ref[...] * e_here
    s_ref[...] = bl_ref[...] + bp_ref[...] * e_here + pb_ref[...] * y_here


def combine(every, initial, pf, lf, pb, bl, bp):
    rows, cols = pf.shape
    shape = jax.ShapeDtypeStruct(pf.shape, jnp.float32)
    return pl.pallas_call(
        combine_kernel,
        out_shape=[shape, shape],
        cost_estimate=pl.CostEstimate(flops=5 * rows * cols, bytes_accessed=28 * rows * cols, transcendentals=0),
    )(every, initial, pf, lf, pb, bl, bp)


def matmul_kernel(core_ref, obs_ref, listed_ref, gain_ref, keep_ref, send_ref, lhs_ref):
    @pl.when(pl.program_id(0) == 0)
    def _():
        for b in range(listed_ref.shape[1]):
            cols = pl.ds(128 * b, 128)
            block = obs_ref[:, cols]
            lhs_ref[:, cols] = jnp.where(listed_ref[:, b:b + 1] > 0, block, jnp.zeros_like(block))

    prod = jnp.dot(lhs_ref[...], gain_ref[...], preferred_element_type=jnp.float32)
    half = prod.shape[1] // 2
    even = core_ref[0] == 0
    keep_ref[0] = jnp.where(even, prod[:, :half], prod[:, half:])
    send_ref[0] = jnp.where(even, prod[:, half:], prod[:, :half])


def listed_matmul(core, observations, listed, gain_rows):
    rows, depth = observations.shape
    modes = gain_rows.shape[1]
    tile = 256
    tiles = modes // tile
    piece = jax.ShapeDtypeStruct((tiles, rows, tile // 2), jnp.float32)
    return pl.pallas_call(
        matmul_kernel,
        grid=(tiles,),
        in_specs=[
            pl.BlockSpec(memory_space=pltpu.SMEM),
            pl.BlockSpec((rows, depth), lambda j: (0, 0)),
            pl.BlockSpec((rows, listed.shape[1]), lambda j: (0, 0)),
            pl.BlockSpec((depth, tile), lambda j: (0, j)),
        ],
        out_specs=[
            pl.BlockSpec((1, rows, tile // 2), lambda j: (j, 0, 0)),
            pl.BlockSpec((1, rows, tile // 2), lambda j: (j, 0, 0)),
        ],
        out_shape=[piece, piece],
        scratch_shapes=[pltpu.VMEM((rows, depth), jnp.bfloat16)],
        compiler_params=pltpu.CompilerParams(dimension_semantics=("arbitrary",)),
        cost_estimate=pl.CostEstimate(
            flops=2 * rows * depth * modes,
            bytes_accessed=2 * rows * depth + 2 * depth * modes + 4 * rows * modes,
            transcendentals=0,
        ),
    )(core, observations, listed, gain_rows)


def sensor_reduce_scatter(keep, send):
    count = lax.axis_size("sensor")
    chips = count // 2
    j = lax.axis_index("sensor")
    chip = j // 2
    chip_sum = keep + lax.ppermute(send, "sensor", [(i, i ^ 1) for i in range(count)])
    parts = [lax.dynamic_index_in_dim(chip_sum, chip, 0, False)]
    for shift in range(1, chips):
        part = lax.dynamic_index_in_dim(chip_sum, (chip + shift) % chips, 0, False)
        perm = [(i, (((i // 2) + shift) % chips) * 2 + i % 2) for i in range(count)]
        parts.append(lax.ppermute(part, "sensor", perm))
    return parts


def gather_tm(copies):
    return lax.all_to_all(copies, "tm", 0, 0, tiled=True)


def per_device(observations, obs_list, gain_rows, decay, smooth_gain, model_rate, first_state):
    sensor_count = lax.axis_size("sensor")
    sensor_index = lax.axis_index("sensor")
    time_index = lax.axis_index("tm")
    time_count = lax.axis_size("tm")
    rows_here = observations.shape[0]
    block_count = observations.shape[1] // 128
    own_blocks = sensor_index * block_count + jnp.arange(block_count, dtype=jnp.int32)
    listed = jnp.any(obs_list[:, :, None] == own_blocks[None, None, :], axis=1).astype(jnp.float32)
    core = (sensor_index % 2).astype(jnp.int32)[None]
    keep, send = listed_matmul(core, observations, listed, gain_rows)
    width = gain_rows.shape[1] // sensor_count
    parts = sensor_reduce_scatter(keep, send)
    start_col = sensor_index * width
    factors = lax.dynamic_slice_in_dim(decay, start_col, width, 1)
    gains = lax.dynamic_slice_in_dim(smooth_gain, start_col, width, 1)
    rates = lax.dynamic_slice_in_dim(model_rate, start_col, width, 0)
    initial = lax.dynamic_slice_in_dim(first_state, start_col, width, 0)
    hour_ids = time_index * rows_here + jnp.arange(rows_here, dtype=jnp.int32)
    total_hours = rows_here * time_count
    step_gain = jnp.where((hour_ids == total_hours - 1)[:, None], jnp.float32(0.0), gains)
    scale = step_gain * rates[None, :]

    prod_fwd, local_fwd, prod_back, back_local, back_prod, summary = local_scans(
        factors, parts, step_gain, scale, time_count
    )
    every = gather_tm(summary)
    filtered, smoothed = combine(
        every, initial[None, :], prod_fwd, local_fwd, prod_back, back_local, back_prod
    )
    return (filtered, smoothed)


def solution(mesh):
    in_specs = (
        P("tm", "sensor"),
        P("tm", "sensor"),
        P("sensor", None),
        P("tm", None),
        P("tm", None),
        P(),
        P(),
    )
    out_specs = (P("tm", "sensor"), P("tm", "sensor"))
    return jax.shard_map(
        per_device, mesh=mesh, in_specs=in_specs, out_specs=out_specs, check_vma=False
    )
```

```python
import jax
import jax.numpy as jnp
from jax import lax
from jax.experimental import pallas as pl
from jax.experimental.pallas import tpu as pltpu
from jax.sharding import PartitionSpec as P


SUB = 8


def _chunk_scan(a, x, rows, reverse):
    sub = lax.broadcasted_iota(jnp.int32, a.shape, 0) % SUB
    for k in (1, 2, 4):
        shift = rows - k if reverse else k
        prev_a = pltpu.roll(a, shift, 0)
        prev_x = [pltpu.roll(v, shift, 0) for v in x]
        inside = sub < SUB - k if reverse else sub >= k
        x = [jnp.where(inside, a * p + v, v) for p, v in zip(prev_x, x)]
        a = jnp.where(inside, a * prev_a, a)
    return a, x


def _carry(a, x, out_a, out_x, rows, reverse):
    chunks = rows // SUB
    order = range(chunks - 1, -1, -1) if reverse else range(chunks)
    edge = 0 if reverse else SUB - 1
    carry_a = None
    for i in order:
        ca = a[i * SUB:(i + 1) * SUB]
        cx = [v[i * SUB:(i + 1) * SUB] for v in x]
        if carry_a is not None:
            cx = [c * px + v for c, px, v in zip([ca] * len(cx), carry_x, cx)]
            ca = ca * carry_a
        if out_a is not None:
            out_a[i * SUB:(i + 1) * SUB, :] = ca
        for o, v in zip(out_x, cx):
            o[i * SUB:(i + 1) * SUB, :] = v
        carry_a = jnp.broadcast_to(ca[edge:edge + 1], ca.shape)
        carry_x = [jnp.broadcast_to(v[edge:edge + 1], v.shape) for v in cx]


def scan_kernel(a_ref, own_ref, r1_ref, r2_ref, r3_ref, g_ref, s_ref, pf_ref, lf_ref, pb_ref, bl_ref,
                bp_ref, sum_ref):
    rows = a_ref.shape[0]
    inflow = ((own_ref[...] + r1_ref[...]) + r2_ref[...]) + r3_ref[...]
    a, (u,) = _chunk_scan(a_ref[...], [inflow], rows, False)
    _carry(a, [u], pf_ref, [lf_ref], rows, False)
    scale = s_ref[...]
    lf = lf_ref[...]
    pf = pf_ref[...]
    g, (ol, op) = _chunk_scan(g_ref[...], [lf - scale * lf, pf - scale * pf], rows, True)
    _carry(g, [ol, op], pb_ref, [bl_ref, bp_ref], rows, True)
    sub = lax.broadcasted_iota(jnp.int32, (SUB, pf_ref.shape[1]), 0)
    tile = jnp.zeros((SUB, pf_ref.shape[1]), jnp.float32)
    for row, value in enumerate(
        [pf_ref[rows - 1:rows, :], lf_ref[rows - 1:rows, :], pb_ref[0:1, :], bl_ref[0:1, :], bp_ref[0:1, :]]
    ):
        tile = jnp.where(sub == row, jnp.broadcast_to(value, tile.shape), tile)
    for k in range(sum_ref.shape[0]):
        sum_ref[k] = tile


def local_scans(factors, parts, step_gain, scale, blocks):
    shape = jax.ShapeDtypeStruct(factors.shape, jnp.float32)
    rows, cols = factors.shape
    return pl.pallas_call(
        scan_kernel,
        out_shape=[shape] * 5 + [jax.ShapeDtypeStruct((blocks, SUB, cols), jnp.float32)],
        cost_estimate=pl.CostEstimate(flops=40 * rows * cols, bytes_accessed=48 * rows * cols, transcendentals=0),
    )(factors, *parts, step_gain, scale)


def combine_kernel(every_ref, init_ref, pf_ref, lf_ref, pb_ref, bl_ref, bp_ref, f_ref, s_ref):
    count = every_ref.shape[0]
    place = lax.axis_index("tm")
    entering = [init_ref[...]]
    for k in range(count - 1):
        tile = every_ref[k]
        entering.append(tile[0:1] * entering[-1] + tile[1:2])
    after = jnp.zeros_like(entering[0])
    e_here = jnp.where(place == count - 1, entering[count - 1], 0.0)
    y_here = jnp.zeros_like(after)
    for k in range(count - 1, 0, -1):
        tile = every_ref[k]
        after = tile[3:4] + tile[4:5] * entering[k] + tile[2:3] * after
        e_here = jnp.where(place == k - 1, entering[k - 1], e_here)
        y_here = jnp.where(place == k - 1, after, y_here)
    f_ref[...] = lf_ref[...] + pf_ref[...] * e_here
    s_ref[...] = bl_ref[...] + bp_ref[...] * e_here + pb_ref[...] * y_here


def combine(every, initial, pf, lf, pb, bl, bp):
    rows, cols = pf.shape
    shape = jax.ShapeDtypeStruct(pf.shape, jnp.float32)
    return pl.pallas_call(
        combine_kernel,
        out_shape=[shape, shape],
        cost_estimate=pl.CostEstimate(flops=5 * rows * cols, bytes_accessed=28 * rows * cols, transcendentals=0),
    )(every, initial, pf, lf, pb, bl, bp)


def matmul_kernel(core_ref, obs_ref, listed_ref, gain_ref, keep_ref, send_ref, lhs_ref):
    @pl.when(pl.program_id(0) == 0)
    def _():
        for b in range(listed_ref.shape[1]):
            cols = pl.ds(128 * b, 128)
            block = obs_ref[:, cols]
            lhs_ref[:, cols] = jnp.where(listed_ref[:, b:b + 1] > 0, block, jnp.zeros_like(block))

    prod = jnp.dot(lhs_ref[...], gain_ref[...], preferred_element_type=jnp.float32)
    half = prod.shape[1] // 2
    even = core_ref[0] == 0
    keep_ref[0] = jnp.where(even, prod[:, :half], prod[:, half:])
    send_ref[0] = jnp.where(even, prod[:, half:], prod[:, :half])


def listed_matmul(core, observations, listed, gain_rows):
    rows, depth = observations.shape
    modes = gain_rows.shape[1]
    tile = 256
    tiles = modes // tile
    piece = jax.ShapeDtypeStruct((tiles, rows, tile // 2), jnp.float32)
    return pl.pallas_call(
        matmul_kernel,
        grid=(tiles,),
        in_specs=[
            pl.BlockSpec(memory_space=pltpu.SMEM),
            pl.BlockSpec((rows, depth), lambda j: (0, 0)),
            pl.BlockSpec((rows, listed.shape[1]), lambda j: (0, 0)),
            pl.BlockSpec((depth, tile), lambda j: (0, j)),
        ],
        out_specs=[
            pl.BlockSpec((1, rows, tile // 2), lambda j: (j, 0, 0)),
            pl.BlockSpec((1, rows, tile // 2), lambda j: (j, 0, 0)),
        ],
        out_shape=[piece, piece],
        scratch_shapes=[pltpu.VMEM((rows, depth), jnp.bfloat16)],
        compiler_params=pltpu.CompilerParams(dimension_semantics=("arbitrary",)),
        cost_estimate=pl.CostEstimate(
            flops=2 * rows * depth * modes,
            bytes_accessed=2 * rows * depth + 2 * depth * modes + 4 * rows * modes,
            transcendentals=0,
        ),
    )(core, observations, listed, gain_rows)


def chip_sum_kernel(keep_ref, recv_ref, *out_refs):
    chips = keep_ref.shape[0]
    chip = lax.axis_index("sensor") // 2
    for shift, out_ref in enumerate(out_refs):
        index = (chip + shift) % chips
        out_ref[...] = keep_ref[index] + recv_ref[index]


def chip_sum(keep, recv):
    chips, rows, cols = keep.shape
    shape = jax.ShapeDtypeStruct((rows, cols), jnp.float32)
    return pl.pallas_call(
        chip_sum_kernel,
        out_shape=[shape] * chips,
        cost_estimate=pl.CostEstimate(flops=chips * rows * cols, bytes_accessed=12 * chips * rows * cols, transcendentals=0),
    )(keep, recv)


def sensor_reduce_scatter(keep, send):
    count = lax.axis_size("sensor")
    chips = count // 2
    summed = chip_sum(keep, lax.ppermute(send, "sensor", [(i, i ^ 1) for i in range(count)]))
    parts = [summed[0]]
    for shift in range(1, chips):
        perm = [(i, (((i // 2) + shift) % chips) * 2 + i % 2) for i in range(count)]
        parts.append(lax.ppermute(summed[shift], "sensor", perm))
    return parts


def gather_tm(copies):
    return lax.all_to_all(copies, "tm", 0, 0, tiled=True)


def per_device(observations, obs_list, gain_rows, decay, smooth_gain, model_rate, first_state):
    sensor_count = lax.axis_size("sensor")
    sensor_index = lax.axis_index("sensor")
    time_index = lax.axis_index("tm")
    time_count = lax.axis_size("tm")
    rows_here = observations.shape[0]
    block_count = observations.shape[1] // 128
    own_blocks = sensor_index * block_count + jnp.arange(block_count, dtype=jnp.int32)
    listed = jnp.any(obs_list[:, :, None] == own_blocks[None, None, :], axis=1).astype(jnp.float32)
    core = (sensor_index % 2).astype(jnp.int32)[None]
    keep, send = listed_matmul(core, observations, listed, gain_rows)
    width = gain_rows.shape[1] // sensor_count
    parts = sensor_reduce_scatter(keep, send)
    start_col = sensor_index * width
    factors = lax.dynamic_slice_in_dim(decay, start_col, width, 1)
    gains = lax.dynamic_slice_in_dim(smooth_gain, start_col, width, 1)
    rates = lax.dynamic_slice_in_dim(model_rate, start_col, width, 0)
    initial = lax.dynamic_slice_in_dim(first_state, start_col, width, 0)
    hour_ids = time_index * rows_here + jnp.arange(rows_here, dtype=jnp.int32)
    total_hours = rows_here * time_count
    step_gain = jnp.where((hour_ids == total_hours - 1)[:, None], jnp.float32(0.0), gains)
    scale = step_gain * rates[None, :]

    prod_fwd, local_fwd, prod_back, back_local, back_prod, summary = local_scans(
        factors, parts, step_gain, scale, time_count
    )
    every = gather_tm(summary)
    filtered, smoothed = combine(
        every, initial[None, :], prod_fwd, local_fwd, prod_back, back_local, back_prod
    )
    return (filtered, smoothed)


def solution(mesh):
    in_specs = (
        P("tm", "sensor"),
        P("tm", "sensor"),
        P("sensor", None),
        P("tm", None),
        P("tm", None),
        P(),
        P(),
    )
    out_specs = (P("tm", "sensor"), P("tm", "sensor"))
    return jax.shard_map(
        per_device, mesh=mesh, in_specs=in_specs, out_specs=out_specs, check_vma=False
    )
```

```python
import jax
import jax.numpy as jnp
from jax import lax
from jax.experimental import pallas as pl
from jax.experimental.pallas import tpu as pltpu
from jax.sharding import PartitionSpec as P


SUB = 8


def _chunk_scan(a, x, rows, reverse):
    sub = lax.broadcasted_iota(jnp.int32, a.shape, 0) % SUB
    for k in (1, 2, 4):
        shift = rows - k if reverse else k
        prev_a = pltpu.roll(a, shift, 0)
        prev_x = [pltpu.roll(v, shift, 0) for v in x]
        inside = sub < SUB - k if reverse else sub >= k
        x = [jnp.where(inside, a * p + v, v) for p, v in zip(prev_x, x)]
        a = jnp.where(inside, a * prev_a, a)
    return a, x


def _carry(a, x, out_a, out_x, rows, reverse):
    chunks = rows // SUB
    order = range(chunks - 1, -1, -1) if reverse else range(chunks)
    edge = 0 if reverse else SUB - 1
    carry_a = None
    for i in order:
        ca = a[i * SUB:(i + 1) * SUB]
        cx = [v[i * SUB:(i + 1) * SUB] for v in x]
        if carry_a is not None:
            cx = [c * px + v for c, px, v in zip([ca] * len(cx), carry_x, cx)]
            ca = ca * carry_a
        if out_a is not None:
            out_a[i * SUB:(i + 1) * SUB, :] = ca
        for o, v in zip(out_x, cx):
            o[i * SUB:(i + 1) * SUB, :] = v
        carry_a = jnp.broadcast_to(ca[edge:edge + 1], ca.shape)
        carry_x = [jnp.broadcast_to(v[edge:edge + 1], v.shape) for v in cx]


def scan_kernel(a_ref, own_ref, r1_ref, r2_ref, r3_ref, g_ref, s_ref, pf_ref, lf_ref, pb_ref, bl_ref,
                bp_ref, sum_ref):
    rows = a_ref.shape[0]
    inflow = ((own_ref[...] + r1_ref[...]) + r2_ref[...]) + r3_ref[...]
    a, (u,) = _chunk_scan(a_ref[...], [inflow], rows, False)
    _carry(a, [u], pf_ref, [lf_ref], rows, False)
    scale = s_ref[...]
    lf = lf_ref[...]
    pf = pf_ref[...]
    g, (ol, op) = _chunk_scan(g_ref[...], [lf - scale * lf, pf - scale * pf], rows, True)
    _carry(g, [ol, op], pb_ref, [bl_ref, bp_ref], rows, True)
    sub = lax.broadcasted_iota(jnp.int32, (SUB, pf_ref.shape[1]), 0)
    tile = jnp.zeros((SUB, pf_ref.shape[1]), jnp.float32)
    for row, value in enumerate(
        [pf_ref[rows - 1:rows, :], lf_ref[rows - 1:rows, :], pb_ref[0:1, :], bl_ref[0:1, :], bp_ref[0:1, :]]
    ):
        tile = jnp.where(sub == row, jnp.broadcast_to(value, tile.shape), tile)
    for k in range(sum_ref.shape[0]):
        sum_ref[k] = tile


def local_scans(factors, parts, step_gain, scale, blocks):
    shape = jax.ShapeDtypeStruct(factors.shape, jnp.float32)
    rows, cols = factors.shape
    return pl.pallas_call(
        scan_kernel,
        out_shape=[shape] * 5 + [jax.ShapeDtypeStruct((blocks, SUB, cols), jnp.float32)],
        cost_estimate=pl.CostEstimate(flops=40 * rows * cols, bytes_accessed=48 * rows * cols, transcendentals=0),
    )(factors, *parts, step_gain, scale)


def combine_kernel(every_ref, init_ref, pf_ref, lf_ref, pb_ref, bl_ref, bp_ref, f_ref, s_ref):
    count = every_ref.shape[0]
    place = lax.axis_index("tm")
    entering = [init_ref[...]]
    for k in range(count - 1):
        tile = every_ref[k]
        entering.append(tile[0:1] * entering[-1] + tile[1:2])
    after = jnp.zeros_like(entering[0])
    e_here = jnp.where(place == count - 1, entering[count - 1], 0.0)
    y_here = jnp.zeros_like(after)
    for k in range(count - 1, 0, -1):
        tile = every_ref[k]
        after = tile[3:4] + tile[4:5] * entering[k] + tile[2:3] * after
        e_here = jnp.where(place == k - 1, entering[k - 1], e_here)
        y_here = jnp.where(place == k - 1, after, y_here)
    f_ref[...] = lf_ref[...] + pf_ref[...] * e_here
    s_ref[...] = bl_ref[...] + bp_ref[...] * e_here + pb_ref[...] * y_here


def combine(every, initial, pf, lf, pb, bl, bp):
    rows, cols = pf.shape
    shape = jax.ShapeDtypeStruct(pf.shape, jnp.float32)
    return pl.pallas_call(
        combine_kernel,
        out_shape=[shape, shape],
        cost_estimate=pl.CostEstimate(flops=5 * rows * cols, bytes_accessed=28 * rows * cols, transcendentals=0),
    )(every, initial, pf, lf, pb, bl, bp)


def matmul_kernel(ids_ref, slots_ref, obs_ref, gain_ref, keep_ref, send_ref, lhs_ref):
    blocks = obs_ref.shape[1] // 128

    @pl.when(pl.program_id(0) == 0)
    def _():
        slots = slots_ref[...]
        shape = (128, slots.shape[1])
        block_of = lax.broadcasted_iota(jnp.int32, shape, 0)
        wanted = jnp.where(block_of < blocks, ids_ref[1] + block_of, -2)
        listed_t = jnp.zeros(shape, jnp.float32)
        for s in range(slots.shape[0]):
            listed_t = jnp.maximum(listed_t, (slots[s:s + 1, :] == wanted).astype(jnp.float32))
        listed = listed_t.T
        for b in range(blocks):
            cols = pl.ds(128 * b, 128)
            block = obs_ref[:, cols]
            lhs_ref[:, cols] = jnp.where(listed[:, b:b + 1] > 0, block, jnp.zeros_like(block))

    prod = jnp.dot(lhs_ref[...], gain_ref[...], preferred_element_type=jnp.float32)
    half = prod.shape[1] // 2
    even = ids_ref[0] == 0
    keep_ref[0] = jnp.where(even, prod[:, :half], prod[:, half:])
    send_ref[0] = jnp.where(even, prod[:, half:], prod[:, :half])


def listed_matmul(ids, slots, observations, gain_rows):
    rows, depth = observations.shape
    modes = gain_rows.shape[1]
    tile = 256
    tiles = modes // tile
    piece = jax.ShapeDtypeStruct((tiles, rows, tile // 2), jnp.float32)
    return pl.pallas_call(
        matmul_kernel,
        grid=(tiles,),
        in_specs=[
            pl.BlockSpec(memory_space=pltpu.SMEM),
            pl.BlockSpec(slots.shape, lambda j: (0, 0)),
            pl.BlockSpec((rows, depth), lambda j: (0, 0)),
            pl.BlockSpec((depth, tile), lambda j: (0, j)),
        ],
        out_specs=[
            pl.BlockSpec((1, rows, tile // 2), lambda j: (j, 0, 0)),
            pl.BlockSpec((1, rows, tile // 2), lambda j: (j, 0, 0)),
        ],
        out_shape=[piece, piece],
        scratch_shapes=[pltpu.VMEM((rows, depth), jnp.bfloat16)],
        compiler_params=pltpu.CompilerParams(dimension_semantics=("arbitrary",)),
        cost_estimate=pl.CostEstimate(
            flops=2 * rows * depth * modes,
            bytes_accessed=2 * rows * depth + 2 * depth * modes + 4 * rows * modes,
            transcendentals=0,
        ),
    )(ids, slots, observations, gain_rows)


def sensor_reduce_scatter(keep, send):
    count = lax.axis_size("sensor")
    chips = count // 2
    j = lax.axis_index("sensor")
    chip = j // 2
    chip_sum = keep + lax.ppermute(send, "sensor", [(i, i ^ 1) for i in range(count)])
    parts = [lax.dynamic_index_in_dim(chip_sum, chip, 0, False)]
    for shift in range(1, chips):
        part = lax.dynamic_index_in_dim(chip_sum, (chip + shift) % chips, 0, False)
        perm = [(i, (((i // 2) + shift) % chips) * 2 + i % 2) for i in range(count)]
        parts.append(lax.ppermute(part, "sensor", perm))
    return parts


def gather_tm(copies):
    return lax.all_to_all(copies, "tm", 0, 0, tiled=True)


def per_device(observations, obs_list, gain_rows, decay, smooth_gain, model_rate, first_state):
    sensor_count = lax.axis_size("sensor")
    sensor_index = lax.axis_index("sensor")
    time_index = lax.axis_index("tm")
    time_count = lax.axis_size("tm")
    rows_here = observations.shape[0]
    block_count = observations.shape[1] // 128
    ids = jnp.stack([sensor_index % 2, sensor_index * block_count]).astype(jnp.int32)
    keep, send = listed_matmul(ids, obs_list.T, observations, gain_rows)
    width = gain_rows.shape[1] // sensor_count
    parts = sensor_reduce_scatter(keep, send)
    start_col = sensor_index * width
    factors = lax.dynamic_slice_in_dim(decay, start_col, width, 1)
    gains = lax.dynamic_slice_in_dim(smooth_gain, start_col, width, 1)
    rates = lax.dynamic_slice_in_dim(model_rate, start_col, width, 0)
    initial = lax.dynamic_slice_in_dim(first_state, start_col, width, 0)
    hour_ids = time_index * rows_here + jnp.arange(rows_here, dtype=jnp.int32)
    total_hours = rows_here * time_count
    step_gain = jnp.where((hour_ids == total_hours - 1)[:, None], jnp.float32(0.0), gains)
    scale = step_gain * rates[None, :]

    prod_fwd, local_fwd, prod_back, back_local, back_prod, summary = local_scans(
        factors, parts, step_gain, scale, time_count
    )
    every = gather_tm(summary)
    filtered, smoothed = combine(
        every, initial[None, :], prod_fwd, local_fwd, prod_back, back_local, back_prod
    )
    return (filtered, smoothed)


def solution(mesh):
    in_specs = (
        P("tm", "sensor"),
        P("tm", "sensor"),
        P("sensor", None),
        P("tm", None),
        P("tm", None),
        P(),
        P(),
    )
    out_specs = (P("tm", "sensor"), P("tm", "sensor"))
    return jax.shard_map(
        per_device, mesh=mesh, in_specs=in_specs, out_specs=out_specs, check_vma=False
    )
```

```python
import jax
import jax.numpy as jnp
from jax import lax
from jax.experimental import pallas as pl
from jax.experimental.pallas import tpu as pltpu
from jax.sharding import PartitionSpec as P


SUB = 8


def _chunk_scan(a, x, rows, reverse):
    sub = lax.broadcasted_iota(jnp.int32, a.shape, 0) % SUB
    for k in (1, 2, 4):
        shift = rows - k if reverse else k
        prev_a = pltpu.roll(a, shift, 0)
        prev_x = [pltpu.roll(v, shift, 0) for v in x]
        inside = sub < SUB - k if reverse else sub >= k
        x = [jnp.where(inside, a * p + v, v) for p, v in zip(prev_x, x)]
        a = jnp.where(inside, a * prev_a, a)
    return a, x


def _carry(a, x, out_a, out_x, rows, reverse):
    chunks = rows // SUB
    order = range(chunks - 1, -1, -1) if reverse else range(chunks)
    edge = 0 if reverse else SUB - 1
    carry_a = None
    for i in order:
        ca = a[i * SUB:(i + 1) * SUB]
        cx = [v[i * SUB:(i + 1) * SUB] for v in x]
        if carry_a is not None:
            cx = [c * px + v for c, px, v in zip([ca] * len(cx), carry_x, cx)]
            ca = ca * carry_a
        if out_a is not None:
            out_a[i * SUB:(i + 1) * SUB, :] = ca
        for o, v in zip(out_x, cx):
            o[i * SUB:(i + 1) * SUB, :] = v
        carry_a = jnp.broadcast_to(ca[edge:edge + 1], ca.shape)
        carry_x = [jnp.broadcast_to(v[edge:edge + 1], v.shape) for v in cx]


def scan_kernel(a_ref, own_ref, r1_ref, r2_ref, r3_ref, g_ref, s_ref, pf_ref, lf_ref, pb_ref, bl_ref,
                bp_ref, sum_ref):
    rows = a_ref.shape[0]
    inflow = ((own_ref[...] + r1_ref[...]) + r2_ref[...]) + r3_ref[...]
    a, (u,) = _chunk_scan(a_ref[...], [inflow], rows, False)
    _carry(a, [u], pf_ref, [lf_ref], rows, False)
    scale = s_ref[...]
    lf = lf_ref[...]
    pf = pf_ref[...]
    g, (ol, op) = _chunk_scan(g_ref[...], [lf - scale * lf, pf - scale * pf], rows, True)
    _carry(g, [ol, op], pb_ref, [bl_ref, bp_ref], rows, True)
    sub = lax.broadcasted_iota(jnp.int32, (SUB, pf_ref.shape[1]), 0)
    tile = jnp.zeros((SUB, pf_ref.shape[1]), jnp.float32)
    for row, value in enumerate(
        [pf_ref[rows - 1:rows, :], lf_ref[rows - 1:rows, :], pb_ref[0:1, :], bl_ref[0:1, :], bp_ref[0:1, :]]
    ):
        tile = jnp.where(sub == row, jnp.broadcast_to(value, tile.shape), tile)
    for k in range(sum_ref.shape[0]):
        sum_ref[k] = tile


def local_scans(factors, parts, step_gain, scale, blocks):
    shape = jax.ShapeDtypeStruct(factors.shape, jnp.float32)
    rows, cols = factors.shape
    return pl.pallas_call(
        scan_kernel,
        out_shape=[shape] * 5 + [jax.ShapeDtypeStruct((blocks, SUB, cols), jnp.float32)],
        cost_estimate=pl.CostEstimate(flops=40 * rows * cols, bytes_accessed=48 * rows * cols, transcendentals=0),
    )(factors, *parts, step_gain, scale)


def combine_kernel(every_ref, init_ref, pf_ref, lf_ref, pb_ref, bl_ref, bp_ref, f_ref, s_ref):
    count = every_ref.shape[0]
    place = lax.axis_index("tm")
    entering = [init_ref[...]]
    for k in range(count - 1):
        tile = every_ref[k]
        entering.append(tile[0:1] * entering[-1] + tile[1:2])
    after = jnp.zeros_like(entering[0])
    e_here = jnp.where(place == count - 1, entering[count - 1], 0.0)
    y_here = jnp.zeros_like(after)
    for k in range(count - 1, 0, -1):
        tile = every_ref[k]
        after = tile[3:4] + tile[4:5] * entering[k] + tile[2:3] * after
        e_here = jnp.where(place == k - 1, entering[k - 1], e_here)
        y_here = jnp.where(place == k - 1, after, y_here)
    f_ref[...] = lf_ref[...] + pf_ref[...] * e_here
    s_ref[...] = bl_ref[...] + bp_ref[...] * e_here + pb_ref[...] * y_here


def combine(every, initial, pf, lf, pb, bl, bp):
    rows, cols = pf.shape
    shape = jax.ShapeDtypeStruct(pf.shape, jnp.float32)
    return pl.pallas_call(
        combine_kernel,
        out_shape=[shape, shape],
        cost_estimate=pl.CostEstimate(flops=5 * rows * cols, bytes_accessed=28 * rows * cols, transcendentals=0),
    )(every, initial, pf, lf, pb, bl, bp)


def matmul_kernel(slots_ref, obs_ref, gain_ref, keep_ref, send_ref, lhs_ref):
    blocks = obs_ref.shape[1] // 128
    sensor = lax.axis_index("sensor")

    @pl.when(pl.program_id(0) == 0)
    def _():
        slots = slots_ref[...]
        shape = (128, slots.shape[1])
        block_of = lax.broadcasted_iota(jnp.int32, shape, 0)
        wanted = jnp.where(block_of < blocks, sensor * blocks + block_of, -2)
        listed_t = jnp.zeros(shape, jnp.float32)
        for s in range(slots.shape[0]):
            listed_t = jnp.maximum(listed_t, (slots[s:s + 1, :] == wanted).astype(jnp.float32))
        listed = listed_t.T
        for b in range(blocks):
            cols = pl.ds(128 * b, 128)
            block = obs_ref[:, cols]
            lhs_ref[:, cols] = jnp.where(listed[:, b:b + 1] > 0, block, jnp.zeros_like(block))

    prod = jnp.dot(lhs_ref[...], gain_ref[...], preferred_element_type=jnp.float32)
    half = prod.shape[1] // 2
    even = sensor % 2 == 0
    keep_ref[0] = jnp.where(even, prod[:, :half], prod[:, half:])
    send_ref[0] = jnp.where(even, prod[:, half:], prod[:, :half])


def listed_matmul(slots, observations, gain_rows):
    rows, depth = observations.shape
    modes = gain_rows.shape[1]
    tile = 256
    tiles = modes // tile
    piece = jax.ShapeDtypeStruct((tiles, rows, tile // 2), jnp.float32)
    return pl.pallas_call(
        matmul_kernel,
        grid=(tiles,),
        in_specs=[
            pl.BlockSpec(slots.shape, lambda j: (0, 0)),
            pl.BlockSpec((rows, depth), lambda j: (0, 0)),
            pl.BlockSpec((depth, tile), lambda j: (0, j)),
        ],
        out_specs=[
            pl.BlockSpec((1, rows, tile // 2), lambda j: (j, 0, 0)),
            pl.BlockSpec((1, rows, tile // 2), lambda j: (j, 0, 0)),
        ],
        out_shape=[piece, piece],
        scratch_shapes=[pltpu.VMEM((rows, depth), jnp.bfloat16)],
        compiler_params=pltpu.CompilerParams(dimension_semantics=("arbitrary",)),
        cost_estimate=pl.CostEstimate(
            flops=2 * rows * depth * modes,
            bytes_accessed=2 * rows * depth + 2 * depth * modes + 4 * rows * modes,
            transcendentals=0,
        ),
    )(slots, observations, gain_rows)


def sensor_reduce_scatter(keep, send):
    count = lax.axis_size("sensor")
    chips = count // 2
    j = lax.axis_index("sensor")
    chip = j // 2
    chip_sum = keep + lax.ppermute(send, "sensor", [(i, i ^ 1) for i in range(count)])
    parts = [lax.dynamic_index_in_dim(chip_sum, chip, 0, False)]
    for shift in range(1, chips):
        part = lax.dynamic_index_in_dim(chip_sum, (chip + shift) % chips, 0, False)
        perm = [(i, (((i // 2) + shift) % chips) * 2 + i % 2) for i in range(count)]
        parts.append(lax.ppermute(part, "sensor", perm))
    return parts


def gather_tm(copies):
    return lax.all_to_all(copies, "tm", 0, 0, tiled=True)


def per_device(observations, obs_list, gain_rows, decay, smooth_gain, model_rate, first_state):
    sensor_count = lax.axis_size("sensor")
    sensor_index = lax.axis_index("sensor")
    time_index = lax.axis_index("tm")
    time_count = lax.axis_size("tm")
    rows_here = observations.shape[0]
    keep, send = listed_matmul(obs_list.T, observations, gain_rows)
    width = gain_rows.shape[1] // sensor_count
    parts = sensor_reduce_scatter(keep, send)
    start_col = sensor_index * width
    factors = lax.dynamic_slice_in_dim(decay, start_col, width, 1)
    gains = lax.dynamic_slice_in_dim(smooth_gain, start_col, width, 1)
    rates = lax.dynamic_slice_in_dim(model_rate, start_col, width, 0)
    initial = lax.dynamic_slice_in_dim(first_state, start_col, width, 0)
    hour_ids = time_index * rows_here + jnp.arange(rows_here, dtype=jnp.int32)
    total_hours = rows_here * time_count
    step_gain = jnp.where((hour_ids == total_hours - 1)[:, None], jnp.float32(0.0), gains)
    scale = step_gain * rates[None, :]

    prod_fwd, local_fwd, prod_back, back_local, back_prod, summary = local_scans(
        factors, parts, step_gain, scale, time_count
    )
    every = gather_tm(summary)
    filtered, smoothed = combine(
        every, initial[None, :], prod_fwd, local_fwd, prod_back, back_local, back_prod
    )
    return (filtered, smoothed)


def solution(mesh):
    in_specs = (
        P("tm", "sensor"),
        P("tm", "sensor"),
        P("sensor", None),
        P("tm", None),
        P("tm", None),
        P(),
        P(),
    )
    out_specs = (P("tm", "sensor"), P("tm", "sensor"))
    return jax.shard_map(
        per_device, mesh=mesh, in_specs=in_specs, out_specs=out_specs, check_vma=False
    )
```

```python
import jax
import jax.numpy as jnp
from jax import lax
from jax.experimental import pallas as pl
from jax.experimental.pallas import tpu as pltpu
from jax.sharding import PartitionSpec as P


SUB = 8


def _chunk_scan(a, x, rows, reverse):
    sub = lax.broadcasted_iota(jnp.int32, a.shape, 0) % SUB
    for k in (1, 2, 4):
        shift = rows - k if reverse else k
        prev_a = pltpu.roll(a, shift, 0)
        prev_x = [pltpu.roll(v, shift, 0) for v in x]
        inside = sub < SUB - k if reverse else sub >= k
        x = [jnp.where(inside, a * p + v, v) for p, v in zip(prev_x, x)]
        a = jnp.where(inside, a * prev_a, a)
    return a, x


def _carry(a, x, out_a, out_x, rows, reverse):
    chunks = rows // SUB
    order = range(chunks - 1, -1, -1) if reverse else range(chunks)
    edge = 0 if reverse else SUB - 1
    carry_a = None
    for i in order:
        ca = a[i * SUB:(i + 1) * SUB]
        cx = [v[i * SUB:(i + 1) * SUB] for v in x]
        if carry_a is not None:
            cx = [c * px + v for c, px, v in zip([ca] * len(cx), carry_x, cx)]
            ca = ca * carry_a
        if out_a is not None:
            out_a[i * SUB:(i + 1) * SUB, :] = ca
        for o, v in zip(out_x, cx):
            o[i * SUB:(i + 1) * SUB, :] = v
        carry_a = jnp.broadcast_to(ca[edge:edge + 1], ca.shape)
        carry_x = [jnp.broadcast_to(v[edge:edge + 1], v.shape) for v in cx]


def scan_kernel(a_ref, own_ref, r1_ref, r2_ref, r3_ref, g_ref, s_ref, pf_ref, lf_ref, pb_ref, bl_ref,
                bp_ref, sum_ref):
    rows = a_ref.shape[0]
    inflow = ((own_ref[...] + r1_ref[...]) + r2_ref[...]) + r3_ref[...]
    a, (u,) = _chunk_scan(a_ref[...], [inflow], rows, False)
    _carry(a, [u], pf_ref, [lf_ref], rows, False)
    scale = s_ref[...]
    lf = lf_ref[...]
    pf = pf_ref[...]
    g, (ol, op) = _chunk_scan(g_ref[...], [lf - scale * lf, pf - scale * pf], rows, True)
    _carry(g, [ol, op], pb_ref, [bl_ref, bp_ref], rows, True)
    sub = lax.broadcasted_iota(jnp.int32, (SUB, pf_ref.shape[1]), 0)
    tile = jnp.zeros((SUB, pf_ref.shape[1]), jnp.float32)
    for row, value in enumerate(
        [pf_ref[rows - 1:rows, :], lf_ref[rows - 1:rows, :], pb_ref[0:1, :], bl_ref[0:1, :], bp_ref[0:1, :]]
    ):
        tile = jnp.where(sub == row, jnp.broadcast_to(value, tile.shape), tile)
    for k in range(sum_ref.shape[0]):
        sum_ref[k] = tile


def local_scans(factors, parts, step_gain, scale, blocks):
    shape = jax.ShapeDtypeStruct(factors.shape, jnp.float32)
    rows, cols = factors.shape
    return pl.pallas_call(
        scan_kernel,
        out_shape=[shape] * 5 + [jax.ShapeDtypeStruct((blocks, SUB, cols), jnp.float32)],
        cost_estimate=pl.CostEstimate(flops=40 * rows * cols, bytes_accessed=48 * rows * cols, transcendentals=0),
    )(factors, *parts, step_gain, scale)


def combine_kernel(every_ref, init_ref, pf_ref, lf_ref, pb_ref, bl_ref, bp_ref, f_ref, s_ref):
    count = every_ref.shape[0]
    place = lax.axis_index("tm")
    entering = [init_ref[...]]
    for k in range(count - 1):
        tile = every_ref[k]
        entering.append(tile[0:1] * entering[-1] + tile[1:2])
    after = jnp.zeros_like(entering[0])
    e_here = jnp.where(place == count - 1, entering[count - 1], 0.0)
    y_here = jnp.zeros_like(after)
    for k in range(count - 1, 0, -1):
        tile = every_ref[k]
        after = tile[3:4] + tile[4:5] * entering[k] + tile[2:3] * after
        e_here = jnp.where(place == k - 1, entering[k - 1], e_here)
        y_here = jnp.where(place == k - 1, after, y_here)
    f_ref[...] = lf_ref[...] + pf_ref[...] * e_here
    s_ref[...] = bl_ref[...] + bp_ref[...] * e_here + pb_ref[...] * y_here


def combine(every, initial, pf, lf, pb, bl, bp):
    rows, cols = pf.shape
    shape = jax.ShapeDtypeStruct(pf.shape, jnp.float32)
    return pl.pallas_call(
        combine_kernel,
        out_shape=[shape, shape],
        cost_estimate=pl.CostEstimate(flops=5 * rows * cols, bytes_accessed=28 * rows * cols, transcendentals=0),
    )(every, initial, pf, lf, pb, bl, bp)


def matmul_kernel(slots_ref, obs_ref, gain_ref, keep_ref, send_ref, lhs_ref):
    blocks = obs_ref.shape[1] // 128
    sensor = lax.axis_index("sensor")

    @pl.when(pl.program_id(0) == 0)
    def _():
        slots = slots_ref[...]
        shape = (128, slots.shape[1])
        block_of = lax.broadcasted_iota(jnp.int32, shape, 0)
        wanted = jnp.where(block_of < blocks, sensor * blocks + block_of, -2)
        listed_t = jnp.zeros(shape, jnp.float32)
        for s in range(slots.shape[0]):
            listed_t = jnp.maximum(listed_t, (slots[s:s + 1, :] == wanted).astype(jnp.float32))
        listed = listed_t.T
        for b in range(blocks):
            cols = pl.ds(128 * b, 128)
            block = obs_ref[:, cols]
            lhs_ref[:, cols] = jnp.where(listed[:, b:b + 1] > 0, block, jnp.zeros_like(block))

    prod = jnp.dot(lhs_ref[...], gain_ref[...], preferred_element_type=jnp.float32)
    half = prod.shape[1] // 2
    even = sensor % 2 == 0
    keep_ref[0] = jnp.where(even, prod[:, :half], prod[:, half:])
    send_ref[0] = jnp.where(even, prod[:, half:], prod[:, :half])


def listed_matmul(slots, observations, gain_rows):
    rows, depth = observations.shape
    modes = gain_rows.shape[1]
    tile = 256
    tiles = modes // tile
    piece = jax.ShapeDtypeStruct((tiles, rows, tile // 2), jnp.float32)
    return pl.pallas_call(
        matmul_kernel,
        grid=(tiles,),
        in_specs=[
            pl.BlockSpec(slots.shape, lambda j: (0, 0)),
            pl.BlockSpec((rows, depth), lambda j: (0, 0)),
            pl.BlockSpec((depth, tile), lambda j: (0, j)),
        ],
        out_specs=[
            pl.BlockSpec((1, rows, tile // 2), lambda j: (j, 0, 0)),
            pl.BlockSpec((1, rows, tile // 2), lambda j: (j, 0, 0)),
        ],
        out_shape=[piece, piece],
        scratch_shapes=[pltpu.VMEM((rows, depth), jnp.bfloat16)],
        compiler_params=pltpu.CompilerParams(dimension_semantics=("arbitrary",)),
        cost_estimate=pl.CostEstimate(
            flops=2 * rows * depth * modes,
            bytes_accessed=2 * rows * depth + 2 * depth * modes + 4 * rows * modes,
            transcendentals=0,
        ),
    )(slots, observations, gain_rows)


def sensor_reduce_scatter(keep, send):
    count = lax.axis_size("sensor")
    chips = count // 2
    j = lax.axis_index("sensor")
    chip = j // 2
    recv = lax.ppermute(send, "sensor", [(i, i ^ 1) for i in range(count)])

    def chip_sum(index):
        return lax.dynamic_index_in_dim(keep, index, 0, False) + lax.dynamic_index_in_dim(recv, index, 0, False)

    parts = [chip_sum(chip)]
    for shift in range(1, chips):
        part = chip_sum((chip + shift) % chips)
        perm = [(i, (((i // 2) + shift) % chips) * 2 + i % 2) for i in range(count)]
        parts.append(lax.ppermute(part, "sensor", perm))
    return parts


def gather_tm(copies):
    return lax.all_to_all(copies, "tm", 0, 0, tiled=True)


def per_device(observations, obs_list, gain_rows, decay, smooth_gain, model_rate, first_state):
    sensor_count = lax.axis_size("sensor")
    sensor_index = lax.axis_index("sensor")
    time_index = lax.axis_index("tm")
    time_count = lax.axis_size("tm")
    rows_here = observations.shape[0]
    keep, send = listed_matmul(obs_list.T, observations, gain_rows)
    width = gain_rows.shape[1] // sensor_count
    parts = sensor_reduce_scatter(keep, send)
    start_col = sensor_index * width
    factors = lax.dynamic_slice_in_dim(decay, start_col, width, 1)
    gains = lax.dynamic_slice_in_dim(smooth_gain, start_col, width, 1)
    rates = lax.dynamic_slice_in_dim(model_rate, start_col, width, 0)
    initial = lax.dynamic_slice_in_dim(first_state, start_col, width, 0)
    hour_ids = time_index * rows_here + jnp.arange(rows_here, dtype=jnp.int32)
    total_hours = rows_here * time_count
    step_gain = jnp.where((hour_ids == total_hours - 1)[:, None], jnp.float32(0.0), gains)
    scale = step_gain * rates[None, :]

    prod_fwd, local_fwd, prod_back, back_local, back_prod, summary = local_scans(
        factors, parts, step_gain, scale, time_count
    )
    every = gather_tm(summary)
    filtered, smoothed = combine(
        every, initial[None, :], prod_fwd, local_fwd, prod_back, back_local, back_prod
    )
    return (filtered, smoothed)


def solution(mesh):
    in_specs = (
        P("tm", "sensor"),
        P("tm", "sensor"),
        P("sensor", None),
        P("tm", None),
        P("tm", None),
        P(),
        P(),
    )
    out_specs = (P("tm", "sensor"), P("tm", "sensor"))
    return jax.shard_map(
        per_device, mesh=mesh, in_specs=in_specs, out_specs=out_specs, check_vma=False
    )
```

```python
import jax
import jax.numpy as jnp
from jax import lax
from jax.experimental import pallas as pl
from jax.experimental.pallas import tpu as pltpu
from jax.sharding import PartitionSpec as P


SUB = 8


def _chunk_scan(a, x, rows, reverse):
    sub = lax.broadcasted_iota(jnp.int32, a.shape, 0) % SUB
    for k in (1, 2, 4):
        shift = rows - k if reverse else k
        prev_a = pltpu.roll(a, shift, 0)
        prev_x = [pltpu.roll(v, shift, 0) for v in x]
        inside = sub < SUB - k if reverse else sub >= k
        x = [jnp.where(inside, a * p + v, v) for p, v in zip(prev_x, x)]
        a = jnp.where(inside, a * prev_a, a)
    return a, x


def _carry(a, x, out_a, out_x, rows, reverse):
    chunks = rows // SUB
    order = range(chunks - 1, -1, -1) if reverse else range(chunks)
    edge = 0 if reverse else SUB - 1
    carry_a = None
    for i in order:
        ca = a[i * SUB:(i + 1) * SUB]
        cx = [v[i * SUB:(i + 1) * SUB] for v in x]
        if carry_a is not None:
            cx = [c * px + v for c, px, v in zip([ca] * len(cx), carry_x, cx)]
            ca = ca * carry_a
        if out_a is not None:
            out_a[i * SUB:(i + 1) * SUB, :] = ca
        for o, v in zip(out_x, cx):
            o[i * SUB:(i + 1) * SUB, :] = v
        carry_a = jnp.broadcast_to(ca[edge:edge + 1], ca.shape)
        carry_x = [jnp.broadcast_to(v[edge:edge + 1], v.shape) for v in cx]


def _summary_tile(rows_by_slot, cols):
    sub = lax.broadcasted_iota(jnp.int32, (SUB, cols), 0)
    tile = jnp.zeros((SUB, cols), jnp.float32)
    for row, value in rows_by_slot:
        tile = jnp.where(sub == row, jnp.broadcast_to(value, tile.shape), tile)
    return tile


def gain_scan_kernel(a_ref, g_ref, s_ref, pf_ref, pb_ref, bp_ref, part_ref):
    rows, cols = a_ref.shape
    a, _ = _chunk_scan(a_ref[...], [], rows, False)
    _carry(a, [], pf_ref, [], rows, False)
    scale = s_ref[...]
    pf = pf_ref[...]
    g, (op,) = _chunk_scan(g_ref[...], [pf - scale * pf], rows, True)
    _carry(g, [op], pb_ref, [bp_ref], rows, True)
    part_ref[...] = _summary_tile(
        [(0, pf_ref[rows - 1:rows, :]), (2, pb_ref[0:1, :]), (4, bp_ref[0:1, :])], cols
    )


def gain_scans(factors, step_gain, scale):
    shape = jax.ShapeDtypeStruct(factors.shape, jnp.float32)
    rows, cols = factors.shape
    return pl.pallas_call(
        gain_scan_kernel,
        out_shape=[shape] * 3 + [jax.ShapeDtypeStruct((SUB, cols), jnp.float32)],
        cost_estimate=pl.CostEstimate(flops=20 * rows * cols, bytes_accessed=24 * rows * cols, transcendentals=0),
    )(factors, step_gain, scale)


def scan_kernel(a_ref, own_ref, r1_ref, r2_ref, r3_ref, g_ref, s_ref, part_ref, lf_ref, bl_ref, sum_ref):
    rows, cols = a_ref.shape
    inflow = ((own_ref[...] + r1_ref[...]) + r2_ref[...]) + r3_ref[...]
    a, (u,) = _chunk_scan(a_ref[...], [inflow], rows, False)
    _carry(a, [u], None, [lf_ref], rows, False)
    scale = s_ref[...]
    lf = lf_ref[...]
    g, (ol,) = _chunk_scan(g_ref[...], [lf - scale * lf], rows, True)
    _carry(g, [ol], None, [bl_ref], rows, True)
    sub = lax.broadcasted_iota(jnp.int32, (SUB, cols), 0)
    tile = jnp.where(
        sub == 1,
        jnp.broadcast_to(lf_ref[rows - 1:rows, :], (SUB, cols)),
        jnp.where(sub == 3, jnp.broadcast_to(bl_ref[0:1, :], (SUB, cols)), part_ref[...]),
    )
    for k in range(sum_ref.shape[0]):
        sum_ref[k] = tile


def local_scans(factors, parts, step_gain, scale, part, blocks):
    shape = jax.ShapeDtypeStruct(factors.shape, jnp.float32)
    rows, cols = factors.shape
    return pl.pallas_call(
        scan_kernel,
        out_shape=[shape] * 2 + [jax.ShapeDtypeStruct((blocks, SUB, cols), jnp.float32)],
        cost_estimate=pl.CostEstimate(flops=20 * rows * cols, bytes_accessed=40 * rows * cols, transcendentals=0),
    )(factors, *parts, step_gain, scale, part)


def combine_kernel(every_ref, init_ref, pf_ref, lf_ref, pb_ref, bl_ref, bp_ref, f_ref, s_ref):
    count = every_ref.shape[0]
    place = lax.axis_index("tm")
    entering = [init_ref[...]]
    for k in range(count - 1):
        tile = every_ref[k]
        entering.append(tile[0:1] * entering[-1] + tile[1:2])
    after = jnp.zeros_like(entering[0])
    e_here = jnp.where(place == count - 1, entering[count - 1], 0.0)
    y_here = jnp.zeros_like(after)
    for k in range(count - 1, 0, -1):
        tile = every_ref[k]
        after = tile[3:4] + tile[4:5] * entering[k] + tile[2:3] * after
        e_here = jnp.where(place == k - 1, entering[k - 1], e_here)
        y_here = jnp.where(place == k - 1, after, y_here)
    f_ref[...] = lf_ref[...] + pf_ref[...] * e_here
    s_ref[...] = bl_ref[...] + bp_ref[...] * e_here + pb_ref[...] * y_here


def combine(every, initial, pf, lf, pb, bl, bp):
    rows, cols = pf.shape
    shape = jax.ShapeDtypeStruct(pf.shape, jnp.float32)
    return pl.pallas_call(
        combine_kernel,
        out_shape=[shape, shape],
        cost_estimate=pl.CostEstimate(flops=5 * rows * cols, bytes_accessed=28 * rows * cols, transcendentals=0),
    )(every, initial, pf, lf, pb, bl, bp)


def matmul_kernel(slots_ref, obs_ref, gain_ref, keep_ref, send_ref, lhs_ref):
    blocks = obs_ref.shape[1] // 128
    sensor = lax.axis_index("sensor")

    @pl.when(pl.program_id(0) == 0)
    def _():
        slots = slots_ref[...]
        shape = (128, slots.shape[1])
        block_of = lax.broadcasted_iota(jnp.int32, shape, 0)
        wanted = jnp.where(block_of < blocks, sensor * blocks + block_of, -2)
        listed_t = jnp.zeros(shape, jnp.float32)
        for s in range(slots.shape[0]):
            listed_t = jnp.maximum(listed_t, (slots[s:s + 1, :] == wanted).astype(jnp.float32))
        listed = listed_t.T
        for b in range(blocks):
            cols = pl.ds(128 * b, 128)
            block = obs_ref[:, cols]
            lhs_ref[:, cols] = jnp.where(listed[:, b:b + 1] > 0, block, jnp.zeros_like(block))

    prod = jnp.dot(lhs_ref[...], gain_ref[...], preferred_element_type=jnp.float32)
    half = prod.shape[1] // 2
    even = sensor % 2 == 0
    keep_ref[0] = jnp.where(even, prod[:, :half], prod[:, half:])
    send_ref[0] = jnp.where(even, prod[:, half:], prod[:, :half])


def listed_matmul(slots, observations, gain_rows):
    rows, depth = observations.shape
    modes = gain_rows.shape[1]
    tile = 256
    tiles = modes // tile
    piece = jax.ShapeDtypeStruct((tiles, rows, tile // 2), jnp.float32)
    return pl.pallas_call(
        matmul_kernel,
        grid=(tiles,),
        in_specs=[
            pl.BlockSpec(slots.shape, lambda j: (0, 0)),
            pl.BlockSpec((rows, depth), lambda j: (0, 0)),
            pl.BlockSpec((depth, tile), lambda j: (0, j)),
        ],
        out_specs=[
            pl.BlockSpec((1, rows, tile // 2), lambda j: (j, 0, 0)),
            pl.BlockSpec((1, rows, tile // 2), lambda j: (j, 0, 0)),
        ],
        out_shape=[piece, piece],
        scratch_shapes=[pltpu.VMEM((rows, depth), jnp.bfloat16)],
        compiler_params=pltpu.CompilerParams(dimension_semantics=("arbitrary",)),
        cost_estimate=pl.CostEstimate(
            flops=2 * rows * depth * modes,
            bytes_accessed=2 * rows * depth + 2 * depth * modes + 4 * rows * modes,
            transcendentals=0,
        ),
    )(slots, observations, gain_rows)


def sensor_reduce_scatter(keep, send):
    count = lax.axis_size("sensor")
    chips = count // 2
    j = lax.axis_index("sensor")
    chip = j // 2
    chip_sum = keep + lax.ppermute(send, "sensor", [(i, i ^ 1) for i in range(count)])
    parts = [lax.dynamic_index_in_dim(chip_sum, chip, 0, False)]
    for shift in range(1, chips):
        part = lax.dynamic_index_in_dim(chip_sum, (chip + shift) % chips, 0, False)
        perm = [(i, (((i // 2) + shift) % chips) * 2 + i % 2) for i in range(count)]
        parts.append(lax.ppermute(part, "sensor", perm))
    return parts


def gather_tm(copies):
    return lax.all_to_all(copies, "tm", 0, 0, tiled=True)


def per_device(observations, obs_list, gain_rows, decay, smooth_gain, model_rate, first_state):
    sensor_count = lax.axis_size("sensor")
    sensor_index = lax.axis_index("sensor")
    time_index = lax.axis_index("tm")
    time_count = lax.axis_size("tm")
    rows_here = observations.shape[0]
    keep, send = listed_matmul(obs_list.T, observations, gain_rows)
    width = gain_rows.shape[1] // sensor_count
    parts = sensor_reduce_scatter(keep, send)
    start_col = sensor_index * width
    factors = lax.dynamic_slice_in_dim(decay, start_col, width, 1)
    gains = lax.dynamic_slice_in_dim(smooth_gain, start_col, width, 1)
    rates = lax.dynamic_slice_in_dim(model_rate, start_col, width, 0)
    initial = lax.dynamic_slice_in_dim(first_state, start_col, width, 0)
    hour_ids = time_index * rows_here + jnp.arange(rows_here, dtype=jnp.int32)
    total_hours = rows_here * time_count
    step_gain = jnp.where((hour_ids == total_hours - 1)[:, None], jnp.float32(0.0), gains)
    scale = step_gain * rates[None, :]

    prod_fwd, prod_back, back_prod, part = gain_scans(factors, step_gain, scale)
    local_fwd, back_local, summary = local_scans(factors, parts, step_gain, scale, part, time_count)
    every = gather_tm(summary)
    filtered, smoothed = combine(
        every, initial[None, :], prod_fwd, local_fwd, prod_back, back_local, back_prod
    )
    return (filtered, smoothed)


def solution(mesh):
    in_specs = (
        P("tm", "sensor"),
        P("tm", "sensor"),
        P("sensor", None),
        P("tm", None),
        P("tm", None),
        P(),
        P(),
    )
    out_specs = (P("tm", "sensor"), P("tm", "sensor"))
    return jax.shard_map(
        per_device, mesh=mesh, in_specs=in_specs, out_specs=out_specs, check_vma=False
    )
```

```python
import jax
import jax.numpy as jnp
from jax import lax
from jax.experimental import pallas as pl
from jax.experimental.pallas import tpu as pltpu
from jax.sharding import PartitionSpec as P


SUB = 8
CHUNK = 64


def _chunk_scan(a, x, rows, reverse):
    sub = lax.broadcasted_iota(jnp.int32, a.shape, 0) % CHUNK
    for k in (1, 2, 4, 8, 16, 32):
        shift = rows - k if reverse else k
        prev_a = pltpu.roll(a, shift, 0)
        prev_x = [pltpu.roll(v, shift, 0) for v in x]
        inside = sub < CHUNK - k if reverse else sub >= k
        x = [jnp.where(inside, a * p + v, v) for p, v in zip(prev_x, x)]
        a = jnp.where(inside, a * prev_a, a)
    return a, x


def _carry(a, x, out_a, out_x, rows, reverse):
    chunks = rows // CHUNK
    order = range(chunks - 1, -1, -1) if reverse else range(chunks)
    edge = 0 if reverse else CHUNK - 1
    carry_a = None
    for i in order:
        ca = a[i * CHUNK:(i + 1) * CHUNK]
        cx = [v[i * CHUNK:(i + 1) * CHUNK] for v in x]
        if carry_a is not None:
            cx = [c * px + v for c, px, v in zip([ca] * len(cx), carry_x, cx)]
            ca = ca * carry_a
        if out_a is not None:
            out_a[i * CHUNK:(i + 1) * CHUNK, :] = ca
        for o, v in zip(out_x, cx):
            o[i * CHUNK:(i + 1) * CHUNK, :] = v
        carry_a = jnp.broadcast_to(ca[edge:edge + 1], ca.shape)
        carry_x = [jnp.broadcast_to(v[edge:edge + 1], v.shape) for v in cx]


def _summary_tile(rows_by_slot, cols):
    sub = lax.broadcasted_iota(jnp.int32, (SUB, cols), 0)
    tile = jnp.zeros((SUB, cols), jnp.float32)
    for row, value in rows_by_slot:
        tile = jnp.where(sub == row, jnp.broadcast_to(value, tile.shape), tile)
    return tile


def gain_scan_kernel(a_ref, g_ref, s_ref, pf_ref, pb_ref, bp_ref, part_ref):
    rows, cols = a_ref.shape
    a, _ = _chunk_scan(a_ref[...], [], rows, False)
    _carry(a, [], pf_ref, [], rows, False)
    scale = s_ref[...]
    pf = pf_ref[...]
    g, (op,) = _chunk_scan(g_ref[...], [pf - scale * pf], rows, True)
    _carry(g, [op], pb_ref, [bp_ref], rows, True)
    part_ref[...] = _summary_tile(
        [(0, pf_ref[rows - 1:rows, :]), (2, pb_ref[0:1, :]), (4, bp_ref[0:1, :])], cols
    )


def gain_scans(factors, step_gain, scale):
    shape = jax.ShapeDtypeStruct(factors.shape, jnp.float32)
    rows, cols = factors.shape
    return pl.pallas_call(
        gain_scan_kernel,
        out_shape=[shape] * 3 + [jax.ShapeDtypeStruct((SUB, cols), jnp.float32)],
        cost_estimate=pl.CostEstimate(flops=20 * rows * cols, bytes_accessed=24 * rows * cols, transcendentals=0),
    )(factors, step_gain, scale)


def scan_kernel(a_ref, own_ref, r1_ref, r2_ref, r3_ref, g_ref, s_ref, part_ref, lf_ref, bl_ref, sum_ref):
    rows, cols = a_ref.shape
    inflow = ((own_ref[...] + r1_ref[...]) + r2_ref[...]) + r3_ref[...]
    a, (u,) = _chunk_scan(a_ref[...], [inflow], rows, False)
    _carry(a, [u], None, [lf_ref], rows, False)
    scale = s_ref[...]
    lf = lf_ref[...]
    g, (ol,) = _chunk_scan(g_ref[...], [lf - scale * lf], rows, True)
    _carry(g, [ol], None, [bl_ref], rows, True)
    sub = lax.broadcasted_iota(jnp.int32, (SUB, cols), 0)
    tile = jnp.where(
        sub == 1,
        jnp.broadcast_to(lf_ref[rows - 1:rows, :], (SUB, cols)),
        jnp.where(sub == 3, jnp.broadcast_to(bl_ref[0:1, :], (SUB, cols)), part_ref[...]),
    )
    for k in range(sum_ref.shape[0]):
        sum_ref[k] = tile


def local_scans(factors, parts, step_gain, scale, part, blocks):
    shape = jax.ShapeDtypeStruct(factors.shape, jnp.float32)
    rows, cols = factors.shape
    return pl.pallas_call(
        scan_kernel,
        out_shape=[shape] * 2 + [jax.ShapeDtypeStruct((blocks, SUB, cols), jnp.float32)],
        cost_estimate=pl.CostEstimate(flops=20 * rows * cols, bytes_accessed=40 * rows * cols, transcendentals=0),
    )(factors, *parts, step_gain, scale, part)


def combine_kernel(every_ref, init_ref, pf_ref, lf_ref, pb_ref, bl_ref, bp_ref, f_ref, s_ref):
    count = every_ref.shape[0]
    place = lax.axis_index("tm")
    entering = [init_ref[...]]
    for k in range(count - 1):
        tile = every_ref[k]
        entering.append(tile[0:1] * entering[-1] + tile[1:2])
    after = jnp.zeros_like(entering[0])
    e_here = jnp.where(place == count - 1, entering[count - 1], 0.0)
    y_here = jnp.zeros_like(after)
    for k in range(count - 1, 0, -1):
        tile = every_ref[k]
        after = tile[3:4] + tile[4:5] * entering[k] + tile[2:3] * after
        e_here = jnp.where(place == k - 1, entering[k - 1], e_here)
        y_here = jnp.where(place == k - 1, after, y_here)
    f_ref[...] = lf_ref[...] + pf_ref[...] * e_here
    s_ref[...] = bl_ref[...] + bp_ref[...] * e_here + pb_ref[...] * y_here


def combine(every, initial, pf, lf, pb, bl, bp):
    rows, cols = pf.shape
    shape = jax.ShapeDtypeStruct(pf.shape, jnp.float32)
    return pl.pallas_call(
        combine_kernel,
        out_shape=[shape, shape],
        cost_estimate=pl.CostEstimate(flops=5 * rows * cols, bytes_accessed=28 * rows * cols, transcendentals=0),
    )(every, initial, pf, lf, pb, bl, bp)


def matmul_kernel(slots_ref, obs_ref, gain_ref, keep_ref, send_ref, lhs_ref):
    blocks = obs_ref.shape[1] // 128
    sensor = lax.axis_index("sensor")

    @pl.when(pl.program_id(0) == 0)
    def _():
        slots = slots_ref[...]
        shape = (128, slots.shape[1])
        block_of = lax.broadcasted_iota(jnp.int32, shape, 0)
        wanted = jnp.where(block_of < blocks, sensor * blocks + block_of, -2)
        listed_t = jnp.zeros(shape, jnp.float32)
        for s in range(slots.shape[0]):
            listed_t = jnp.maximum(listed_t, (slots[s:s + 1, :] == wanted).astype(jnp.float32))
        listed = listed_t.T
        for b in range(blocks):
            cols = pl.ds(128 * b, 128)
            block = obs_ref[:, cols]
            lhs_ref[:, cols] = jnp.where(listed[:, b:b + 1] > 0, block, jnp.zeros_like(block))

    prod = jnp.dot(lhs_ref[...], gain_ref[...], preferred_element_type=jnp.float32)
    half = prod.shape[1] // 2
    even = sensor % 2 == 0
    keep_ref[0] = jnp.where(even, prod[:, :half], prod[:, half:])
    send_ref[0] = jnp.where(even, prod[:, half:], prod[:, :half])


def listed_matmul(slots, observations, gain_rows):
    rows, depth = observations.shape
    modes = gain_rows.shape[1]
    tile = 256
    tiles = modes // tile
    piece = jax.ShapeDtypeStruct((tiles, rows, tile // 2), jnp.float32)
    return pl.pallas_call(
        matmul_kernel,
        grid=(tiles,),
        in_specs=[
            pl.BlockSpec(slots.shape, lambda j: (0, 0)),
            pl.BlockSpec((rows, depth), lambda j: (0, 0)),
            pl.BlockSpec((depth, tile), lambda j: (0, j)),
        ],
        out_specs=[
            pl.BlockSpec((1, rows, tile // 2), lambda j: (j, 0, 0)),
            pl.BlockSpec((1, rows, tile // 2), lambda j: (j, 0, 0)),
        ],
        out_shape=[piece, piece],
        scratch_shapes=[pltpu.VMEM((rows, depth), jnp.bfloat16)],
        compiler_params=pltpu.CompilerParams(dimension_semantics=("arbitrary",)),
        cost_estimate=pl.CostEstimate(
            flops=2 * rows * depth * modes,
            bytes_accessed=2 * rows * depth + 2 * depth * modes + 4 * rows * modes,
            transcendentals=0,
        ),
    )(slots, observations, gain_rows)


def sensor_reduce_scatter(keep, send):
    count = lax.axis_size("sensor")
    chips = count // 2
    j = lax.axis_index("sensor")
    chip = j // 2
    chip_sum = keep + lax.ppermute(send, "sensor", [(i, i ^ 1) for i in range(count)])
    parts = [lax.dynamic_index_in_dim(chip_sum, chip, 0, False)]
    for shift in range(1, chips):
        part = lax.dynamic_index_in_dim(chip_sum, (chip + shift) % chips, 0, False)
        perm = [(i, (((i // 2) + shift) % chips) * 2 + i % 2) for i in range(count)]
        parts.append(lax.ppermute(part, "sensor", perm))
    return parts


def gather_tm(copies):
    return lax.all_to_all(copies, "tm", 0, 0, tiled=True)


def per_device(observations, obs_list, gain_rows, decay, smooth_gain, model_rate, first_state):
    sensor_count = lax.axis_size("sensor")
    sensor_index = lax.axis_index("sensor")
    time_index = lax.axis_index("tm")
    time_count = lax.axis_size("tm")
    rows_here = observations.shape[0]
    keep, send = listed_matmul(obs_list.T, observations, gain_rows)
    width = gain_rows.shape[1] // sensor_count
    parts = sensor_reduce_scatter(keep, send)
    start_col = sensor_index * width
    factors = lax.dynamic_slice_in_dim(decay, start_col, width, 1)
    gains = lax.dynamic_slice_in_dim(smooth_gain, start_col, width, 1)
    rates = lax.dynamic_slice_in_dim(model_rate, start_col, width, 0)
    initial = lax.dynamic_slice_in_dim(first_state, start_col, width, 0)
    hour_ids = time_index * rows_here + jnp.arange(rows_here, dtype=jnp.int32)
    total_hours = rows_here * time_count
    step_gain = jnp.where((hour_ids == total_hours - 1)[:, None], jnp.float32(0.0), gains)
    scale = step_gain * rates[None, :]

    prod_fwd, prod_back, back_prod, part = gain_scans(factors, step_gain, scale)
    local_fwd, back_local, summary = local_scans(factors, parts, step_gain, scale, part, time_count)
    every = gather_tm(summary)
    filtered, smoothed = combine(
        every, initial[None, :], prod_fwd, local_fwd, prod_back, back_local, back_prod
    )
    return (filtered, smoothed)


def solution(mesh):
    in_specs = (
        P("tm", "sensor"),
        P("tm", "sensor"),
        P("sensor", None),
        P("tm", None),
        P("tm", None),
        P(),
        P(),
    )
    out_specs = (P("tm", "sensor"), P("tm", "sensor"))
    return jax.shard_map(
        per_device, mesh=mesh, in_specs=in_specs, out_specs=out_specs, check_vma=False
    )
```

```python
import jax
import jax.numpy as jnp
from jax import lax
from jax.experimental import pallas as pl
from jax.experimental.pallas import tpu as pltpu
from jax.sharding import PartitionSpec as P


SUB = 8
CHUNK = 64


def _chunk_scan(a, x, rows, reverse):
    sub = lax.broadcasted_iota(jnp.int32, a.shape, 0) % CHUNK
    for k in (1, 2, 4, 8, 16, 32):
        shift = rows - k if reverse else k
        prev_a = pltpu.roll(a, shift, 0)
        prev_x = [pltpu.roll(v, shift, 0) for v in x]
        inside = sub < CHUNK - k if reverse else sub >= k
        x = [jnp.where(inside, a * p + v, v) for p, v in zip(prev_x, x)]
        a = jnp.where(inside, a * prev_a, a)
    return a, x


def _carry(a, x, out_a, out_x, rows, reverse):
    chunks = rows // CHUNK
    order = range(chunks - 1, -1, -1) if reverse else range(chunks)
    edge = 0 if reverse else CHUNK - 1
    carry_a = None
    for i in order:
        ca = a[i * CHUNK:(i + 1) * CHUNK]
        cx = [v[i * CHUNK:(i + 1) * CHUNK] for v in x]
        if carry_a is not None:
            cx = [c * px + v for c, px, v in zip([ca] * len(cx), carry_x, cx)]
            ca = ca * carry_a
        if out_a is not None:
            out_a[i * CHUNK:(i + 1) * CHUNK, :] = ca
        for o, v in zip(out_x, cx):
            o[i * CHUNK:(i + 1) * CHUNK, :] = v
        carry_a = jnp.broadcast_to(ca[edge:edge + 1], ca.shape)
        carry_x = [jnp.broadcast_to(v[edge:edge + 1], v.shape) for v in cx]


def _summary_tile(rows_by_slot, cols):
    sub = lax.broadcasted_iota(jnp.int32, (SUB, cols), 0)
    tile = jnp.zeros((SUB, cols), jnp.float32)
    for row, value in rows_by_slot:
        tile = jnp.where(sub == row, jnp.broadcast_to(value, tile.shape), tile)
    return tile


def gain_scan_kernel(a_ref, g_ref, s_ref, pf_ref, pb_ref, bp_ref, part_ref):
    rows, cols = a_ref.shape
    a, _ = _chunk_scan(a_ref[...], [], rows, False)
    _carry(a, [], pf_ref, [], rows, False)
    scale = s_ref[...]
    pf = pf_ref[...]
    g, (op,) = _chunk_scan(g_ref[...], [pf - scale * pf], rows, True)
    _carry(g, [op], pb_ref, [bp_ref], rows, True)
    part_ref[...] = _summary_tile(
        [(0, pf_ref[rows - 1:rows, :]), (2, pb_ref[0:1, :]), (4, bp_ref[0:1, :])], cols
    )


def gain_scans(factors, step_gain, scale):
    shape = jax.ShapeDtypeStruct(factors.shape, jnp.float32)
    rows, cols = factors.shape
    return pl.pallas_call(
        gain_scan_kernel,
        out_shape=[shape] * 3 + [jax.ShapeDtypeStruct((SUB, cols), jnp.float32)],
        cost_estimate=pl.CostEstimate(flops=20 * rows * cols, bytes_accessed=24 * rows * cols, transcendentals=0),
    )(factors, step_gain, scale)


def scan_kernel(a_ref, own_ref, r1_ref, r2_ref, r3_ref, g_ref, s_ref, part_ref, lf_ref, bl_ref, sum_ref):
    rows, cols = a_ref.shape
    inflow = ((own_ref[...] + r1_ref[...]) + r2_ref[...]) + r3_ref[...]
    a, (u,) = _chunk_scan(a_ref[...], [inflow], rows, False)
    _carry(a, [u], None, [lf_ref], rows, False)
    scale = s_ref[...]
    lf = lf_ref[...]
    g, (ol,) = _chunk_scan(g_ref[...], [lf - scale * lf], rows, True)
    _carry(g, [ol], None, [bl_ref], rows, True)
    sub = lax.broadcasted_iota(jnp.int32, (SUB, cols), 0)
    tile = jnp.where(
        sub == 1,
        jnp.broadcast_to(lf_ref[rows - 1:rows, :], (SUB, cols)),
        jnp.where(sub == 3, jnp.broadcast_to(bl_ref[0:1, :], (SUB, cols)), part_ref[...]),
    )
    for k in range(sum_ref.shape[0]):
        sum_ref[k] = tile


def local_scans(factors, parts, step_gain, scale, part, blocks):
    shape = jax.ShapeDtypeStruct(factors.shape, jnp.float32)
    rows, cols = factors.shape
    return pl.pallas_call(
        scan_kernel,
        out_shape=[shape] * 2 + [jax.ShapeDtypeStruct((blocks, SUB, cols), jnp.float32)],
        cost_estimate=pl.CostEstimate(flops=20 * rows * cols, bytes_accessed=40 * rows * cols, transcendentals=0),
    )(factors, *parts, step_gain, scale, part)


def combine_kernel(every_ref, init_ref, pf_ref, lf_ref, pb_ref, bl_ref, bp_ref, f_ref, s_ref):
    count = every_ref.shape[0]
    place = lax.axis_index("tm")
    entering = [init_ref[...]]
    for k in range(count - 1):
        tile = every_ref[k]
        entering.append(tile[0:1] * entering[-1] + tile[1:2])
    after = jnp.zeros_like(entering[0])
    e_here = jnp.where(place == count - 1, entering[count - 1], 0.0)
    y_here = jnp.zeros_like(after)
    for k in range(count - 1, 0, -1):
        tile = every_ref[k]
        after = tile[3:4] + tile[4:5] * entering[k] + tile[2:3] * after
        e_here = jnp.where(place == k - 1, entering[k - 1], e_here)
        y_here = jnp.where(place == k - 1, after, y_here)
    f_ref[...] = lf_ref[...] + pf_ref[...] * e_here
    s_ref[...] = bl_ref[...] + bp_ref[...] * e_here + pb_ref[...] * y_here


def combine(every, initial, pf, lf, pb, bl, bp):
    rows, cols = pf.shape
    shape = jax.ShapeDtypeStruct(pf.shape, jnp.float32)
    return pl.pallas_call(
        combine_kernel,
        out_shape=[shape, shape],
        cost_estimate=pl.CostEstimate(flops=5 * rows * cols, bytes_accessed=28 * rows * cols, transcendentals=0),
    )(every, initial, pf, lf, pb, bl, bp)


def matmul_kernel(slots_ref, obs_ref, gain_ref, keep_ref, send_ref, mask_ref, acc_ref):
    step = pl.program_id(0)
    per_step = obs_ref.shape[1] // 128
    blocks = mask_ref.shape[0]
    sensor = lax.axis_index("sensor")

    @pl.when(step == 0)
    def _():
        slots = slots_ref[...]
        shape = (128, slots.shape[1])
        block_of = lax.broadcasted_iota(jnp.int32, shape, 0)
        wanted = jnp.where(block_of < blocks, sensor * blocks + block_of, -2)
        listed_t = jnp.zeros(shape, jnp.float32)
        for s in range(slots.shape[0]):
            listed_t = jnp.maximum(listed_t, (slots[s:s + 1, :] == wanted).astype(jnp.float32))
        listed = listed_t.T
        for b in range(blocks):
            mask_ref[b] = jnp.broadcast_to(listed[:, b:b + 1], mask_ref.shape[1:])

    pieces = []
    for b in range(per_step):
        block = obs_ref[:, pl.ds(128 * b, 128)]
        pieces.append(jnp.where(mask_ref[step * per_step + b] > 0, block, jnp.zeros_like(block)))
    prod = jnp.dot(jnp.concatenate(pieces, 1), gain_ref[...], preferred_element_type=jnp.float32)

    @pl.when(step == 0)
    def _():
        acc_ref[...] = prod

    @pl.when(step > 0)
    def _():
        acc_ref[...] += prod

    @pl.when(step == pl.num_programs(0) - 1)
    def _():
        even = sensor % 2 == 0
        for j in range(keep_ref.shape[0]):
            left = acc_ref[:, pl.ds(256 * j, 128)]
            right = acc_ref[:, pl.ds(256 * j + 128, 128)]
            keep_ref[j] = jnp.where(even, left, right)
            send_ref[j] = jnp.where(even, right, left)


def listed_matmul(slots, observations, gain_rows):
    rows, depth = observations.shape
    modes = gain_rows.shape[1]
    slab = 512
    piece = jax.ShapeDtypeStruct((modes // 256, rows, 128), jnp.float32)
    return pl.pallas_call(
        matmul_kernel,
        grid=(depth // slab,),
        in_specs=[
            pl.BlockSpec(slots.shape, lambda k: (0, 0)),
            pl.BlockSpec((rows, slab), lambda k: (0, k)),
            pl.BlockSpec((slab, modes), lambda k: (k, 0)),
        ],
        out_specs=[
            pl.BlockSpec(piece.shape, lambda k: (0, 0, 0)),
            pl.BlockSpec(piece.shape, lambda k: (0, 0, 0)),
        ],
        out_shape=[piece, piece],
        scratch_shapes=[
            pltpu.VMEM((depth // 128, rows, 128), jnp.float32),
            pltpu.VMEM((rows, modes), jnp.float32),
        ],
        compiler_params=pltpu.CompilerParams(dimension_semantics=("arbitrary",)),
        cost_estimate=pl.CostEstimate(
            flops=2 * rows * depth * modes,
            bytes_accessed=2 * rows * depth + 2 * depth * modes + 4 * rows * modes,
            transcendentals=0,
        ),
    )(slots, observations, gain_rows)


def sensor_reduce_scatter(keep, send):
    count = lax.axis_size("sensor")
    chips = count // 2
    j = lax.axis_index("sensor")
    chip = j // 2
    chip_sum = keep + lax.ppermute(send, "sensor", [(i, i ^ 1) for i in range(count)])
    parts = [lax.dynamic_index_in_dim(chip_sum, chip, 0, False)]
    for shift in range(1, chips):
        part = lax.dynamic_index_in_dim(chip_sum, (chip + shift) % chips, 0, False)
        perm = [(i, (((i // 2) + shift) % chips) * 2 + i % 2) for i in range(count)]
        parts.append(lax.ppermute(part, "sensor", perm))
    return parts


def gather_tm(copies):
    return lax.all_to_all(copies, "tm", 0, 0, tiled=True)


def per_device(observations, obs_list, gain_rows, decay, smooth_gain, model_rate, first_state):
    sensor_count = lax.axis_size("sensor")
    sensor_index = lax.axis_index("sensor")
    time_index = lax.axis_index("tm")
    time_count = lax.axis_size("tm")
    rows_here = observations.shape[0]
    keep, send = listed_matmul(obs_list.T, observations, gain_rows)
    width = gain_rows.shape[1] // sensor_count
    parts = sensor_reduce_scatter(keep, send)
    start_col = sensor_index * width
    factors = lax.dynamic_slice_in_dim(decay, start_col, width, 1)
    gains = lax.dynamic_slice_in_dim(smooth_gain, start_col, width, 1)
    rates = lax.dynamic_slice_in_dim(model_rate, start_col, width, 0)
    initial = lax.dynamic_slice_in_dim(first_state, start_col, width, 0)
    hour_ids = time_index * rows_here + jnp.arange(rows_here, dtype=jnp.int32)
    total_hours = rows_here * time_count
    step_gain = jnp.where((hour_ids == total_hours - 1)[:, None], jnp.float32(0.0), gains)
    scale = step_gain * rates[None, :]

    prod_fwd, prod_back, back_prod, part = gain_scans(factors, step_gain, scale)
    local_fwd, back_local, summary = local_scans(factors, parts, step_gain, scale, part, time_count)
    every = gather_tm(summary)
    filtered, smoothed = combine(
        every, initial[None, :], prod_fwd, local_fwd, prod_back, back_local, back_prod
    )
    return (filtered, smoothed)


def solution(mesh):
    in_specs = (
        P("tm", "sensor"),
        P("tm", "sensor"),
        P("sensor", None),
        P("tm", None),
        P("tm", None),
        P(),
        P(),
    )
    out_specs = (P("tm", "sensor"), P("tm", "sensor"))
    return jax.shard_map(
        per_device, mesh=mesh, in_specs=in_specs, out_specs=out_specs, check_vma=False
    )
```

```python
import jax
import jax.numpy as jnp
from jax import lax
from jax.experimental import pallas as pl
from jax.experimental.pallas import tpu as pltpu
from jax.sharding import PartitionSpec as P


SUB = 8
CHUNK = 64


def _chunk_scan(a, x, rows, reverse):
    sub = lax.broadcasted_iota(jnp.int32, a.shape, 0) % CHUNK
    for k in (1, 2, 4, 8, 16, 32):
        shift = rows - k if reverse else k
        prev_a = pltpu.roll(a, shift, 0)
        prev_x = [pltpu.roll(v, shift, 0) for v in x]
        inside = sub < CHUNK - k if reverse else sub >= k
        x = [jnp.where(inside, a * p + v, v) for p, v in zip(prev_x, x)]
        a = jnp.where(inside, a * prev_a, a)
    return a, x


def _carry(a, x, out_a, out_x, rows, reverse):
    chunks = rows // CHUNK
    order = range(chunks - 1, -1, -1) if reverse else range(chunks)
    edge = 0 if reverse else CHUNK - 1
    carry_a = None
    for i in order:
        ca = a[i * CHUNK:(i + 1) * CHUNK]
        cx = [v[i * CHUNK:(i + 1) * CHUNK] for v in x]
        if carry_a is not None:
            cx = [c * px + v for c, px, v in zip([ca] * len(cx), carry_x, cx)]
            ca = ca * carry_a
        if out_a is not None:
            out_a[i * CHUNK:(i + 1) * CHUNK, :] = ca
        for o, v in zip(out_x, cx):
            o[i * CHUNK:(i + 1) * CHUNK, :] = v
        carry_a = jnp.broadcast_to(ca[edge:edge + 1], ca.shape)
        carry_x = [jnp.broadcast_to(v[edge:edge + 1], v.shape) for v in cx]


def _summary_tile(rows_by_slot, cols):
    sub = lax.broadcasted_iota(jnp.int32, (SUB, cols), 0)
    tile = jnp.zeros((SUB, cols), jnp.float32)
    for row, value in rows_by_slot:
        tile = jnp.where(sub == row, jnp.broadcast_to(value, tile.shape), tile)
    return tile


def gain_scan_kernel(a_ref, g_ref, s_ref, pf_ref, pb_ref, bp_ref, part_ref):
    rows, cols = a_ref.shape
    a, _ = _chunk_scan(a_ref[...], [], rows, False)
    _carry(a, [], pf_ref, [], rows, False)
    scale = s_ref[...]
    pf = pf_ref[...]
    g, (op,) = _chunk_scan(g_ref[...], [pf - scale * pf], rows, True)
    _carry(g, [op], pb_ref, [bp_ref], rows, True)
    part_ref[...] = _summary_tile(
        [(0, pf_ref[rows - 1:rows, :]), (2, pb_ref[0:1, :]), (4, bp_ref[0:1, :])], cols
    )


def gain_scans(factors, step_gain, scale):
    shape = jax.ShapeDtypeStruct(factors.shape, jnp.float32)
    rows, cols = factors.shape
    return pl.pallas_call(
        gain_scan_kernel,
        out_shape=[shape] * 3 + [jax.ShapeDtypeStruct((SUB, cols), jnp.float32)],
        cost_estimate=pl.CostEstimate(flops=20 * rows * cols, bytes_accessed=24 * rows * cols, transcendentals=0),
    )(factors, step_gain, scale)


def scan_kernel(a_ref, own_ref, r1_ref, r2_ref, r3_ref, g_ref, s_ref, part_ref, lf_ref, bl_ref, sum_ref):
    rows, cols = a_ref.shape
    inflow = ((own_ref[...] + r1_ref[...]) + r2_ref[...]) + r3_ref[...]
    a, (u,) = _chunk_scan(a_ref[...], [inflow], rows, False)
    _carry(a, [u], None, [lf_ref], rows, False)
    scale = s_ref[...]
    lf = lf_ref[...]
    g, (ol,) = _chunk_scan(g_ref[...], [lf - scale * lf], rows, True)
    _carry(g, [ol], None, [bl_ref], rows, True)
    sub = lax.broadcasted_iota(jnp.int32, (SUB, cols), 0)
    tile = jnp.where(
        sub == 1,
        jnp.broadcast_to(lf_ref[rows - 1:rows, :], (SUB, cols)),
        jnp.where(sub == 3, jnp.broadcast_to(bl_ref[0:1, :], (SUB, cols)), part_ref[...]),
    )
    for k in range(sum_ref.shape[0]):
        sum_ref[k] = tile


def local_scans(factors, parts, step_gain, scale, part, blocks):
    shape = jax.ShapeDtypeStruct(factors.shape, jnp.float32)
    rows, cols = factors.shape
    return pl.pallas_call(
        scan_kernel,
        out_shape=[shape] * 2 + [jax.ShapeDtypeStruct((blocks, SUB, cols), jnp.float32)],
        cost_estimate=pl.CostEstimate(flops=20 * rows * cols, bytes_accessed=40 * rows * cols, transcendentals=0),
    )(factors, *parts, step_gain, scale, part)


def combine_kernel(every_ref, init_ref, pf_ref, lf_ref, pb_ref, bl_ref, bp_ref, f_ref, s_ref):
    count = every_ref.shape[0]
    place = lax.axis_index("tm")
    prod, local, back_gain, back_local, back_prod = (every_ref[:, r, :] for r in range(5))
    row = lax.broadcasted_iota(jnp.int32, prod.shape, 0)
    step = 1
    while step < count:
        earlier_a = pltpu.roll(prod, step, 0)
        earlier_x = pltpu.roll(local, step, 0)
        inside = row >= step
        local = jnp.where(inside, prod * earlier_x + local, local)
        prod = jnp.where(inside, prod * earlier_a, prod)
        step *= 2
    initial = init_ref[...]
    entering = jnp.where(row == 0, initial, pltpu.roll(prod * initial + local, 1, 0))
    gain, after = back_gain, back_local + back_prod * entering
    step = 1
    while step < count:
        later_a = pltpu.roll(gain, count - step, 0)
        later_x = pltpu.roll(after, count - step, 0)
        inside = row < count - step
        after = jnp.where(inside, gain * later_x + after, after)
        gain = jnp.where(inside, gain * later_a, gain)
        step *= 2
    e_here = jnp.sum(jnp.where(row == place, entering, 0.0), axis=0, keepdims=True)
    y_here = jnp.sum(jnp.where(row == place + 1, after, 0.0), axis=0, keepdims=True)
    f_ref[...] = lf_ref[...] + pf_ref[...] * e_here
    s_ref[...] = bl_ref[...] + bp_ref[...] * e_here + pb_ref[...] * y_here


def combine(every, initial, pf, lf, pb, bl, bp):
    rows, cols = pf.shape
    shape = jax.ShapeDtypeStruct(pf.shape, jnp.float32)
    return pl.pallas_call(
        combine_kernel,
        out_shape=[shape, shape],
        cost_estimate=pl.CostEstimate(flops=5 * rows * cols, bytes_accessed=28 * rows * cols, transcendentals=0),
    )(every, initial, pf, lf, pb, bl, bp)


def matmul_kernel(slots_ref, obs_ref, gain_ref, keep_ref, send_ref, lhs_ref):
    blocks = obs_ref.shape[1] // 128
    sensor = lax.axis_index("sensor")

    @pl.when(pl.program_id(0) == 0)
    def _():
        slots = slots_ref[...]
        shape = (128, slots.shape[1])
        block_of = lax.broadcasted_iota(jnp.int32, shape, 0)
        wanted = jnp.where(block_of < blocks, sensor * blocks + block_of, -2)
        listed_t = jnp.zeros(shape, jnp.float32)
        for s in range(slots.shape[0]):
            listed_t = jnp.maximum(listed_t, (slots[s:s + 1, :] == wanted).astype(jnp.float32))
        listed = listed_t.T
        for b in range(blocks):
            cols = pl.ds(128 * b, 128)
            block = obs_ref[:, cols]
            lhs_ref[:, cols] = jnp.where(listed[:, b:b + 1] > 0, block, jnp.zeros_like(block))

    prod = jnp.dot(lhs_ref[...], gain_ref[...], preferred_element_type=jnp.float32)
    half = prod.shape[1] // 2
    even = sensor % 2 == 0
    keep_ref[0] = jnp.where(even, prod[:, :half], prod[:, half:])
    send_ref[0] = jnp.where(even, prod[:, half:], prod[:, :half])


def listed_matmul(slots, observations, gain_rows):
    rows, depth = observations.shape
    modes = gain_rows.shape[1]
    tile = 256
    tiles = modes // tile
    piece = jax.ShapeDtypeStruct((tiles, rows, tile // 2), jnp.float32)
    return pl.pallas_call(
        matmul_kernel,
        grid=(tiles,),
        in_specs=[
            pl.BlockSpec(slots.shape, lambda j: (0, 0)),
            pl.BlockSpec((rows, depth), lambda j: (0, 0)),
            pl.BlockSpec((depth, tile), lambda j: (0, j)),
        ],
        out_specs=[
            pl.BlockSpec((1, rows, tile // 2), lambda j: (j, 0, 0)),
            pl.BlockSpec((1, rows, tile // 2), lambda j: (j, 0, 0)),
        ],
        out_shape=[piece, piece],
        scratch_shapes=[pltpu.VMEM((rows, depth), jnp.bfloat16)],
        compiler_params=pltpu.CompilerParams(dimension_semantics=("arbitrary",)),
        cost_estimate=pl.CostEstimate(
            flops=2 * rows * depth * modes,
            bytes_accessed=2 * rows * depth + 2 * depth * modes + 4 * rows * modes,
            transcendentals=0,
        ),
    )(slots, observations, gain_rows)


def sensor_reduce_scatter(keep, send):
    count = lax.axis_size("sensor")
    chips = count // 2
    j = lax.axis_index("sensor")
    chip = j // 2
    chip_sum = keep + lax.ppermute(send, "sensor", [(i, i ^ 1) for i in range(count)])
    parts = [lax.dynamic_index_in_dim(chip_sum, chip, 0, False)]
    for shift in range(1, chips):
        part = lax.dynamic_index_in_dim(chip_sum, (chip + shift) % chips, 0, False)
        perm = [(i, (((i // 2) + shift) % chips) * 2 + i % 2) for i in range(count)]
        parts.append(lax.ppermute(part, "sensor", perm))
    return parts


def gather_tm(copies):
    return lax.all_to_all(copies, "tm", 0, 0, tiled=True)


def per_device(observations, obs_list, gain_rows, decay, smooth_gain, model_rate, first_state):
    sensor_count = lax.axis_size("sensor")
    sensor_index = lax.axis_index("sensor")
    time_index = lax.axis_index("tm")
    time_count = lax.axis_size("tm")
    rows_here = observations.shape[0]
    keep, send = listed_matmul(obs_list.T, observations, gain_rows)
    width = gain_rows.shape[1] // sensor_count
    parts = sensor_reduce_scatter(keep, send)
    start_col = sensor_index * width
    factors = lax.dynamic_slice_in_dim(decay, start_col, width, 1)
    gains = lax.dynamic_slice_in_dim(smooth_gain, start_col, width, 1)
    rates = lax.dynamic_slice_in_dim(model_rate, start_col, width, 0)
    initial = lax.dynamic_slice_in_dim(first_state, start_col, width, 0)
    hour_ids = time_index * rows_here + jnp.arange(rows_here, dtype=jnp.int32)
    total_hours = rows_here * time_count
    step_gain = jnp.where((hour_ids == total_hours - 1)[:, None], jnp.float32(0.0), gains)
    scale = step_gain * rates[None, :]

    prod_fwd, prod_back, back_prod, part = gain_scans(factors, step_gain, scale)
    local_fwd, back_local, summary = local_scans(factors, parts, step_gain, scale, part, time_count)
    every = gather_tm(summary)
    filtered, smoothed = combine(
        every, initial[None, :], prod_fwd, local_fwd, prod_back, back_local, back_prod
    )
    return (filtered, smoothed)


def solution(mesh):
    in_specs = (
        P("tm", "sensor"),
        P("tm", "sensor"),
        P("sensor", None),
        P("tm", None),
        P("tm", None),
        P(),
        P(),
    )
    out_specs = (P("tm", "sensor"), P("tm", "sensor"))
    return jax.shard_map(
        per_device, mesh=mesh, in_specs=in_specs, out_specs=out_specs, check_vma=False
    )
```

```python
import jax
import jax.numpy as jnp
from jax import lax
from jax.experimental import pallas as pl
from jax.experimental.pallas import tpu as pltpu
from jax.sharding import PartitionSpec as P


SUB = 8
CHUNK = 64


def _chunk_scan(a, x, rows, reverse):
    sub = lax.broadcasted_iota(jnp.int32, a.shape, 0) % CHUNK
    for k in (1, 2, 4, 8, 16, 32):
        shift = rows - k if reverse else k
        prev_a = pltpu.roll(a, shift, 0)
        prev_x = [pltpu.roll(v, shift, 0) for v in x]
        inside = sub < CHUNK - k if reverse else sub >= k
        x = [jnp.where(inside, a * p + v, v) for p, v in zip(prev_x, x)]
        a = jnp.where(inside, a * prev_a, a)
    return a, x


def _carry(a, x, out_a, out_x, rows, reverse):
    chunks = rows // CHUNK
    order = range(chunks - 1, -1, -1) if reverse else range(chunks)
    edge = 0 if reverse else CHUNK - 1
    carry_a = None
    for i in order:
        ca = a[i * CHUNK:(i + 1) * CHUNK]
        cx = [v[i * CHUNK:(i + 1) * CHUNK] for v in x]
        if carry_a is not None:
            cx = [c * px + v for c, px, v in zip([ca] * len(cx), carry_x, cx)]
            ca = ca * carry_a
        if out_a is not None:
            out_a[i * CHUNK:(i + 1) * CHUNK, :] = ca
        for o, v in zip(out_x, cx):
            o[i * CHUNK:(i + 1) * CHUNK, :] = v
        carry_a = jnp.broadcast_to(ca[edge:edge + 1], ca.shape)
        carry_x = [jnp.broadcast_to(v[edge:edge + 1], v.shape) for v in cx]


def _summary_tile(rows_by_slot, cols):
    sub = lax.broadcasted_iota(jnp.int32, (SUB, cols), 0)
    tile = jnp.zeros((SUB, cols), jnp.float32)
    for row, value in rows_by_slot:
        tile = jnp.where(sub == row, jnp.broadcast_to(value, tile.shape), tile)
    return tile


def gain_scan_kernel(a_ref, g_ref, s_ref, pf_ref, pb_ref, bp_ref, part_ref):
    rows, cols = a_ref.shape
    a, _ = _chunk_scan(a_ref[...], [], rows, False)
    _carry(a, [], pf_ref, [], rows, False)
    scale = s_ref[...]
    pf = pf_ref[...]
    g, (op,) = _chunk_scan(g_ref[...], [pf - scale * pf], rows, True)
    _carry(g, [op], pb_ref, [bp_ref], rows, True)
    part_ref[...] = _summary_tile(
        [(0, pf_ref[rows - 1:rows, :]), (2, pb_ref[0:1, :]), (4, bp_ref[0:1, :])], cols
    )


def gain_scans(factors, step_gain, scale):
    shape = jax.ShapeDtypeStruct(factors.shape, jnp.float32)
    rows, cols = factors.shape
    return pl.pallas_call(
        gain_scan_kernel,
        out_shape=[shape] * 3 + [jax.ShapeDtypeStruct((SUB, cols), jnp.float32)],
        cost_estimate=pl.CostEstimate(flops=20 * rows * cols, bytes_accessed=24 * rows * cols, transcendentals=0),
    )(factors, step_gain, scale)


def scan_kernel(a_ref, own_ref, r1_ref, r2_ref, r3_ref, g_ref, s_ref, part_ref, lf_ref, bl_ref, sum_ref):
    rows, cols = a_ref.shape
    inflow = ((own_ref[...] + r1_ref[...]) + r2_ref[...]) + r3_ref[...]
    a, (u,) = _chunk_scan(a_ref[...], [inflow], rows, False)
    _carry(a, [u], None, [lf_ref], rows, False)
    scale = s_ref[...]
    lf = lf_ref[...]
    g, (ol,) = _chunk_scan(g_ref[...], [lf - scale * lf], rows, True)
    _carry(g, [ol], None, [bl_ref], rows, True)
    sub = lax.broadcasted_iota(jnp.int32, (SUB, cols), 0)
    tile = jnp.where(
        sub == 1,
        jnp.broadcast_to(lf_ref[rows - 1:rows, :], (SUB, cols)),
        jnp.where(sub == 3, jnp.broadcast_to(bl_ref[0:1, :], (SUB, cols)), part_ref[...]),
    )
    for k in range(sum_ref.shape[0]):
        sum_ref[k] = tile


def local_scans(factors, parts, step_gain, scale, part, blocks):
    shape = jax.ShapeDtypeStruct(factors.shape, jnp.float32)
    rows, cols = factors.shape
    return pl.pallas_call(
        scan_kernel,
        out_shape=[shape] * 2 + [jax.ShapeDtypeStruct((blocks, SUB, cols), jnp.float32)],
        cost_estimate=pl.CostEstimate(flops=20 * rows * cols, bytes_accessed=40 * rows * cols, transcendentals=0),
    )(factors, *parts, step_gain, scale, part)


def matmul_kernel(slots_ref, obs_ref, gain_ref, keep_ref, send_ref, lhs_ref):
    blocks = obs_ref.shape[1] // 128
    sensor = lax.axis_index("sensor")

    @pl.when(pl.program_id(0) == 0)
    def _():
        slots = slots_ref[...]
        shape = (128, slots.shape[1])
        block_of = lax.broadcasted_iota(jnp.int32, shape, 0)
        wanted = jnp.where(block_of < blocks, sensor * blocks + block_of, -2)
        listed_t = jnp.zeros(shape, jnp.float32)
        for s in range(slots.shape[0]):
            listed_t = jnp.maximum(listed_t, (slots[s:s + 1, :] == wanted).astype(jnp.float32))
        listed = listed_t.T
        for b in range(blocks):
            cols = pl.ds(128 * b, 128)
            block = obs_ref[:, cols]
            lhs_ref[:, cols] = jnp.where(listed[:, b:b + 1] > 0, block, jnp.zeros_like(block))

    prod = jnp.dot(lhs_ref[...], gain_ref[...], preferred_element_type=jnp.float32)
    half = prod.shape[1] // 2
    even = sensor % 2 == 0
    keep_ref[0] = jnp.where(even, prod[:, :half], prod[:, half:])
    send_ref[0] = jnp.where(even, prod[:, half:], prod[:, :half])


def listed_matmul(slots, observations, gain_rows):
    rows, depth = observations.shape
    modes = gain_rows.shape[1]
    tile = 256
    tiles = modes // tile
    piece = jax.ShapeDtypeStruct((tiles, rows, tile // 2), jnp.float32)
    return pl.pallas_call(
        matmul_kernel,
        grid=(tiles,),
        in_specs=[
            pl.BlockSpec(slots.shape, lambda j: (0, 0)),
            pl.BlockSpec((rows, depth), lambda j: (0, 0)),
            pl.BlockSpec((depth, tile), lambda j: (0, j)),
        ],
        out_specs=[
            pl.BlockSpec((1, rows, tile // 2), lambda j: (j, 0, 0)),
            pl.BlockSpec((1, rows, tile // 2), lambda j: (j, 0, 0)),
        ],
        out_shape=[piece, piece],
        scratch_shapes=[pltpu.VMEM((rows, depth), jnp.bfloat16)],
        compiler_params=pltpu.CompilerParams(dimension_semantics=("arbitrary",)),
        cost_estimate=pl.CostEstimate(
            flops=2 * rows * depth * modes,
            bytes_accessed=2 * rows * depth + 2 * depth * modes + 4 * rows * modes,
            transcendentals=0,
        ),
    )(slots, observations, gain_rows)


def sensor_reduce_scatter(keep, send):
    count = lax.axis_size("sensor")
    chips = count // 2
    j = lax.axis_index("sensor")
    chip = j // 2
    chip_sum = keep + lax.ppermute(send, "sensor", [(i, i ^ 1) for i in range(count)])
    parts = [lax.dynamic_index_in_dim(chip_sum, chip, 0, False)]
    for shift in range(1, chips):
        part = lax.dynamic_index_in_dim(chip_sum, (chip + shift) % chips, 0, False)
        perm = [(i, (((i // 2) + shift) % chips) * 2 + i % 2) for i in range(count)]
        parts.append(lax.ppermute(part, "sensor", perm))
    return parts


def gather_tm(copies):
    return lax.all_to_all(copies, "tm", 0, 0, tiled=True)


def per_device(observations, obs_list, gain_rows, decay, smooth_gain, model_rate, first_state):
    sensor_count = lax.axis_size("sensor")
    sensor_index = lax.axis_index("sensor")
    time_index = lax.axis_index("tm")
    time_count = lax.axis_size("tm")
    rows_here = observations.shape[0]
    keep, send = listed_matmul(obs_list.T, observations, gain_rows)
    width = gain_rows.shape[1] // sensor_count
    parts = sensor_reduce_scatter(keep, send)
    start_col = sensor_index * width
    factors = lax.dynamic_slice_in_dim(decay, start_col, width, 1)
    gains = lax.dynamic_slice_in_dim(smooth_gain, start_col, width, 1)
    rates = lax.dynamic_slice_in_dim(model_rate, start_col, width, 0)
    initial = lax.dynamic_slice_in_dim(first_state, start_col, width, 0)
    hour_ids = time_index * rows_here + jnp.arange(rows_here, dtype=jnp.int32)
    total_hours = rows_here * time_count
    step_gain = jnp.where((hour_ids == total_hours - 1)[:, None], jnp.float32(0.0), gains)
    scale = step_gain * rates[None, :]

    prod_fwd, prod_back, back_prod, part = gain_scans(factors, step_gain, scale)
    local_fwd, back_local, summary = local_scans(factors, parts, step_gain, scale, part, time_count)
    every = gather_tm(summary)
    entering = [initial]
    for k in range(time_count - 1):
        entering.append(every[k, 0] * entering[-1] + every[k, 1])
    after = [jnp.zeros_like(initial)]
    for k in range(time_count - 1, 0, -1):
        after.append(every[k, 3] + every[k, 4] * entering[k] + every[k, 2] * after[-1])
    after = after[::-1]
    entering_here = lax.dynamic_index_in_dim(jnp.stack(entering, 0), time_index, 0, False)
    after_here = lax.dynamic_index_in_dim(jnp.stack(after, 0), time_index, 0, False)
    filtered = local_fwd + prod_fwd * entering_here[None, :]
    smoothed = back_local + back_prod * entering_here[None, :] + prod_back * after_here[None, :]
    return (filtered, smoothed)


def solution(mesh):
    in_specs = (
        P("tm", "sensor"),
        P("tm", "sensor"),
        P("sensor", None),
        P("tm", None),
        P("tm", None),
        P(),
        P(),
    )
    out_specs = (P("tm", "sensor"), P("tm", "sensor"))
    return jax.shard_map(
        per_device, mesh=mesh, in_specs=in_specs, out_specs=out_specs, check_vma=False
    )
```

```python
import jax
import jax.numpy as jnp
from jax import lax
from jax.experimental import pallas as pl
from jax.experimental.pallas import tpu as pltpu
from jax.sharding import PartitionSpec as P


SUB = 8
CHUNK = 64


def _chunk_scan(a, x, rows, reverse):
    sub = lax.broadcasted_iota(jnp.int32, a.shape, 0) % CHUNK
    for k in (1, 2, 4, 8, 16, 32):
        shift = rows - k if reverse else k
        prev_a = pltpu.roll(a, shift, 0)
        prev_x = [pltpu.roll(v, shift, 0) for v in x]
        inside = sub < CHUNK - k if reverse else sub >= k
        x = [jnp.where(inside, a * p + v, v) for p, v in zip(prev_x, x)]
        a = jnp.where(inside, a * prev_a, a)
    return a, x


def _carry(a, x, out_a, out_x, rows, reverse):
    chunks = rows // CHUNK
    order = range(chunks - 1, -1, -1) if reverse else range(chunks)
    edge = 0 if reverse else CHUNK - 1
    carry_a = None
    for i in order:
        ca = a[i * CHUNK:(i + 1) * CHUNK]
        cx = [v[i * CHUNK:(i + 1) * CHUNK] for v in x]
        if carry_a is not None:
            cx = [c * px + v for c, px, v in zip([ca] * len(cx), carry_x, cx)]
            ca = ca * carry_a
        if out_a is not None:
            out_a[i * CHUNK:(i + 1) * CHUNK, :] = ca
        for o, v in zip(out_x, cx):
            o[i * CHUNK:(i + 1) * CHUNK, :] = v
        carry_a = jnp.broadcast_to(ca[edge:edge + 1], ca.shape)
        carry_x = [jnp.broadcast_to(v[edge:edge + 1], v.shape) for v in cx]


def _summary_tile(rows_by_slot, cols):
    sub = lax.broadcasted_iota(jnp.int32, (SUB, cols), 0)
    tile = jnp.zeros((SUB, cols), jnp.float32)
    for row, value in rows_by_slot:
        tile = jnp.where(sub == row, jnp.broadcast_to(value, tile.shape), tile)
    return tile


def gain_scan_kernel(a_ref, g_ref, s_ref, pf_ref, pb_ref, bp_ref, part_ref):
    rows, cols = a_ref.shape
    a, _ = _chunk_scan(a_ref[...], [], rows, False)
    _carry(a, [], pf_ref, [], rows, False)
    scale = s_ref[...]
    pf = pf_ref[...]
    g, (op,) = _chunk_scan(g_ref[...], [pf - scale * pf], rows, True)
    _carry(g, [op], pb_ref, [bp_ref], rows, True)
    part_ref[...] = _summary_tile(
        [(0, pf_ref[rows - 1:rows, :]), (2, pb_ref[0:1, :]), (4, bp_ref[0:1, :])], cols
    )


def gain_scans(factors, step_gain, scale):
    shape = jax.ShapeDtypeStruct(factors.shape, jnp.float32)
    rows, cols = factors.shape
    return pl.pallas_call(
        gain_scan_kernel,
        out_shape=[shape] * 3 + [jax.ShapeDtypeStruct((SUB, cols), jnp.float32)],
        cost_estimate=pl.CostEstimate(flops=20 * rows * cols, bytes_accessed=24 * rows * cols, transcendentals=0),
    )(factors, step_gain, scale)


def scan_kernel(a_ref, own_ref, r1_ref, r2_ref, r3_ref, g_ref, s_ref, part_ref, lf_ref, bl_ref, sum_ref):
    rows, cols = a_ref.shape
    inflow = ((own_ref[...] + r1_ref[...]) + r2_ref[...]) + r3_ref[...]
    a, (u,) = _chunk_scan(a_ref[...], [inflow], rows, False)
    _carry(a, [u], None, [lf_ref], rows, False)
    scale = s_ref[...]
    lf = lf_ref[...]
    g, (ol,) = _chunk_scan(g_ref[...], [lf - scale * lf], rows, True)
    _carry(g, [ol], None, [bl_ref], rows, True)
    sub = lax.broadcasted_iota(jnp.int32, (SUB, cols), 0)
    tile = jnp.where(
        sub == 1,
        jnp.broadcast_to(lf_ref[rows - 1:rows, :], (SUB, cols)),
        jnp.where(sub == 3, jnp.broadcast_to(bl_ref[0:1, :], (SUB, cols)), part_ref[...]),
    )
    for k in range(sum_ref.shape[0]):
        sum_ref[k] = tile


def local_scans(factors, parts, step_gain, scale, part, blocks):
    shape = jax.ShapeDtypeStruct(factors.shape, jnp.float32)
    rows, cols = factors.shape
    return pl.pallas_call(
        scan_kernel,
        out_shape=[shape] * 2 + [jax.ShapeDtypeStruct((blocks, SUB, cols), jnp.float32)],
        cost_estimate=pl.CostEstimate(flops=20 * rows * cols, bytes_accessed=40 * rows * cols, transcendentals=0),
    )(factors, *parts, step_gain, scale, part)


def combine_kernel(every_ref, init_ref, pf_ref, lf_ref, pb_ref, bl_ref, bp_ref, f_ref, s_ref):
    count = every_ref.shape[0]
    place = lax.axis_index("tm")
    entering = [init_ref[...]]
    for k in range(count - 1):
        tile = every_ref[k]
        entering.append(tile[0:1] * entering[-1] + tile[1:2])
    after = jnp.zeros_like(entering[0])
    e_here = jnp.where(place == count - 1, entering[count - 1], 0.0)
    y_here = jnp.zeros_like(after)
    for k in range(count - 1, 0, -1):
        tile = every_ref[k]
        after = tile[3:4] + tile[4:5] * entering[k] + tile[2:3] * after
        e_here = jnp.where(place == k - 1, entering[k - 1], e_here)
        y_here = jnp.where(place == k - 1, after, y_here)
    f_ref[...] = lf_ref[...] + pf_ref[...] * e_here
    s_ref[...] = bl_ref[...] + bp_ref[...] * e_here + pb_ref[...] * y_here


def combine(every, initial, pf, lf, pb, bl, bp):
    rows, cols = pf.shape
    shape = jax.ShapeDtypeStruct(pf.shape, jnp.float32)
    return pl.pallas_call(
        combine_kernel,
        out_shape=[shape, shape],
        cost_estimate=pl.CostEstimate(flops=5 * rows * cols, bytes_accessed=28 * rows * cols, transcendentals=0),
    )(every, initial, pf, lf, pb, bl, bp)


def matmul_kernel(slots_ref, obs_ref, gain_ref, keep_ref, send_ref, lhs_ref):
    blocks = obs_ref.shape[1] // 128
    sensor = lax.axis_index("sensor")

    @pl.when(pl.program_id(0) == 0)
    def _():
        slots = slots_ref[...]
        shape = (128, slots.shape[1])
        block_of = lax.broadcasted_iota(jnp.int32, shape, 0)
        wanted = jnp.where(block_of < blocks, sensor * blocks + block_of, -2)
        listed_t = jnp.zeros(shape, jnp.float32)
        for s in range(slots.shape[0]):
            listed_t = jnp.maximum(listed_t, (slots[s:s + 1, :] == wanted).astype(jnp.float32))
        listed = listed_t.T
        for b in range(blocks):
            cols = pl.ds(128 * b, 128)
            block = obs_ref[:, cols]
            lhs_ref[:, cols] = jnp.where(listed[:, b:b + 1] > 0, block, jnp.zeros_like(block))

    prod = jnp.dot(lhs_ref[...], gain_ref[...], preferred_element_type=jnp.float32)
    even = sensor % 2 == 0
    for c in range(keep_ref.shape[0]):
        left = prod[:, 256 * c:256 * c + 128]
        right = prod[:, 256 * c + 128:256 * c + 256]
        keep_ref[c] = jnp.where(even, left, right)
        send_ref[c] = jnp.where(even, right, left)


def listed_matmul(slots, observations, gain_rows):
    rows, depth = observations.shape
    modes = gain_rows.shape[1]
    tile = 512
    tiles = modes // tile
    chips_per_tile = tile // 256
    piece = jax.ShapeDtypeStruct((modes // 256, rows, 128), jnp.float32)
    return pl.pallas_call(
        matmul_kernel,
        grid=(tiles,),
        in_specs=[
            pl.BlockSpec(slots.shape, lambda j: (0, 0)),
            pl.BlockSpec((rows, depth), lambda j: (0, 0)),
            pl.BlockSpec((depth, tile), lambda j: (0, j)),
        ],
        out_specs=[
            pl.BlockSpec((chips_per_tile, rows, 128), lambda j: (j, 0, 0)),
            pl.BlockSpec((chips_per_tile, rows, 128), lambda j: (j, 0, 0)),
        ],
        out_shape=[piece, piece],
        scratch_shapes=[pltpu.VMEM((rows, depth), jnp.bfloat16)],
        compiler_params=pltpu.CompilerParams(dimension_semantics=("arbitrary",)),
        cost_estimate=pl.CostEstimate(
            flops=2 * rows * depth * modes,
            bytes_accessed=2 * rows * depth + 2 * depth * modes + 4 * rows * modes,
            transcendentals=0,
        ),
    )(slots, observations, gain_rows)


def sensor_reduce_scatter(keep, send):
    count = lax.axis_size("sensor")
    chips = count // 2
    j = lax.axis_index("sensor")
    chip = j // 2
    chip_sum = keep + lax.ppermute(send, "sensor", [(i, i ^ 1) for i in range(count)])
    parts = [lax.dynamic_index_in_dim(chip_sum, chip, 0, False)]
    for shift in range(1, chips):
        part = lax.dynamic_index_in_dim(chip_sum, (chip + shift) % chips, 0, False)
        perm = [(i, (((i // 2) + shift) % chips) * 2 + i % 2) for i in range(count)]
        parts.append(lax.ppermute(part, "sensor", perm))
    return parts


def gather_tm(copies):
    return lax.all_to_all(copies, "tm", 0, 0, tiled=True)


def per_device(observations, obs_list, gain_rows, decay, smooth_gain, model_rate, first_state):
    sensor_count = lax.axis_size("sensor")
    sensor_index = lax.axis_index("sensor")
    time_index = lax.axis_index("tm")
    time_count = lax.axis_size("tm")
    rows_here = observations.shape[0]
    keep, send = listed_matmul(obs_list.T, observations, gain_rows)
    width = gain_rows.shape[1] // sensor_count
    parts = sensor_reduce_scatter(keep, send)
    start_col = sensor_index * width
    factors = lax.dynamic_slice_in_dim(decay, start_col, width, 1)
    gains = lax.dynamic_slice_in_dim(smooth_gain, start_col, width, 1)
    rates = lax.dynamic_slice_in_dim(model_rate, start_col, width, 0)
    initial = lax.dynamic_slice_in_dim(first_state, start_col, width, 0)
    hour_ids = time_index * rows_here + jnp.arange(rows_here, dtype=jnp.int32)
    total_hours = rows_here * time_count
    step_gain = jnp.where((hour_ids == total_hours - 1)[:, None], jnp.float32(0.0), gains)
    scale = step_gain * rates[None, :]

    prod_fwd, prod_back, back_prod, part = gain_scans(factors, step_gain, scale)
    local_fwd, back_local, summary = local_scans(factors, parts, step_gain, scale, part, time_count)
    every = gather_tm(summary)
    filtered, smoothed = combine(
        every, initial[None, :], prod_fwd, local_fwd, prod_back, back_local, back_prod
    )
    return (filtered, smoothed)


def solution(mesh):
    in_specs = (
        P("tm", "sensor"),
        P("tm", "sensor"),
        P("sensor", None),
        P("tm", None),
        P("tm", None),
        P(),
        P(),
    )
    out_specs = (P("tm", "sensor"), P("tm", "sensor"))
    return jax.shard_map(
        per_device, mesh=mesh, in_specs=in_specs, out_specs=out_specs, check_vma=False
    )
```

```python
import jax
import jax.numpy as jnp
from jax import lax
from jax.experimental import pallas as pl
from jax.experimental.pallas import tpu as pltpu
from jax.sharding import PartitionSpec as P


SUB = 8
CHUNK = 64


def _chunk_scan(a, x, rows, reverse):
    sub = lax.broadcasted_iota(jnp.int32, a.shape, 0) % CHUNK
    for k in (1, 2, 4, 8, 16, 32):
        shift = rows - k if reverse else k
        prev_a = pltpu.roll(a, shift, 0)
        prev_x = [pltpu.roll(v, shift, 0) for v in x]
        inside = sub < CHUNK - k if reverse else sub >= k
        x = [jnp.where(inside, a * p + v, v) for p, v in zip(prev_x, x)]
        a = jnp.where(inside, a * prev_a, a)
    return a, x


def _carry(a, x, out_a, out_x, rows, reverse):
    chunks = rows // CHUNK
    order = range(chunks - 1, -1, -1) if reverse else range(chunks)
    edge = 0 if reverse else CHUNK - 1
    carry_a = None
    for i in order:
        ca = a[i * CHUNK:(i + 1) * CHUNK]
        cx = [v[i * CHUNK:(i + 1) * CHUNK] for v in x]
        if carry_a is not None:
            cx = [c * px + v for c, px, v in zip([ca] * len(cx), carry_x, cx)]
            ca = ca * carry_a
        if out_a is not None:
            out_a[i * CHUNK:(i + 1) * CHUNK, :] = ca
        for o, v in zip(out_x, cx):
            o[i * CHUNK:(i + 1) * CHUNK, :] = v
        carry_a = jnp.broadcast_to(ca[edge:edge + 1], ca.shape)
        carry_x = [jnp.broadcast_to(v[edge:edge + 1], v.shape) for v in cx]


def _summary_tile(rows_by_slot, cols):
    sub = lax.broadcasted_iota(jnp.int32, (SUB, cols), 0)
    tile = jnp.zeros((SUB, cols), jnp.float32)
    for row, value in rows_by_slot:
        tile = jnp.where(sub == row, jnp.broadcast_to(value, tile.shape), tile)
    return tile


def gain_scan_kernel(a_ref, g_ref, s_ref, pf_ref, pb_ref, bp_ref, part_ref):
    rows, cols = a_ref.shape
    a, _ = _chunk_scan(a_ref[...], [], rows, False)
    _carry(a, [], pf_ref, [], rows, False)
    scale = s_ref[...]
    pf = pf_ref[...]
    g, (op,) = _chunk_scan(g_ref[...], [pf - scale * pf], rows, True)
    _carry(g, [op], pb_ref, [bp_ref], rows, True)
    part_ref[...] = _summary_tile(
        [(0, pf_ref[rows - 1:rows, :]), (2, pb_ref[0:1, :]), (4, bp_ref[0:1, :])], cols
    )


def gain_scans(factors, step_gain, scale):
    shape = jax.ShapeDtypeStruct(factors.shape, jnp.float32)
    rows, cols = factors.shape
    return pl.pallas_call(
        gain_scan_kernel,
        out_shape=[shape] * 3 + [jax.ShapeDtypeStruct((SUB, cols), jnp.float32)],
        cost_estimate=pl.CostEstimate(flops=20 * rows * cols, bytes_accessed=24 * rows * cols, transcendentals=0),
    )(factors, step_gain, scale)


def scan_kernel(a_ref, own_ref, r1_ref, r2_ref, r3_ref, g_ref, s_ref, part_ref, lf_ref, bl_ref, sum_ref):
    rows, cols = a_ref.shape
    inflow = ((own_ref[...] + r1_ref[...]) + r2_ref[...]) + r3_ref[...]
    a, (u,) = _chunk_scan(a_ref[...], [inflow], rows, False)
    _carry(a, [u], None, [lf_ref], rows, False)
    scale = s_ref[...]
    lf = lf_ref[...]
    g, (ol,) = _chunk_scan(g_ref[...], [lf - scale * lf], rows, True)
    _carry(g, [ol], None, [bl_ref], rows, True)
    sub = lax.broadcasted_iota(jnp.int32, (SUB, cols), 0)
    tile = jnp.where(
        sub == 1,
        jnp.broadcast_to(lf_ref[rows - 1:rows, :], (SUB, cols)),
        jnp.where(sub == 3, jnp.broadcast_to(bl_ref[0:1, :], (SUB, cols)), part_ref[...]),
    )
    for k in range(sum_ref.shape[0]):
        sum_ref[k] = tile


def local_scans(factors, parts, step_gain, scale, part, blocks):
    shape = jax.ShapeDtypeStruct(factors.shape, jnp.float32)
    rows, cols = factors.shape
    return pl.pallas_call(
        scan_kernel,
        out_shape=[shape] * 2 + [jax.ShapeDtypeStruct((blocks, SUB, cols), jnp.float32)],
        cost_estimate=pl.CostEstimate(flops=20 * rows * cols, bytes_accessed=40 * rows * cols, transcendentals=0),
    )(factors, *parts, step_gain, scale, part)


def combine_kernel(every_ref, init_ref, pf_ref, lf_ref, pb_ref, bl_ref, bp_ref, f_ref, s_ref):
    count = every_ref.shape[0]
    place = lax.axis_index("tm")
    entering = [init_ref[...]]
    for k in range(count - 1):
        tile = every_ref[k]
        entering.append(tile[0:1] * entering[-1] + tile[1:2])
    after = jnp.zeros_like(entering[0])
    e_here = jnp.where(place == count - 1, entering[count - 1], 0.0)
    y_here = jnp.zeros_like(after)
    for k in range(count - 1, 0, -1):
        tile = every_ref[k]
        after = tile[3:4] + tile[4:5] * entering[k] + tile[2:3] * after
        e_here = jnp.where(place == k - 1, entering[k - 1], e_here)
        y_here = jnp.where(place == k - 1, after, y_here)
    f_ref[...] = lf_ref[...] + pf_ref[...] * e_here
    s_ref[...] = bl_ref[...] + bp_ref[...] * e_here + pb_ref[...] * y_here


def combine(every, initial, pf, lf, pb, bl, bp):
    rows, cols = pf.shape
    shape = jax.ShapeDtypeStruct(pf.shape, jnp.float32)
    return pl.pallas_call(
        combine_kernel,
        out_shape=[shape, shape],
        cost_estimate=pl.CostEstimate(flops=5 * rows * cols, bytes_accessed=28 * rows * cols, transcendentals=0),
    )(every, initial, pf, lf, pb, bl, bp)


def matmul_kernel(slots_ref, obs_ref, gain_ref, keep_ref, send_ref, lhs_ref):
    blocks = obs_ref.shape[1] // 128
    sensor = lax.axis_index("sensor")

    @pl.when(pl.program_id(0) == 0)
    def _():
        slots = slots_ref[...]
        shape = (128, slots.shape[1])
        block_of = lax.broadcasted_iota(jnp.int32, shape, 0)
        wanted = jnp.where(block_of < blocks, sensor * blocks + block_of, -2)
        listed_t = jnp.zeros(shape, jnp.float32)
        for s in range(slots.shape[0]):
            listed_t = jnp.maximum(listed_t, (slots[s:s + 1, :] == wanted).astype(jnp.float32))
        listed = listed_t.T
        for b in range(blocks):
            cols = pl.ds(128 * b, 128)
            block = obs_ref[:, cols]
            lhs_ref[:, cols] = jnp.where(listed[:, b:b + 1] > 0, block, jnp.zeros_like(block))

    prod = jnp.dot(lhs_ref[...], gain_ref[...], preferred_element_type=jnp.float32)
    even = sensor % 2 == 0
    for c in range(keep_ref.shape[0]):
        left = prod[:, 256 * c:256 * c + 128]
        right = prod[:, 256 * c + 128:256 * c + 256]
        keep_ref[c] = jnp.where(even, left, right)
        send_ref[c] = jnp.where(even, right, left)


def listed_matmul(slots, observations, gain_rows):
    rows, depth = observations.shape
    modes = gain_rows.shape[1]
    tile = 1024
    tiles = modes // tile
    chips_per_tile = tile // 256
    piece = jax.ShapeDtypeStruct((modes // 256, rows, 128), jnp.float32)
    return pl.pallas_call(
        matmul_kernel,
        grid=(tiles,),
        in_specs=[
            pl.BlockSpec(slots.shape, lambda j: (0, 0)),
            pl.BlockSpec((rows, depth), lambda j: (0, 0)),
            pl.BlockSpec((depth, tile), lambda j: (0, j)),
        ],
        out_specs=[
            pl.BlockSpec((chips_per_tile, rows, 128), lambda j: (j, 0, 0)),
            pl.BlockSpec((chips_per_tile, rows, 128), lambda j: (j, 0, 0)),
        ],
        out_shape=[piece, piece],
        scratch_shapes=[pltpu.VMEM((rows, depth), jnp.bfloat16)],
        compiler_params=pltpu.CompilerParams(dimension_semantics=("arbitrary",)),
        cost_estimate=pl.CostEstimate(
            flops=2 * rows * depth * modes,
            bytes_accessed=2 * rows * depth + 2 * depth * modes + 4 * rows * modes,
            transcendentals=0,
        ),
    )(slots, observations, gain_rows)


def sensor_reduce_scatter(keep, send):
    count = lax.axis_size("sensor")
    chips = count // 2
    j = lax.axis_index("sensor")
    chip = j // 2
    chip_sum = keep + lax.ppermute(send, "sensor", [(i, i ^ 1) for i in range(count)])
    parts = [lax.dynamic_index_in_dim(chip_sum, chip, 0, False)]
    for shift in range(1, chips):
        part = lax.dynamic_index_in_dim(chip_sum, (chip + shift) % chips, 0, False)
        perm = [(i, (((i // 2) + shift) % chips) * 2 + i % 2) for i in range(count)]
        parts.append(lax.ppermute(part, "sensor", perm))
    return parts


def gather_tm(copies):
    return lax.all_to_all(copies, "tm", 0, 0, tiled=True)


def per_device(observations, obs_list, gain_rows, decay, smooth_gain, model_rate, first_state):
    sensor_count = lax.axis_size("sensor")
    sensor_index = lax.axis_index("sensor")
    time_index = lax.axis_index("tm")
    time_count = lax.axis_size("tm")
    rows_here = observations.shape[0]
    keep, send = listed_matmul(obs_list.T, observations, gain_rows)
    width = gain_rows.shape[1] // sensor_count
    parts = sensor_reduce_scatter(keep, send)
    start_col = sensor_index * width
    factors = lax.dynamic_slice_in_dim(decay, start_col, width, 1)
    gains = lax.dynamic_slice_in_dim(smooth_gain, start_col, width, 1)
    rates = lax.dynamic_slice_in_dim(model_rate, start_col, width, 0)
    initial = lax.dynamic_slice_in_dim(first_state, start_col, width, 0)
    hour_ids = time_index * rows_here + jnp.arange(rows_here, dtype=jnp.int32)
    total_hours = rows_here * time_count
    step_gain = jnp.where((hour_ids == total_hours - 1)[:, None], jnp.float32(0.0), gains)
    scale = step_gain * rates[None, :]

    prod_fwd, prod_back, back_prod, part = gain_scans(factors, step_gain, scale)
    local_fwd, back_local, summary = local_scans(factors, parts, step_gain, scale, part, time_count)
    every = gather_tm(summary)
    filtered, smoothed = combine(
        every, initial[None, :], prod_fwd, local_fwd, prod_back, back_local, back_prod
    )
    return (filtered, smoothed)


def solution(mesh):
    in_specs = (
        P("tm", "sensor"),
        P("tm", "sensor"),
        P("sensor", None),
        P("tm", None),
        P("tm", None),
        P(),
        P(),
    )
    out_specs = (P("tm", "sensor"), P("tm", "sensor"))
    return jax.shard_map(
        per_device, mesh=mesh, in_specs=in_specs, out_specs=out_specs, check_vma=False
    )
```

```python
import jax
import jax.numpy as jnp
from jax import lax
from jax.experimental import pallas as pl
from jax.experimental.pallas import tpu as pltpu
from jax.sharding import PartitionSpec as P


SUB = 8
CHUNK = 64


def _chunk_scan(a, x, rows, reverse):
    sub = lax.broadcasted_iota(jnp.int32, a.shape, 0) % CHUNK
    for k in (1, 2, 4, 8, 16, 32):
        shift = rows - k if reverse else k
        prev_a = pltpu.roll(a, shift, 0)
        prev_x = [pltpu.roll(v, shift, 0) for v in x]
        inside = sub < CHUNK - k if reverse else sub >= k
        x = [jnp.where(inside, a * p + v, v) for p, v in zip(prev_x, x)]
        a = jnp.where(inside, a * prev_a, a)
    return a, x


def _carry(a, x, out_a, out_x, rows, reverse):
    chunks = rows // CHUNK
    order = range(chunks - 1, -1, -1) if reverse else range(chunks)
    edge = 0 if reverse else CHUNK - 1
    carry_a = None
    for i in order:
        ca = a[i * CHUNK:(i + 1) * CHUNK]
        cx = [v[i * CHUNK:(i + 1) * CHUNK] for v in x]
        if carry_a is not None:
            cx = [c * px + v for c, px, v in zip([ca] * len(cx), carry_x, cx)]
            ca = ca * carry_a
        if out_a is not None:
            out_a[i * CHUNK:(i + 1) * CHUNK, :] = ca
        for o, v in zip(out_x, cx):
            o[i * CHUNK:(i + 1) * CHUNK, :] = v
        carry_a = jnp.broadcast_to(ca[edge:edge + 1], ca.shape)
        carry_x = [jnp.broadcast_to(v[edge:edge + 1], v.shape) for v in cx]


def _summary_tile(rows_by_slot, cols):
    sub = lax.broadcasted_iota(jnp.int32, (SUB, cols), 0)
    tile = jnp.zeros((SUB, cols), jnp.float32)
    for row, value in rows_by_slot:
        tile = jnp.where(sub == row, jnp.broadcast_to(value, tile.shape), tile)
    return tile


def gain_scan_kernel(a_ref, g_ref, s_ref, pf_ref, pb_ref, bp_ref, part_ref):
    rows, cols = a_ref.shape
    a, _ = _chunk_scan(a_ref[...], [], rows, False)
    _carry(a, [], pf_ref, [], rows, False)
    scale = s_ref[...]
    pf = pf_ref[...]
    g, (op,) = _chunk_scan(g_ref[...], [pf - scale * pf], rows, True)
    _carry(g, [op], pb_ref, [bp_ref], rows, True)
    part_ref[...] = _summary_tile(
        [(0, pf_ref[rows - 1:rows, :]), (2, pb_ref[0:1, :]), (4, bp_ref[0:1, :])], cols
    )


def gain_scans(factors, step_gain, scale):
    shape = jax.ShapeDtypeStruct(factors.shape, jnp.float32)
    rows, cols = factors.shape
    return pl.pallas_call(
        gain_scan_kernel,
        out_shape=[shape] * 3 + [jax.ShapeDtypeStruct((SUB, cols), jnp.float32)],
        cost_estimate=pl.CostEstimate(flops=20 * rows * cols, bytes_accessed=24 * rows * cols, transcendentals=0),
    )(factors, step_gain, scale)


def scan_kernel(a_ref, own_ref, r1_ref, r2_ref, r3_ref, g_ref, s_ref, part_ref, lf_ref, bl_ref, sum_ref):
    rows, cols = a_ref.shape
    inflow = ((own_ref[...] + r1_ref[...]) + r2_ref[...]) + r3_ref[...]
    a, (u,) = _chunk_scan(a_ref[...], [inflow], rows, False)
    _carry(a, [u], None, [lf_ref], rows, False)
    scale = s_ref[...]
    lf = lf_ref[...]
    g, (ol,) = _chunk_scan(g_ref[...], [lf - scale * lf], rows, True)
    _carry(g, [ol], None, [bl_ref], rows, True)
    sub = lax.broadcasted_iota(jnp.int32, (SUB, cols), 0)
    tile = jnp.where(
        sub == 1,
        jnp.broadcast_to(lf_ref[rows - 1:rows, :], (SUB, cols)),
        jnp.where(sub == 3, jnp.broadcast_to(bl_ref[0:1, :], (SUB, cols)), part_ref[...]),
    )
    for k in range(sum_ref.shape[0]):
        sum_ref[k] = tile


def local_scans(factors, parts, step_gain, scale, part, blocks):
    shape = jax.ShapeDtypeStruct(factors.shape, jnp.float32)
    rows, cols = factors.shape
    return pl.pallas_call(
        scan_kernel,
        out_shape=[shape] * 2 + [jax.ShapeDtypeStruct((blocks, SUB, cols), jnp.float32)],
        cost_estimate=pl.CostEstimate(flops=20 * rows * cols, bytes_accessed=40 * rows * cols, transcendentals=0),
    )(factors, *parts, step_gain, scale, part)


def combine_kernel(every_ref, init_ref, pf_ref, lf_ref, pb_ref, bl_ref, bp_ref, f_ref, s_ref):
    count = every_ref.shape[0]
    place = lax.axis_index("tm")
    prod, local, back_gain, back_local, back_prod = (every_ref[:, r, :] for r in range(5))
    row = lax.broadcasted_iota(jnp.int32, prod.shape, 0)
    step = 1
    while step < count:
        earlier_a = pltpu.roll(prod, step, 0)
        earlier_x = pltpu.roll(local, step, 0)
        inside = row >= step
        local = jnp.where(inside, prod * earlier_x + local, local)
        prod = jnp.where(inside, prod * earlier_a, prod)
        step *= 2
    initial = init_ref[...]
    entering = jnp.where(row == 0, initial, pltpu.roll(prod * initial + local, 1, 0))
    gain, after = back_gain, back_local + back_prod * entering
    step = 1
    while step < count:
        later_a = pltpu.roll(gain, count - step, 0)
        later_x = pltpu.roll(after, count - step, 0)
        inside = row < count - step
        after = jnp.where(inside, gain * later_x + after, after)
        gain = jnp.where(inside, gain * later_a, gain)
        step *= 2
    e_here = jnp.sum(jnp.where(row == place, entering, 0.0), axis=0, keepdims=True)
    y_here = jnp.sum(jnp.where(row == place + 1, after, 0.0), axis=0, keepdims=True)
    f_ref[...] = lf_ref[...] + pf_ref[...] * e_here
    s_ref[...] = bl_ref[...] + bp_ref[...] * e_here + pb_ref[...] * y_here


def combine(every, initial, pf, lf, pb, bl, bp):
    rows, cols = pf.shape
    shape = jax.ShapeDtypeStruct(pf.shape, jnp.float32)
    return pl.pallas_call(
        combine_kernel,
        out_shape=[shape, shape],
        cost_estimate=pl.CostEstimate(flops=5 * rows * cols, bytes_accessed=28 * rows * cols, transcendentals=0),
    )(every, initial, pf, lf, pb, bl, bp)


def matmul_kernel(slots_ref, obs_ref, gain_ref, keep_ref, send_ref, lhs_ref):
    blocks = obs_ref.shape[1] // 128
    sensor = lax.axis_index("sensor")

    @pl.when(pl.program_id(0) == 0)
    def _():
        slots = slots_ref[...]
        shape = (128, slots.shape[1])
        block_of = lax.broadcasted_iota(jnp.int32, shape, 0)
        wanted = jnp.where(block_of < blocks, sensor * blocks + block_of, -2)
        listed_t = jnp.zeros(shape, jnp.float32)
        for s in range(slots.shape[0]):
            listed_t = jnp.maximum(listed_t, (slots[s:s + 1, :] == wanted).astype(jnp.float32))
        listed = listed_t.T
        for b in range(blocks):
            cols = pl.ds(128 * b, 128)
            block = obs_ref[:, cols]
            lhs_ref[:, cols] = jnp.where(listed[:, b:b + 1] > 0, block, jnp.zeros_like(block))

    prod = jnp.dot(lhs_ref[...], gain_ref[...], preferred_element_type=jnp.float32)
    even = sensor % 2 == 0
    for c in range(keep_ref.shape[0]):
        left = prod[:, 256 * c:256 * c + 128]
        right = prod[:, 256 * c + 128:256 * c + 256]
        keep_ref[c] = jnp.where(even, left, right)
        send_ref[c] = jnp.where(even, right, left)


def listed_matmul(slots, observations, gain_rows):
    rows, depth = observations.shape
    modes = gain_rows.shape[1]
    tile = 512
    tiles = modes // tile
    chips_per_tile = tile // 256
    piece = jax.ShapeDtypeStruct((modes // 256, rows, 128), jnp.float32)
    return pl.pallas_call(
        matmul_kernel,
        grid=(tiles,),
        in_specs=[
            pl.BlockSpec(slots.shape, lambda j: (0, 0)),
            pl.BlockSpec((rows, depth), lambda j: (0, 0)),
            pl.BlockSpec((depth, tile), lambda j: (0, j)),
        ],
        out_specs=[
            pl.BlockSpec((chips_per_tile, rows, 128), lambda j: (j, 0, 0)),
            pl.BlockSpec((chips_per_tile, rows, 128), lambda j: (j, 0, 0)),
        ],
        out_shape=[piece, piece],
        scratch_shapes=[pltpu.VMEM((rows, depth), jnp.bfloat16)],
        compiler_params=pltpu.CompilerParams(dimension_semantics=("arbitrary",)),
        cost_estimate=pl.CostEstimate(
            flops=2 * rows * depth * modes,
            bytes_accessed=2 * rows * depth + 2 * depth * modes + 4 * rows * modes,
            transcendentals=0,
        ),
    )(slots, observations, gain_rows)


def sensor_reduce_scatter(keep, send):
    count = lax.axis_size("sensor")
    chips = count // 2
    j = lax.axis_index("sensor")
    chip = j // 2
    chip_sum = keep + lax.ppermute(send, "sensor", [(i, i ^ 1) for i in range(count)])
    parts = [lax.dynamic_index_in_dim(chip_sum, chip, 0, False)]
    for shift in range(1, chips):
        part = lax.dynamic_index_in_dim(chip_sum, (chip + shift) % chips, 0, False)
        perm = [(i, (((i // 2) + shift) % chips) * 2 + i % 2) for i in range(count)]
        parts.append(lax.ppermute(part, "sensor", perm))
    return parts


def gather_tm(copies):
    return lax.all_to_all(copies, "tm", 0, 0, tiled=True)


def per_device(observations, obs_list, gain_rows, decay, smooth_gain, model_rate, first_state):
    sensor_count = lax.axis_size("sensor")
    sensor_index = lax.axis_index("sensor")
    time_index = lax.axis_index("tm")
    time_count = lax.axis_size("tm")
    rows_here = observations.shape[0]
    keep, send = listed_matmul(obs_list.T, observations, gain_rows)
    width = gain_rows.shape[1] // sensor_count
    parts = sensor_reduce_scatter(keep, send)
    start_col = sensor_index * width
    factors = lax.dynamic_slice_in_dim(decay, start_col, width, 1)
    gains = lax.dynamic_slice_in_dim(smooth_gain, start_col, width, 1)
    rates = lax.dynamic_slice_in_dim(model_rate, start_col, width, 0)
    initial = lax.dynamic_slice_in_dim(first_state, start_col, width, 0)
    hour_ids = time_index * rows_here + jnp.arange(rows_here, dtype=jnp.int32)
    total_hours = rows_here * time_count
    step_gain = jnp.where((hour_ids == total_hours - 1)[:, None], jnp.float32(0.0), gains)
    scale = step_gain * rates[None, :]

    prod_fwd, prod_back, back_prod, part = gain_scans(factors, step_gain, scale)
    local_fwd, back_local, summary = local_scans(factors, parts, step_gain, scale, part, time_count)
    every = gather_tm(summary)
    filtered, smoothed = combine(
        every, initial[None, :], prod_fwd, local_fwd, prod_back, back_local, back_prod
    )
    return (filtered, smoothed)


def solution(mesh):
    in_specs = (
        P("tm", "sensor"),
        P("tm", "sensor"),
        P("sensor", None),
        P("tm", None),
        P("tm", None),
        P(),
        P(),
    )
    out_specs = (P("tm", "sensor"), P("tm", "sensor"))
    return jax.shard_map(
        per_device, mesh=mesh, in_specs=in_specs, out_specs=out_specs, check_vma=False
    )
```

```python
import jax
import jax.numpy as jnp
from jax import lax
from jax.experimental import pallas as pl
from jax.experimental.pallas import tpu as pltpu
from jax.sharding import PartitionSpec as P


SUB = 8
CHUNK = 128


def _chunk_scan(a, x, rows, reverse):
    sub = lax.broadcasted_iota(jnp.int32, a.shape, 0) % CHUNK
    for k in (1, 2, 4, 8, 16, 32, 64):
        shift = rows - k if reverse else k
        prev_a = pltpu.roll(a, shift, 0)
        prev_x = [pltpu.roll(v, shift, 0) for v in x]
        inside = sub < CHUNK - k if reverse else sub >= k
        x = [jnp.where(inside, a * p + v, v) for p, v in zip(prev_x, x)]
        a = jnp.where(inside, a * prev_a, a)
    return a, x


def _carry(a, x, out_a, out_x, rows, reverse):
    chunks = rows // CHUNK
    order = range(chunks - 1, -1, -1) if reverse else range(chunks)
    edge = 0 if reverse else CHUNK - 1
    carry_a = None
    for i in order:
        ca = a[i * CHUNK:(i + 1) * CHUNK]
        cx = [v[i * CHUNK:(i + 1) * CHUNK] for v in x]
        if carry_a is not None:
            cx = [c * px + v for c, px, v in zip([ca] * len(cx), carry_x, cx)]
            ca = ca * carry_a
        if out_a is not None:
            out_a[i * CHUNK:(i + 1) * CHUNK, :] = ca
        for o, v in zip(out_x, cx):
            o[i * CHUNK:(i + 1) * CHUNK, :] = v
        carry_a = jnp.broadcast_to(ca[edge:edge + 1], ca.shape)
        carry_x = [jnp.broadcast_to(v[edge:edge + 1], v.shape) for v in cx]


def _summary_tile(rows_by_slot, cols):
    sub = lax.broadcasted_iota(jnp.int32, (SUB, cols), 0)
    tile = jnp.zeros((SUB, cols), jnp.float32)
    for row, value in rows_by_slot:
        tile = jnp.where(sub == row, jnp.broadcast_to(value, tile.shape), tile)
    return tile


def gain_scan_kernel(a_ref, g_ref, s_ref, pf_ref, pb_ref, bp_ref, part_ref):
    rows, cols = a_ref.shape
    a, _ = _chunk_scan(a_ref[...], [], rows, False)
    _carry(a, [], pf_ref, [], rows, False)
    scale = s_ref[...]
    pf = pf_ref[...]
    g, (op,) = _chunk_scan(g_ref[...], [pf - scale * pf], rows, True)
    _carry(g, [op], pb_ref, [bp_ref], rows, True)
    part_ref[...] = _summary_tile(
        [(0, pf_ref[rows - 1:rows, :]), (2, pb_ref[0:1, :]), (4, bp_ref[0:1, :])], cols
    )


def gain_scans(factors, step_gain, scale):
    shape = jax.ShapeDtypeStruct(factors.shape, jnp.float32)
    rows, cols = factors.shape
    return pl.pallas_call(
        gain_scan_kernel,
        out_shape=[shape] * 3 + [jax.ShapeDtypeStruct((SUB, cols), jnp.float32)],
        cost_estimate=pl.CostEstimate(flops=20 * rows * cols, bytes_accessed=24 * rows * cols, transcendentals=0),
    )(factors, step_gain, scale)


def scan_kernel(a_ref, own_ref, r1_ref, r2_ref, r3_ref, g_ref, s_ref, part_ref, lf_ref, bl_ref, sum_ref):
    rows, cols = a_ref.shape
    inflow = ((own_ref[...] + r1_ref[...]) + r2_ref[...]) + r3_ref[...]
    a, (u,) = _chunk_scan(a_ref[...], [inflow], rows, False)
    _carry(a, [u], None, [lf_ref], rows, False)
    scale = s_ref[...]
    lf = lf_ref[...]
    g, (ol,) = _chunk_scan(g_ref[...], [lf - scale * lf], rows, True)
    _carry(g, [ol], None, [bl_ref], rows, True)
    sub = lax.broadcasted_iota(jnp.int32, (SUB, cols), 0)
    tile = jnp.where(
        sub == 1,
        jnp.broadcast_to(lf_ref[rows - 1:rows, :], (SUB, cols)),
        jnp.where(sub == 3, jnp.broadcast_to(bl_ref[0:1, :], (SUB, cols)), part_ref[...]),
    )
    for k in range(sum_ref.shape[0]):
        sum_ref[k] = tile


def local_scans(factors, parts, step_gain, scale, part, blocks):
    shape = jax.ShapeDtypeStruct(factors.shape, jnp.float32)
    rows, cols = factors.shape
    return pl.pallas_call(
        scan_kernel,
        out_shape=[shape] * 2 + [jax.ShapeDtypeStruct((blocks, SUB, cols), jnp.float32)],
        cost_estimate=pl.CostEstimate(flops=20 * rows * cols, bytes_accessed=40 * rows * cols, transcendentals=0),
    )(factors, *parts, step_gain, scale, part)


def combine_kernel(every_ref, init_ref, pf_ref, lf_ref, pb_ref, bl_ref, bp_ref, f_ref, s_ref):
    count = every_ref.shape[0]
    place = lax.axis_index("tm")
    entering = [init_ref[...]]
    for k in range(count - 1):
        tile = every_ref[k]
        entering.append(tile[0:1] * entering[-1] + tile[1:2])
    after = jnp.zeros_like(entering[0])
    e_here = jnp.where(place == count - 1, entering[count - 1], 0.0)
    y_here = jnp.zeros_like(after)
    for k in range(count - 1, 0, -1):
        tile = every_ref[k]
        after = tile[3:4] + tile[4:5] * entering[k] + tile[2:3] * after
        e_here = jnp.where(place == k - 1, entering[k - 1], e_here)
        y_here = jnp.where(place == k - 1, after, y_here)
    f_ref[...] = lf_ref[...] + pf_ref[...] * e_here
    s_ref[...] = bl_ref[...] + bp_ref[...] * e_here + pb_ref[...] * y_here


def combine(every, initial, pf, lf, pb, bl, bp):
    rows, cols = pf.shape
    shape = jax.ShapeDtypeStruct(pf.shape, jnp.float32)
    return pl.pallas_call(
        combine_kernel,
        out_shape=[shape, shape],
        cost_estimate=pl.CostEstimate(flops=5 * rows * cols, bytes_accessed=28 * rows * cols, transcendentals=0),
    )(every, initial, pf, lf, pb, bl, bp)


def matmul_kernel(slots_ref, obs_ref, gain_ref, keep_ref, send_ref, lhs_ref):
    blocks = obs_ref.shape[1] // 128
    sensor = lax.axis_index("sensor")

    @pl.when(pl.program_id(0) == 0)
    def _():
        slots = slots_ref[...]
        shape = (128, slots.shape[1])
        block_of = lax.broadcasted_iota(jnp.int32, shape, 0)
        wanted = jnp.where(block_of < blocks, sensor * blocks + block_of, -2)
        listed_t = jnp.zeros(shape, jnp.float32)
        for s in range(slots.shape[0]):
            listed_t = jnp.maximum(listed_t, (slots[s:s + 1, :] == wanted).astype(jnp.float32))
        listed = listed_t.T
        for b in range(blocks):
            cols = pl.ds(128 * b, 128)
            block = obs_ref[:, cols]
            lhs_ref[:, cols] = jnp.where(listed[:, b:b + 1] > 0, block, jnp.zeros_like(block))

    prod = jnp.dot(lhs_ref[...], gain_ref[...], preferred_element_type=jnp.float32)
    even = sensor % 2 == 0
    for c in range(keep_ref.shape[0]):
        left = prod[:, 256 * c:256 * c + 128]
        right = prod[:, 256 * c + 128:256 * c + 256]
        keep_ref[c] = jnp.where(even, left, right)
        send_ref[c] = jnp.where(even, right, left)


def listed_matmul(slots, observations, gain_rows):
    rows, depth = observations.shape
    modes = gain_rows.shape[1]
    tile = 512
    tiles = modes // tile
    chips_per_tile = tile // 256
    piece = jax.ShapeDtypeStruct((modes // 256, rows, 128), jnp.float32)
    return pl.pallas_call(
        matmul_kernel,
        grid=(tiles,),
        in_specs=[
            pl.BlockSpec(slots.shape, lambda j: (0, 0)),
            pl.BlockSpec((rows, depth), lambda j: (0, 0)),
            pl.BlockSpec((depth, tile), lambda j: (0, j)),
        ],
        out_specs=[
            pl.BlockSpec((chips_per_tile, rows, 128), lambda j: (j, 0, 0)),
            pl.BlockSpec((chips_per_tile, rows, 128), lambda j: (j, 0, 0)),
        ],
        out_shape=[piece, piece],
        scratch_shapes=[pltpu.VMEM((rows, depth), jnp.bfloat16)],
        compiler_params=pltpu.CompilerParams(dimension_semantics=("arbitrary",)),
        cost_estimate=pl.CostEstimate(
            flops=2 * rows * depth * modes,
            bytes_accessed=2 * rows * depth + 2 * depth * modes + 4 * rows * modes,
            transcendentals=0,
        ),
    )(slots, observations, gain_rows)


def sensor_reduce_scatter(keep, send):
    count = lax.axis_size("sensor")
    chips = count // 2
    j = lax.axis_index("sensor")
    chip = j // 2
    chip_sum = keep + lax.ppermute(send, "sensor", [(i, i ^ 1) for i in range(count)])
    parts = [lax.dynamic_index_in_dim(chip_sum, chip, 0, False)]
    for shift in range(1, chips):
        part = lax.dynamic_index_in_dim(chip_sum, (chip + shift) % chips, 0, False)
        perm = [(i, (((i // 2) + shift) % chips) * 2 + i % 2) for i in range(count)]
        parts.append(lax.ppermute(part, "sensor", perm))
    return parts


def gather_tm(copies):
    return lax.all_to_all(copies, "tm", 0, 0, tiled=True)


def per_device(observations, obs_list, gain_rows, decay, smooth_gain, model_rate, first_state):
    sensor_count = lax.axis_size("sensor")
    sensor_index = lax.axis_index("sensor")
    time_index = lax.axis_index("tm")
    time_count = lax.axis_size("tm")
    rows_here = observations.shape[0]
    keep, send = listed_matmul(obs_list.T, observations, gain_rows)
    width = gain_rows.shape[1] // sensor_count
    parts = sensor_reduce_scatter(keep, send)
    start_col = sensor_index * width
    factors = lax.dynamic_slice_in_dim(decay, start_col, width, 1)
    gains = lax.dynamic_slice_in_dim(smooth_gain, start_col, width, 1)
    rates = lax.dynamic_slice_in_dim(model_rate, start_col, width, 0)
    initial = lax.dynamic_slice_in_dim(first_state, start_col, width, 0)
    hour_ids = time_index * rows_here + jnp.arange(rows_here, dtype=jnp.int32)
    total_hours = rows_here * time_count
    step_gain = jnp.where((hour_ids == total_hours - 1)[:, None], jnp.float32(0.0), gains)
    scale = step_gain * rates[None, :]

    prod_fwd, prod_back, back_prod, part = gain_scans(factors, step_gain, scale)
    local_fwd, back_local, summary = local_scans(factors, parts, step_gain, scale, part, time_count)
    every = gather_tm(summary)
    filtered, smoothed = combine(
        every, initial[None, :], prod_fwd, local_fwd, prod_back, back_local, back_prod
    )
    return (filtered, smoothed)


def solution(mesh):
    in_specs = (
        P("tm", "sensor"),
        P("tm", "sensor"),
        P("sensor", None),
        P("tm", None),
        P("tm", None),
        P(),
        P(),
    )
    out_specs = (P("tm", "sensor"), P("tm", "sensor"))
    return jax.shard_map(
        per_device, mesh=mesh, in_specs=in_specs, out_specs=out_specs, check_vma=False
    )
```
